128 devices in a mesh: shot: 8 (over x, y_hi), space: 16 (over y_lo, z, core).
Axes of the slice: x: 4, y: 4 (y_hi: 2, y_lo: 2; y = y_hi * 2 + y_lo), z: 4, core: 2. Of those that a mesh axis runs over, the one named last changes fastest.
Arguments:
- residual: bfloat16 [8, 4096, 1536], P('shot', 'space'), may hold values from -6 to 6
- record_tile: int32 [8, 4096, 1], P('shot', 'space'), may hold values from 0 to 15; in each aligned block of 256 rows (0 to 255, 256 to 511, ..., all dimensions but the last counted through in order) at most 48 rows name the same one
- record_cell: int32 [8, 4096], P('shot', 'space'), may hold values from 0 to 1023
- time_filter: bfloat16 [6, 1536], replicated, may hold values from -0.15625 to 0.15625
- offsets: int32 [8], P('shot'), may hold values from 0 to 16
- velocity: float32 [8, 64, 256, 256], P('shot', None, 'space'), may hold values from 0.05 to 0.19
- adjoint_prev: float32 [8, 64, 256, 256], P('shot', None, 'space'), may hold values from -6 to 6
- adjoint_now: float32 [8, 64, 256, 256], P('shot', None, 'space'), may hold values from -6 to 6
- forward_accel: bfloat16 [8, 6, 64, 256, 256], P('shot', None, None, 'space'), may hold values from -6 to 6
Outputs:
- gradient: float32 [80, 256, 256], P('shot', 'space')
- adjoint_last: float32 [8, 64, 256, 256], P('shot', None, 'space')
The draws below stay inside these ranges and needn't reach their ends.
Inputs may be any that keep to these rules, and one draw needn't show every extreme that they name: `record_tile`: among the 256 records of one device, at most 48 name the same tile.
All inputs are finite; a program needn't handle non-finite values.
Results may differ from the reference program's by a relative error of at most 0.0003.
Values sent between devices are 32-bit elements; how exact they have to be, the bound alone decides.
No kernel may reach another device: no remote copies, remote signals or barrier semaphores. Data moves between devices by JAX's collectives and lax.ppermute only.
A program may use at most 64 MiB of HBM per device.

```python
import math
import jax
import jax.numpy as jnp
import numpy as np
from jax import lax

CX = 16
NY = 64
NZ = 256
REC_DEV = 256
NT = 1536
STEPS = 6
SHOTS = 8
NX = 256
RECS = 4096
CAP = 48
GY = 80
N_SPACE = 16


def draw_adjoint_prev(key, part):
    own_key = jax.random.fold_in(key, 11)
    extent = (SHOTS, NY, NX, NZ)
    return jnp.clip(jax.random.normal(own_key, extent, jnp.float32), -6.0, 6.0)


def draw_adjoint_now(key, part):
    own_key = jax.random.fold_in(key, 12)
    extent = (SHOTS, NY, NX, NZ)
    return jnp.clip(jax.random.normal(own_key, extent, jnp.float32), -6.0, 6.0)


def set_ends(entries, key, low, largest):
    place = [jax.random.randint(jax.random.fold_in(key, axis), (), 0, length) for axis, length in enumerate(entries.shape)]
    widest = entries.shape.index(max(entries.shape))
    beside = place[:widest] + [(place[widest] + 1) % entries.shape[widest]] + place[widest + 1:]
    return entries.at[tuple(place)].set(low).at[tuple(beside)].set(largest)


def level_of(key, shape, split, low, high):
    def one(axis_at, blocks):
        draws = jax.random.uniform(jax.random.fold_in(jax.random.fold_in(key, 6), axis_at), (blocks,), jnp.float32, low / len(split), high / len(split))
        return jnp.repeat(jnp.exp(draws), shape[axis_at] // blocks).reshape((-1,) + (1,) * (len(shape) - axis_at - 1))

    factor_of = one(*split[0])
    for cut in split[1:]:
        factor_of = factor_of * one(*cut)
    return factor_of


def assign_block(rng, own, number, rows, amount, top, most, lean):
    ranking = jax.random.permutation(rng, amount)
    heavy_load, ordinary = load_shares(amount, rows * top, most, lean, True), load_shares(amount, rows * top, most, lean, False)
    places = jnp.arange(amount)

    def named(lengths, turn):
        used = int((lengths > 0).sum())
        fixed = max(1, used // 4)
        moved = fixed + (places - fixed + turn * (used - fixed)) % max(1, amount - fixed)
        return jnp.zeros((amount,), jnp.int32).at[ranking[jnp.where(places < fixed, places, moved)]].set(jnp.asarray(lengths, jnp.int32))

    lengths = jnp.where(number % 4 == 0, named(heavy_load, number // 4), named(ordinary, number - number // 4 - 1))
    mixed = jax.random.permutation(jax.random.fold_in(own, 3), amount)
    source_of, sink = mixed[0:amount // 2 * 2:2], mixed[1:amount // 2 * 2:2]
    room = jnp.minimum(lengths[source_of] - 1, most - lengths[sink]) // 2
    room = jnp.where((source_of == ranking[0]) | (sink == ranking[0]) | (lengths[sink] == 0), 0, jnp.maximum(room, 0))
    moved = jax.random.randint(jax.random.fold_in(own, 4), (amount // 2,), 0, 1 << 20) % (room + 1)
    lengths = lengths.at[source_of].add(-moved).at[sink].add(moved)
    members = jnp.searchsorted(jnp.cumsum(lengths), jnp.arange(rows * top), side="right").astype(jnp.int32)
    listing = members.reshape(top, rows).T
    listing = listing[jax.random.permutation(jax.random.fold_in(own, 1), rows)]
    turn = jax.random.randint(jax.random.fold_in(own, 2), (rows, 1), 0, top)
    return jnp.take_along_axis(listing, (jnp.arange(top)[None, :] + turn) % top, axis=1)


def load_shares(amount, total, limit, skew, full):
    portions = [(1 << 20) // math.isqrt(standing ** skew) + 1 for standing in range(1, amount + 1)]
    largest = limit if full else min(limit, max(-(-total // amount), total * portions[0] // sum(portions)))
    least = 1 if total - largest >= amount - 1 else 0
    counts, spare = [largest] + [least] * (amount - 1), total - largest - least * (amount - 1)
    while spare > 0:
        movable = [i for i in range(1, amount) if counts[i] < largest] or [i for i in range(1, amount) if counts[i] < limit]
        whole, left = sum([portions[i] for i in movable]), spare
        for i in movable:
            more = min(limit - counts[i], max(1, left * portions[i] // whole), spare)
            counts[i] = counts[i] + more
            spare = spare - more
    return np.array(counts)


def gaussian(stream_key, shape, deviation, bound, pieces=(), held_as=jnp.bfloat16):
    factor_of = level_of(stream_key, shape, pieces, -0.22, 0.18) if pieces else 1.0
    result = jax.random.normal(stream_key, shape, jnp.float32) * deviation * factor_of
    return jnp.minimum(jnp.maximum(result, -bound), bound).astype(held_as)


def setup_inputs(seed: int = 0) -> dict:
    arg_keys = jax.random.split(jax.random.key(seed), 10)
    residual = gaussian(arg_keys[0], (SHOTS, RECS, NT), 1.0, 6.0, ((0, 8), (1, 16)))
    record_tile_keys = jax.random.split(jax.random.fold_in(arg_keys[1], 1), SHOTS * RECS // REC_DEV)
    record_tile_turns = jax.random.permutation(jax.random.fold_in(arg_keys[1], 3), SHOTS * RECS // REC_DEV)
    record_tile = jax.vmap(lambda own, number: assign_block(jax.random.fold_in(arg_keys[1], 2), own, number, REC_DEV, N_SPACE, 1, CAP, 2))(record_tile_keys, record_tile_turns).reshape((SHOTS, RECS, 1))
    record_cell = set_ends(jax.random.randint(arg_keys[2], (SHOTS, RECS), 0, NY * CX), jax.random.fold_in(arg_keys[2], 1), 0, (NY * CX) - 1).astype(jnp.int32)
    time_filter = gaussian(arg_keys[3], (STEPS, NT), NT ** -0.5, 0.15625)
    offsets = set_ends(jax.random.randint(arg_keys[4], (SHOTS,), 0, NY // 4 + 1), jax.random.fold_in(arg_keys[4], 1), 0, (NY // 4 + 1) - 1).astype(jnp.int32)
    velocity = jnp.clip(0.05 + 0.14 * jax.random.uniform(arg_keys[5], (SHOTS, NY, NX, NZ), jnp.float32) ** level_of(arg_keys[5], (SHOTS, NY, NX, NZ), ((0, 8), (2, 16)), -0.2, 0.2), 0.05, 0.19)
    adjoint_prev = draw_adjoint_prev(jax.random.fold_in(arg_keys[9], 71), 0)
    adjoint_now = draw_adjoint_now(jax.random.fold_in(arg_keys[9], 71), 0)
    forward_accel = gaussian(arg_keys[8], (SHOTS, STEPS, NY, NX, NZ), 1.0, 6.0, ((0, 8), (3, 16)))
    return {"residual": residual, "record_tile": record_tile, "record_cell": record_cell, "time_filter": time_filter, "offsets": offsets, "velocity": velocity, "adjoint_prev": adjoint_prev, "adjoint_now": adjoint_now, "forward_accel": forward_accel}


STENCIL = (-205.0 / 72.0, 8.0 / 5.0, -1.0 / 5.0, 8.0 / 315.0, -1.0 / 560.0)


def laplace(padded):
    span_y = padded.shape[0] - 8
    span_x = padded.shape[1] - 8
    span_z = padded.shape[2] - 8

    def window(shift_y, shift_x, shift_z):
        return padded[4 + shift_y:4 + shift_y + span_y, 4 + shift_x:4 + shift_x + span_x, 4 + shift_z:4 + shift_z + span_z]

    summed = 3.0 * STENCIL[0] * window(0, 0, 0)
    for reach in range(1, 5):
        beside_all = window(reach, 0, 0) + window(-reach, 0, 0) + window(0, reach, 0) + window(0, -reach, 0) + window(0, 0, reach) + window(0, 0, -reach)
        summed = summed + STENCIL[reach] * beside_all
    return summed


def reference(residual, record_tile, record_cell, time_filter, offsets, velocity, adjoint_prev, adjoint_now, forward_accel):
    gradient = jnp.zeros((GY, NX, NZ), jnp.float32)
    finals = []
    zero_index = jnp.zeros((), jnp.int32)
    for shot in range(SHOTS):
        values = jnp.dot(residual[shot], time_filter.T, preferred_element_type=jnp.float32)
        cell_ids = record_cell[shot]
        column = record_tile[shot, :, 0] * CX + cell_ids % CX
        surface_index = (cell_ids // CX) * NX + column
        source = jax.ops.segment_sum(values, surface_index, num_segments=NY * NX)
        source = source.T.reshape(STEPS, NY, NX)
        speed_sq = velocity[shot]
        previous = adjoint_prev[shot]
        current = adjoint_now[shot]
        imaging = jnp.zeros_like(current)
        for moment in range(STEPS):
            advanced = 2.0 * current - previous + speed_sq * laplace(jnp.pad(current, 4))
            advanced = advanced.at[:, :, 0].add(source[moment])
            imaging = imaging + forward_accel[shot, moment].astype(jnp.float32) * advanced
            previous, current = current, advanced
        placed = lax.dynamic_update_slice(jnp.zeros((GY, NX, NZ), jnp.float32), imaging, (offsets[shot].astype(jnp.int32), zero_index, zero_index))
        gradient = gradient + placed
        finals.append(current)
    return gradient, jnp.stack(finals)
```

```python
import jax
import jax.numpy as jnp
from jax import lax
from jax.sharding import PartitionSpec as P

STENCIL = (-205.0 / 72.0, 8.0 / 5.0, -1.0 / 5.0, 8.0 / 315.0, -1.0 / 560.0)


def extended(shard, sides, width):
    for axis, dim in sides:
        devices, length = (lax.axis_size(axis), shard.shape[dim])
        up = [(i, (i + 1) % devices) for i in range(devices - 1)]
        down = [(j, i) for i, j in up]
        last = lax.slice_in_dim(shard, length - width, length, axis=dim)
        leading = lax.slice_in_dim(shard, 0, width, axis=dim)
        before = lax.ppermute(last, axis, up)
        after = lax.ppermute(leading, axis, down)
        shard = jnp.concatenate([before, shard, after], axis=dim)
    return shard


def laplace(padded):
    span_y = padded.shape[0] - 8
    span_x = padded.shape[1] - 8
    span_z = padded.shape[2] - 8

    def window(shift_y, shift_x, shift_z):
        return padded[
            4 + shift_y : 4 + shift_y + span_y,
            4 + shift_x : 4 + shift_x + span_x,
            4 + shift_z : 4 + shift_z + span_z,
        ]

    summed = 3.0 * STENCIL[0] * window(0, 0, 0)
    for reach in range(1, 5):
        beside_all = (
            window(reach, 0, 0)
            + window(-reach, 0, 0)
            + window(0, reach, 0)
            + window(0, -reach, 0)
            + window(0, 0, reach)
            + window(0, 0, -reach)
        )
        summed = summed + STENCIL[reach] * beside_all
    return summed


def pad_sides(field):
    return jnp.pad(field, ((4, 4), (0, 0), (4, 4)))


def local(
    residual,
    record_tile,
    record_cell,
    time_filter,
    offsets,
    velocity,
    adjoint_prev,
    adjoint_now,
    forward_accel,
):
    tiles_count = lax.axis_size("space")
    record_count = residual.shape[1]
    cells_y = velocity.shape[1]
    cells_x = velocity.shape[2]
    step_count = forward_accel.shape[1]
    slot_count = record_count * 3 // 16
    surface = cells_y * cells_x
    block_rows = (cells_y + cells_y // 4) // lax.axis_size("shot")
    trace_rows = residual[0]
    tile_ids = record_tile[0, :, 0]
    cell_ids = record_cell[0]
    one_hot = (tile_ids[:, None] == jnp.arange(tiles_count, dtype=jnp.int32)[None, :]).astype(
        jnp.int32
    )
    order_rank = jnp.sum((jnp.cumsum(one_hot, axis=0) - 1) * one_hot, axis=1)
    slot_index = tile_ids * slot_count + order_rank
    cell_buffer = (
        jnp.full((tiles_count * slot_count,), surface, jnp.int32).at[slot_index].set(cell_ids)
    )
    cell_buffer = cell_buffer.reshape(tiles_count, slot_count)
    filtered = jnp.dot(trace_rows, time_filter.T, preferred_element_type=jnp.float32)
    value_buffer = (
        jnp.zeros((tiles_count * slot_count, step_count), jnp.float32).at[slot_index].set(filtered)
    )
    value_buffer = value_buffer.reshape(tiles_count, slot_count, step_count)
    values, arrived_cells = (
        lax.all_to_all(value_buffer, "space", split_axis=0, concat_axis=0, tiled=True),
        lax.all_to_all(cell_buffer, "space", split_axis=0, concat_axis=0, tiled=True),
    )
    source = jax.ops.segment_sum(
        values.reshape(-1, step_count), arrived_cells.reshape(-1), num_segments=surface + 1
    )[:surface]
    source = source.T.reshape(step_count, cells_y, cells_x)
    shift_rows = offsets[0]
    speed_sq = velocity[0]
    previous = adjoint_prev[0]
    current = adjoint_now[0]
    forward = forward_accel[0]
    imaging = jnp.zeros_like(current)
    for moment in range(step_count):
        rimmed = extended(current, (("space", 1),), 4)
        advanced = 2.0 * current - previous + speed_sq * laplace(pad_sides(rimmed))
        depth = lax.broadcasted_iota(jnp.int32, advanced.shape, 2)
        advanced = jnp.where(depth == 0, advanced + source[moment][:, :, None], advanced)
        imaging = imaging + forward[moment] * advanced
        previous, current = (current, advanced)
    row_index = jnp.arange(lax.axis_size("shot") * block_rows, dtype=jnp.int32) - shift_rows
    inside = (row_index >= 0) & (row_index < cells_y)
    chosen = jnp.take(imaging, jnp.clip(row_index, 0, cells_y - 1), axis=0)
    placed = jnp.where(inside[:, None, None], chosen, 0.0)
    shots = lax.axis_size("shot")
    placed = placed.reshape((shots, block_rows) + placed.shape[1:])
    arrived = lax.all_to_all(placed, "shot", split_axis=0, concat_axis=0, tiled=True)
    gradient = jnp.sum(arrived, axis=0)
    return (gradient, current[None])


def solution(mesh):
    in_specs = (
        P("shot", "space", None),
        P("shot", "space", None),
        P("shot", "space"),
        P(),
        P("shot"),
        P("shot", None, "space", None),
        P("shot", None, "space", None),
        P("shot", None, "space", None),
        P("shot", None, None, "space", None),
    )
    out_specs = (P("shot", "space", None), P("shot", None, "space", None))
    return jax.shard_map(local, mesh=mesh, in_specs=in_specs, out_specs=out_specs, check_vma=False)
```

```python
import jax
import jax.numpy as jnp
from jax import lax
from jax.sharding import PartitionSpec as P
from jax.experimental import pallas as pl
from jax.experimental.pallas import tpu as pltpu

STENCIL = (-205.0 / 72.0, 8.0 / 5.0, -1.0 / 5.0, 8.0 / 315.0, -1.0 / 560.0)


def extended(shard, sides, width):
    for axis, dim in sides:
        devices, length = (lax.axis_size(axis), shard.shape[dim])
        up = [(i, (i + 1) % devices) for i in range(devices - 1)]
        down = [(j, i) for i, j in up]
        last = lax.slice_in_dim(shard, length - width, length, axis=dim)
        leading = lax.slice_in_dim(shard, 0, width, axis=dim)
        before = lax.ppermute(last, axis, up)
        after = lax.ppermute(leading, axis, down)
        shard = jnp.concatenate([before, shard, after], axis=dim)
    return shard


def laplace(padded):
    span_y = padded.shape[0] - 8
    span_x = padded.shape[1] - 8
    span_z = padded.shape[2] - 8

    def window(shift_y, shift_x, shift_z):
        return padded[
            4 + shift_y : 4 + shift_y + span_y,
            4 + shift_x : 4 + shift_x + span_x,
            4 + shift_z : 4 + shift_z + span_z,
        ]

    summed = 3.0 * STENCIL[0] * window(0, 0, 0)
    for reach in range(1, 5):
        beside_all = (
            window(reach, 0, 0)
            + window(-reach, 0, 0)
            + window(0, reach, 0)
            + window(0, -reach, 0)
            + window(0, 0, reach)
            + window(0, 0, -reach)
        )
        summed = summed + STENCIL[reach] * beside_all
    return summed


def pad_sides(field):
    return jnp.pad(field, ((4, 4), (0, 0), (4, 4)))


ROWS = 2


def step_kernel(cur_ref, prev_ref, lo_ref, hi_ref, vel_ref, fwd_ref, src_ref, img_ref,
                next_ref, img_out_ref, first_ref, last_ref, pad_ref):
    cells_y, cells_x, cells_z = cur_ref.shape
    width = lo_ref.shape[1]
    zeros = jnp.zeros((4, pad_ref.shape[1], cells_z), jnp.float32)
    pad_ref[0:4] = zeros
    pad_ref[4 + cells_y : 8 + cells_y] = zeros
    pad_ref[4 : 4 + cells_y, 8 - width : 8] = lo_ref[...]
    pad_ref[4 : 4 + cells_y, 8 : 8 + cells_x] = cur_ref[...]
    pad_ref[4 : 4 + cells_y, 8 + cells_x : 8 + cells_x + width] = hi_ref[...]

    def body(chunk, carry):
        y0 = pl.multiple_of(chunk * ROWS, ROWS)

        def window(shift_y, shift_x):
            return pad_ref[pl.ds(y0 + 4 + shift_y, ROWS), 8 + shift_x : 8 + shift_x + cells_x, :]

        center = window(0, 0)
        depth = lax.broadcasted_iota(jnp.int32, center.shape, 2)

        def along_z(reach):
            up = pltpu.roll(center, cells_z - reach, 2)
            down = pltpu.roll(center, reach, 2)
            return (
                jnp.where(depth + reach < cells_z, up, 0.0),
                jnp.where(depth - reach >= 0, down, 0.0),
            )

        summed = 3.0 * STENCIL[0] * center
        for reach in range(1, 5):
            z_up, z_down = along_z(reach)
            beside_all = (
                window(reach, 0)
                + window(-reach, 0)
                + window(0, reach)
                + window(0, -reach)
                + z_up
                + z_down
            )
            summed = summed + STENCIL[reach] * beside_all
        rows = pl.ds(y0, ROWS)
        advanced = 2.0 * center - prev_ref[rows] + vel_ref[rows] * summed
        source = jnp.broadcast_to(src_ref[rows], advanced.shape)
        advanced = jnp.where(depth == 0, advanced + source, advanced)
        next_ref[rows] = advanced
        img_out_ref[rows] = img_ref[rows] + fwd_ref[rows].astype(jnp.float32) * advanced
        first_ref[rows] = advanced[:, :width]
        last_ref[rows] = advanced[:, cells_x - width :]
        return carry

    lax.fori_loop(0, cells_y // ROWS, body, 0)


def step_call(moment, current, previous, lo, hi, speed_sq, forward, source, imaging):
    cells_y, cells_x, cells_z = current.shape
    width = lo.shape[1]
    field = pl.BlockSpec((cells_y, cells_x, cells_z), lambda i: (0, 0, 0))
    rim = pl.BlockSpec((cells_y, width, cells_z), lambda i: (0, 0, 0))
    fwd_spec = pl.BlockSpec((None, cells_y, cells_x, cells_z), lambda i: (moment, 0, 0, 0))
    src_spec = pl.BlockSpec((None, cells_y, cells_x, 1), lambda i: (moment, 0, 0, 0))
    f32 = jnp.float32
    return pl.pallas_call(
        step_kernel,
        grid=(1,),
        out_shape=(
            jax.ShapeDtypeStruct(current.shape, f32),
            jax.ShapeDtypeStruct(current.shape, f32),
            jax.ShapeDtypeStruct(lo.shape, f32),
            jax.ShapeDtypeStruct(lo.shape, f32),
        ),
        in_specs=[field, field, rim, rim, field, fwd_spec, src_spec, field],
        out_specs=(field, field, rim, rim),
        scratch_shapes=[pltpu.VMEM((cells_y + 8, cells_x + 16, cells_z), f32)],
        input_output_aliases={7: 1},
        compiler_params=pltpu.CompilerParams(vmem_limit_bytes=48 * 1024 * 1024),
    )(current, previous, lo, hi, speed_sq, forward, source, imaging)


def halo(first, last):
    axis = "space"
    devices = lax.axis_size(axis)
    up = [(i, (i + 1) % devices) for i in range(devices - 1)]
    down = [(j, i) for i, j in up]
    return lax.ppermute(last, axis, up), lax.ppermute(first, axis, down)


def local(
    residual,
    record_tile,
    record_cell,
    time_filter,
    offsets,
    velocity,
    adjoint_prev,
    adjoint_now,
    forward_accel,
):
    tiles_count = lax.axis_size("space")
    record_count = residual.shape[1]
    cells_y = velocity.shape[1]
    cells_x = velocity.shape[2]
    step_count = forward_accel.shape[1]
    slot_count = record_count * 3 // 16
    surface = cells_y * cells_x
    block_rows = (cells_y + cells_y // 4) // lax.axis_size("shot")
    trace_rows = residual[0]
    tile_ids = record_tile[0, :, 0]
    cell_ids = record_cell[0]
    one_hot = (tile_ids[:, None] == jnp.arange(tiles_count, dtype=jnp.int32)[None, :]).astype(
        jnp.int32
    )
    order_rank = jnp.sum((jnp.cumsum(one_hot, axis=0) - 1) * one_hot, axis=1)
    slot_index = tile_ids * slot_count + order_rank
    cell_buffer = (
        jnp.full((tiles_count * slot_count,), surface, jnp.int32).at[slot_index].set(cell_ids)
    )
    cell_buffer = cell_buffer.reshape(tiles_count, slot_count)
    filtered = jnp.dot(trace_rows, time_filter.T, preferred_element_type=jnp.float32)
    value_buffer = (
        jnp.zeros((tiles_count * slot_count, step_count), jnp.float32).at[slot_index].set(filtered)
    )
    value_buffer = value_buffer.reshape(tiles_count, slot_count, step_count)
    values, arrived_cells = (
        lax.all_to_all(value_buffer, "space", split_axis=0, concat_axis=0, tiled=True),
        lax.all_to_all(cell_buffer, "space", split_axis=0, concat_axis=0, tiled=True),
    )
    source = jax.ops.segment_sum(
        values.reshape(-1, step_count), arrived_cells.reshape(-1), num_segments=surface + 1
    )[:surface]
    source = source.T.reshape(step_count, cells_y, cells_x)
    shift_rows = offsets[0]
    speed_sq = velocity[0]
    previous = adjoint_prev[0]
    current = adjoint_now[0]
    forward = forward_accel[0]
    imaging = jnp.zeros_like(current)
    source = source.reshape(source.shape + (1,))
    width = 4
    first = current[:, :width]
    last = current[:, cells_x - width :]
    for moment in range(step_count):
        lo, hi = halo(first, last)
        advanced, imaging, first, last = step_call(
            moment, current, previous, lo, hi, speed_sq, forward, source, imaging
        )
        previous, current = (current, advanced)
    row_index = jnp.arange(lax.axis_size("shot") * block_rows, dtype=jnp.int32) - shift_rows
    inside = (row_index >= 0) & (row_index < cells_y)
    chosen = jnp.take(imaging, jnp.clip(row_index, 0, cells_y - 1), axis=0)
    placed = jnp.where(inside[:, None, None], chosen, 0.0)
    shots = lax.axis_size("shot")
    placed = placed.reshape((shots, block_rows) + placed.shape[1:])
    arrived = lax.all_to_all(placed, "shot", split_axis=0, concat_axis=0, tiled=True)
    gradient = jnp.sum(arrived, axis=0)
    return (gradient, current[None])


def solution(mesh):
    in_specs = (
        P("shot", "space", None),
        P("shot", "space", None),
        P("shot", "space"),
        P(),
        P("shot"),
        P("shot", None, "space", None),
        P("shot", None, "space", None),
        P("shot", None, "space", None),
        P("shot", None, None, "space", None),
    )
    out_specs = (P("shot", "space", None), P("shot", None, "space", None))
    return jax.shard_map(local, mesh=mesh, in_specs=in_specs, out_specs=out_specs, check_vma=False)
```

```python
import functools

import jax
import jax.numpy as jnp
from jax import lax
from jax.sharding import PartitionSpec as P
from jax.experimental import pallas as pl
from jax.experimental.pallas import tpu as pltpu

STENCIL = (-205.0 / 72.0, 8.0 / 5.0, -1.0 / 5.0, 8.0 / 315.0, -1.0 / 560.0)


def extended(shard, sides, width):
    for axis, dim in sides:
        devices, length = (lax.axis_size(axis), shard.shape[dim])
        up = [(i, (i + 1) % devices) for i in range(devices - 1)]
        down = [(j, i) for i, j in up]
        last = lax.slice_in_dim(shard, length - width, length, axis=dim)
        leading = lax.slice_in_dim(shard, 0, width, axis=dim)
        before = lax.ppermute(last, axis, up)
        after = lax.ppermute(leading, axis, down)
        shard = jnp.concatenate([before, shard, after], axis=dim)
    return shard


def laplace(padded):
    span_y = padded.shape[0] - 8
    span_x = padded.shape[1] - 8
    span_z = padded.shape[2] - 8

    def window(shift_y, shift_x, shift_z):
        return padded[
            4 + shift_y : 4 + shift_y + span_y,
            4 + shift_x : 4 + shift_x + span_x,
            4 + shift_z : 4 + shift_z + span_z,
        ]

    summed = 3.0 * STENCIL[0] * window(0, 0, 0)
    for reach in range(1, 5):
        beside_all = (
            window(reach, 0, 0)
            + window(-reach, 0, 0)
            + window(0, reach, 0)
            + window(0, -reach, 0)
            + window(0, 0, reach)
            + window(0, 0, -reach)
        )
        summed = summed + STENCIL[reach] * beside_all
    return summed


def pad_sides(field):
    return jnp.pad(field, ((4, 4), (0, 0), (4, 4)))


ROWS = 2


def step_kernel(moment, cur_ref, prev_ref, lo_ref, hi_ref, vel_ref, fwd_ref, src_ref, img_ref,
                next_ref, img_out_ref, first_ref, last_ref, pad_ref):
    cells_y, cells_x, cells_z = cur_ref.shape
    width = lo_ref.shape[1]
    zeros = jnp.zeros((4, pad_ref.shape[1], cells_z), jnp.float32)
    pad_ref[0:4] = zeros
    pad_ref[4 + cells_y : 8 + cells_y] = zeros
    pad_ref[4 : 4 + cells_y, 8 - width : 8] = lo_ref[...]
    pad_ref[4 : 4 + cells_y, 8 : 8 + cells_x] = cur_ref[...]
    pad_ref[4 : 4 + cells_y, 8 + cells_x : 8 + cells_x + width] = hi_ref[...]

    def body(chunk, carry):
        y0 = pl.multiple_of(chunk * ROWS, ROWS)

        def window(shift_y, shift_x):
            return pad_ref[pl.ds(y0 + 4 + shift_y, ROWS), 8 + shift_x : 8 + shift_x + cells_x, :]

        center = window(0, 0)
        depth = lax.broadcasted_iota(jnp.int32, center.shape, 2)

        def along_z(reach):
            up = pltpu.roll(center, cells_z - reach, 2)
            down = pltpu.roll(center, reach, 2)
            return (
                jnp.where(depth + reach < cells_z, up, 0.0),
                jnp.where(depth - reach >= 0, down, 0.0),
            )

        summed = 3.0 * STENCIL[0] * center
        for reach in range(1, 5):
            z_up, z_down = along_z(reach)
            beside_all = (
                window(reach, 0)
                + window(-reach, 0)
                + window(0, reach)
                + window(0, -reach)
                + z_up
                + z_down
            )
            summed = summed + STENCIL[reach] * beside_all
        rows = pl.ds(y0, ROWS)
        advanced = 2.0 * center - prev_ref[rows] + vel_ref[rows] * summed
        source = jnp.broadcast_to(src_ref[rows, :, pl.ds(moment, 1)], advanced.shape)
        advanced = jnp.where(depth == 0, advanced + source, advanced)
        next_ref[rows] = advanced
        img_out_ref[rows] = img_ref[rows] + fwd_ref[rows].astype(jnp.float32) * advanced
        first_ref[rows] = advanced[:, :width]
        last_ref[rows] = advanced[:, cells_x - width :]
        return carry

    lax.fori_loop(0, cells_y // ROWS, body, 0)


def step_call(moment, current, previous, lo, hi, speed_sq, forward, source, imaging):
    cells_y, cells_x, cells_z = current.shape
    width = lo.shape[1]
    field = pl.BlockSpec((cells_y, cells_x, cells_z), lambda i: (0, 0, 0))
    rim = pl.BlockSpec((cells_y, width, cells_z), lambda i: (0, 0, 0))
    fwd_spec = pl.BlockSpec((None, cells_y, cells_x, cells_z), lambda i: (moment, 0, 0, 0))
    src_spec = pl.BlockSpec(source.shape, lambda i: (0, 0, 0))
    f32 = jnp.float32
    return pl.pallas_call(
        functools.partial(step_kernel, moment),
        grid=(1,),
        out_shape=(
            jax.ShapeDtypeStruct(current.shape, f32),
            jax.ShapeDtypeStruct(current.shape, f32),
            jax.ShapeDtypeStruct(lo.shape, f32),
            jax.ShapeDtypeStruct(lo.shape, f32),
        ),
        in_specs=[field, field, rim, rim, field, fwd_spec, src_spec, field],
        out_specs=(field, field, rim, rim),
        scratch_shapes=[pltpu.VMEM((cells_y + 8, cells_x + 16, cells_z), f32)],
        input_output_aliases={7: 1},
        compiler_params=pltpu.CompilerParams(vmem_limit_bytes=48 * 1024 * 1024),
    )(current, previous, lo, hi, speed_sq, forward, source, imaging)


def halo(first, last):
    axis = "space"
    devices = lax.axis_size(axis)
    up = [(i, (i + 1) % devices) for i in range(devices - 1)]
    down = [(j, i) for i, j in up]
    return lax.ppermute(last, axis, up), lax.ppermute(first, axis, down)


def local(
    residual,
    record_tile,
    record_cell,
    time_filter,
    offsets,
    velocity,
    adjoint_prev,
    adjoint_now,
    forward_accel,
):
    tiles_count = lax.axis_size("space")
    record_count = residual.shape[1]
    cells_y = velocity.shape[1]
    cells_x = velocity.shape[2]
    step_count = forward_accel.shape[1]
    slot_count = record_count * 3 // 16
    surface = cells_y * cells_x
    block_rows = (cells_y + cells_y // 4) // lax.axis_size("shot")
    trace_rows = residual[0]
    tile_ids = record_tile[0, :, 0]
    cell_ids = record_cell[0]
    one_hot = (tile_ids[:, None] == jnp.arange(tiles_count, dtype=jnp.int32)[None, :]).astype(
        jnp.int32
    )
    order_rank = jnp.sum((jnp.cumsum(one_hot, axis=0) - 1) * one_hot, axis=1)
    slot_index = tile_ids * slot_count + order_rank
    filtered = jnp.dot(trace_rows, time_filter.T, preferred_element_type=jnp.float32)
    payload = jnp.concatenate(
        [filtered, (cell_ids + 1).astype(jnp.float32)[:, None]], axis=1
    )
    slots = tiles_count * slot_count
    placing = (
        slot_index[None, :] == jnp.arange(slots, dtype=jnp.int32)[:, None]
    ).astype(jnp.float32)
    buffer = jnp.dot(placing, payload, precision=lax.Precision.HIGHEST)
    buffer = buffer.reshape(tiles_count, slot_count, step_count + 1)
    arrived = lax.all_to_all(buffer, "space", split_axis=0, concat_axis=0, tiled=True)
    arrived = arrived.reshape(slots, step_count + 1)
    cell_of = arrived[:, step_count].astype(jnp.int32)
    gathering = (
        cell_of[:, None] == jnp.arange(1, surface + 1, dtype=jnp.int32)[None, :]
    ).astype(jnp.float32)
    source = lax.dot_general(
        gathering,
        arrived[:, :step_count],
        (((0,), (0,)), ((), ())),
        precision=lax.Precision.HIGHEST,
    )
    source = source.reshape(cells_y, cells_x, step_count)
    shift_rows = offsets[0]
    speed_sq = velocity[0]
    previous = adjoint_prev[0]
    current = adjoint_now[0]
    forward = forward_accel[0]
    imaging = jnp.zeros_like(current)
    width = 4
    first = current[:, :width]
    last = current[:, cells_x - width :]
    for moment in range(step_count):
        lo, hi = halo(first, last)
        advanced, imaging, first, last = step_call(
            moment, current, previous, lo, hi, speed_sq, forward, source, imaging
        )
        previous, current = (current, advanced)
    row_index = jnp.arange(lax.axis_size("shot") * block_rows, dtype=jnp.int32) - shift_rows
    inside = (row_index >= 0) & (row_index < cells_y)
    chosen = jnp.take(imaging, jnp.clip(row_index, 0, cells_y - 1), axis=0)
    placed = jnp.where(inside[:, None, None], chosen, 0.0)
    shots = lax.axis_size("shot")
    placed = placed.reshape((shots, block_rows) + placed.shape[1:])
    arrived = lax.all_to_all(placed, "shot", split_axis=0, concat_axis=0, tiled=True)
    gradient = jnp.sum(arrived, axis=0)
    return (gradient, current[None])


def solution(mesh):
    in_specs = (
        P("shot", "space", None),
        P("shot", "space", None),
        P("shot", "space"),
        P(),
        P("shot"),
        P("shot", None, "space", None),
        P("shot", None, "space", None),
        P("shot", None, "space", None),
        P("shot", None, None, "space", None),
    )
    out_specs = (P("shot", "space", None), P("shot", None, "space", None))
    return jax.shard_map(local, mesh=mesh, in_specs=in_specs, out_specs=out_specs, check_vma=False)
```

```python
import functools

import jax
import jax.numpy as jnp
from jax import lax
from jax.sharding import PartitionSpec as P
from jax.experimental import pallas as pl
from jax.experimental.pallas import tpu as pltpu

STENCIL = (-205.0 / 72.0, 8.0 / 5.0, -1.0 / 5.0, 8.0 / 315.0, -1.0 / 560.0)


def extended(shard, sides, width):
    for axis, dim in sides:
        devices, length = (lax.axis_size(axis), shard.shape[dim])
        up = [(i, (i + 1) % devices) for i in range(devices - 1)]
        down = [(j, i) for i, j in up]
        last = lax.slice_in_dim(shard, length - width, length, axis=dim)
        leading = lax.slice_in_dim(shard, 0, width, axis=dim)
        before = lax.ppermute(last, axis, up)
        after = lax.ppermute(leading, axis, down)
        shard = jnp.concatenate([before, shard, after], axis=dim)
    return shard


def laplace(padded):
    span_y = padded.shape[0] - 8
    span_x = padded.shape[1] - 8
    span_z = padded.shape[2] - 8

    def window(shift_y, shift_x, shift_z):
        return padded[
            4 + shift_y : 4 + shift_y + span_y,
            4 + shift_x : 4 + shift_x + span_x,
            4 + shift_z : 4 + shift_z + span_z,
        ]

    summed = 3.0 * STENCIL[0] * window(0, 0, 0)
    for reach in range(1, 5):
        beside_all = (
            window(reach, 0, 0)
            + window(-reach, 0, 0)
            + window(0, reach, 0)
            + window(0, -reach, 0)
            + window(0, 0, reach)
            + window(0, 0, -reach)
        )
        summed = summed + STENCIL[reach] * beside_all
    return summed


def pad_sides(field):
    return jnp.pad(field, ((4, 4), (0, 0), (4, 4)))


ROWS = 1
BLOCK = 8


def step_kernel(moment, cur_ref, prev_ref, lo_ref, hi_ref, vel_ref, fwd_ref, src_ref, img_ref,
                next_ref, img_out_ref, first_ref, last_ref, pad_ref):
    cells_y, cells_x, cells_z = cur_ref.shape
    width = lo_ref.shape[1]
    block = pl.program_id(0)

    @pl.when(block == 0)
    def _():
        zeros = jnp.zeros((4, pad_ref.shape[1], cells_z), jnp.float32)
        pad_ref[0:4] = zeros
        pad_ref[4 + cells_y : 8 + cells_y] = zeros
        pad_ref[4 : 4 + cells_y, 8 - width : 8] = lo_ref[...]
        pad_ref[4 : 4 + cells_y, 8 : 8 + cells_x] = cur_ref[...]
        pad_ref[4 : 4 + cells_y, 8 + cells_x : 8 + cells_x + width] = hi_ref[...]

    def body(chunk, carry):
        y0 = pl.multiple_of(chunk * ROWS, ROWS)
        base = block * BLOCK + y0 + 4

        def window(shift_y, shift_x):
            return pad_ref[pl.ds(base + shift_y, ROWS), 8 + shift_x : 8 + shift_x + cells_x, :]

        center = window(0, 0)
        depth = lax.broadcasted_iota(jnp.int32, center.shape, 2)
        half = cells_z // 2
        low, high = center[..., :half], center[..., half:]
        lane = lax.broadcasted_iota(jnp.int32, low.shape, 2)

        def along_z(reach):
            low_up = pltpu.roll(low, half - reach, 2)
            high_up = pltpu.roll(high, half - reach, 2)
            low_down = pltpu.roll(low, reach, 2)
            high_down = pltpu.roll(high, reach, 2)
            head = lane < half - reach
            tail = lane >= reach
            up = jnp.concatenate(
                [jnp.where(head, low_up, high_up), jnp.where(head, high_up, 0.0)], axis=2
            )
            down = jnp.concatenate(
                [jnp.where(tail, low_down, 0.0), jnp.where(tail, high_down, low_down)], axis=2
            )
            return up, down

        summed = 3.0 * STENCIL[0] * center
        for reach in range(1, 5):
            z_up, z_down = along_z(reach)
            beside_all = (
                window(reach, 0)
                + window(-reach, 0)
                + window(0, reach)
                + window(0, -reach)
                + z_up
                + z_down
            )
            summed = summed + STENCIL[reach] * beside_all
        rows = pl.ds(y0, ROWS)
        advanced = 2.0 * center - prev_ref[rows] + vel_ref[rows] * summed
        source_rows = pl.ds(block * BLOCK + y0, ROWS)
        source = jnp.broadcast_to(src_ref[source_rows, :, pl.ds(moment, 1)], advanced.shape)
        advanced = jnp.where(depth == 0, advanced + source, advanced)
        next_ref[rows] = advanced
        img_out_ref[rows] = img_ref[rows] + fwd_ref[rows].astype(jnp.float32) * advanced
        first_ref[rows] = advanced[:, :width]
        last_ref[rows] = advanced[:, cells_x - width :]
        return carry

    lax.fori_loop(0, BLOCK // ROWS, body, 0, unroll=4)


def step_call(moment, current, previous, lo, hi, speed_sq, forward, source, imaging):
    cells_y, cells_x, cells_z = current.shape
    width = lo.shape[1]
    whole = pl.BlockSpec((cells_y, cells_x, cells_z), lambda i: (0, 0, 0))
    whole_rim = pl.BlockSpec((cells_y, width, cells_z), lambda i: (0, 0, 0))
    field = pl.BlockSpec((BLOCK, cells_x, cells_z), lambda i: (i, 0, 0))
    rim = pl.BlockSpec((BLOCK, width, cells_z), lambda i: (i, 0, 0))
    fwd_spec = pl.BlockSpec((None, BLOCK, cells_x, cells_z), lambda i: (moment, i, 0, 0))
    src_spec = pl.BlockSpec(source.shape, lambda i: (0, 0, 0))
    f32 = jnp.float32
    return pl.pallas_call(
        functools.partial(step_kernel, moment),
        grid=(cells_y // BLOCK,),
        out_shape=(
            jax.ShapeDtypeStruct(current.shape, f32),
            jax.ShapeDtypeStruct(current.shape, f32),
            jax.ShapeDtypeStruct(lo.shape, f32),
            jax.ShapeDtypeStruct(lo.shape, f32),
        ),
        in_specs=[whole, field, whole_rim, whole_rim, field, fwd_spec, src_spec, field],
        out_specs=(field, field, rim, rim),
        scratch_shapes=[pltpu.VMEM((cells_y + 8, cells_x + 16, cells_z), f32)],
        input_output_aliases={7: 1},
        compiler_params=pltpu.CompilerParams(
            dimension_semantics=("arbitrary",), vmem_limit_bytes=48 * 1024 * 1024
        ),
    )(current, previous, lo, hi, speed_sq, forward, source, imaging)


def halo(first, last):
    axis = "space"
    devices = lax.axis_size(axis)
    even = lax.axis_index(axis) % 2 == 0
    within = [(i, i ^ 1) for i in range(devices)]
    across = [(i, i + 1 - 2 * ((i + 1) % 2)) for i in range(1, devices - 1)]
    got_within = lax.ppermute(jnp.where(even, last, first), axis, within)
    got_across = lax.ppermute(jnp.where(even, first, last), axis, across)
    lo = jnp.where(even, got_across, got_within)
    hi = jnp.where(even, got_within, got_across)
    return lo, hi


def local(
    residual,
    record_tile,
    record_cell,
    time_filter,
    offsets,
    velocity,
    adjoint_prev,
    adjoint_now,
    forward_accel,
):
    tiles_count = lax.axis_size("space")
    record_count = residual.shape[1]
    cells_y = velocity.shape[1]
    cells_x = velocity.shape[2]
    step_count = forward_accel.shape[1]
    slot_count = record_count * 3 // 16
    surface = cells_y * cells_x
    block_rows = (cells_y + cells_y // 4) // lax.axis_size("shot")
    trace_rows = residual[0]
    tile_ids = record_tile[0, :, 0]
    cell_ids = record_cell[0]
    one_hot = (tile_ids[:, None] == jnp.arange(tiles_count, dtype=jnp.int32)[None, :]).astype(
        jnp.int32
    )
    order_rank = jnp.sum((jnp.cumsum(one_hot, axis=0) - 1) * one_hot, axis=1)
    slot_index = tile_ids * slot_count + order_rank
    filtered = jnp.dot(trace_rows, time_filter.T, preferred_element_type=jnp.float32)
    payload = jnp.concatenate(
        [filtered, (cell_ids + 1).astype(jnp.float32)[:, None]], axis=1
    )
    slots = tiles_count * slot_count
    placing = (
        slot_index[None, :] == jnp.arange(slots, dtype=jnp.int32)[:, None]
    ).astype(jnp.float32)
    buffer = jnp.dot(placing, payload, precision=lax.Precision.HIGHEST)
    buffer = buffer.reshape(tiles_count, slot_count, step_count + 1)
    arrived = lax.all_to_all(buffer, "space", split_axis=0, concat_axis=0, tiled=True)
    arrived = arrived.reshape(slots, step_count + 1)
    cell_of = arrived[:, step_count].astype(jnp.int32)
    gathering = (
        cell_of[:, None] == jnp.arange(1, surface + 1, dtype=jnp.int32)[None, :]
    ).astype(jnp.float32)
    source = lax.dot_general(
        gathering,
        arrived[:, :step_count],
        (((0,), (0,)), ((), ())),
        precision=lax.Precision.HIGHEST,
    )
    source = source.reshape(cells_y, cells_x, step_count)
    shift_rows = offsets[0]
    speed_sq = velocity[0]
    previous = adjoint_prev[0]
    current = adjoint_now[0]
    forward = forward_accel[0]
    imaging = jnp.zeros_like(current)
    width = 4
    first = current[:, :width]
    last = current[:, cells_x - width :]
    for moment in range(step_count):
        lo, hi = halo(first, last)
        advanced, imaging, first, last = step_call(
            moment, current, previous, lo, hi, speed_sq, forward, source, imaging
        )
        previous, current = (current, advanced)
    row_index = jnp.arange(lax.axis_size("shot") * block_rows, dtype=jnp.int32) - shift_rows
    inside = (row_index >= 0) & (row_index < cells_y)
    chosen = jnp.take(imaging, jnp.clip(row_index, 0, cells_y - 1), axis=0)
    placed = jnp.where(inside[:, None, None], chosen, 0.0)
    shots = lax.axis_size("shot")
    placed = placed.reshape((shots, block_rows) + placed.shape[1:])
    arrived = lax.all_to_all(placed, "shot", split_axis=0, concat_axis=0, tiled=True)
    gradient = jnp.sum(arrived, axis=0)
    return (gradient, current[None])


def solution(mesh):
    in_specs = (
        P("shot", "space", None),
        P("shot", "space", None),
        P("shot", "space"),
        P(),
        P("shot"),
        P("shot", None, "space", None),
        P("shot", None, "space", None),
        P("shot", None, "space", None),
        P("shot", None, None, "space", None),
    )
    out_specs = (P("shot", "space", None), P("shot", None, "space", None))
    return jax.shard_map(local, mesh=mesh, in_specs=in_specs, out_specs=out_specs, check_vma=False)
```

```python
import functools

import jax
import jax.numpy as jnp
from jax import lax
from jax.sharding import PartitionSpec as P
from jax.experimental import pallas as pl
from jax.experimental.pallas import tpu as pltpu

STENCIL = (-205.0 / 72.0, 8.0 / 5.0, -1.0 / 5.0, 8.0 / 315.0, -1.0 / 560.0)


def extended(shard, sides, width):
    for axis, dim in sides:
        devices, length = (lax.axis_size(axis), shard.shape[dim])
        up = [(i, (i + 1) % devices) for i in range(devices - 1)]
        down = [(j, i) for i, j in up]
        last = lax.slice_in_dim(shard, length - width, length, axis=dim)
        leading = lax.slice_in_dim(shard, 0, width, axis=dim)
        before = lax.ppermute(last, axis, up)
        after = lax.ppermute(leading, axis, down)
        shard = jnp.concatenate([before, shard, after], axis=dim)
    return shard


def laplace(padded):
    span_y = padded.shape[0] - 8
    span_x = padded.shape[1] - 8
    span_z = padded.shape[2] - 8

    def window(shift_y, shift_x, shift_z):
        return padded[
            4 + shift_y : 4 + shift_y + span_y,
            4 + shift_x : 4 + shift_x + span_x,
            4 + shift_z : 4 + shift_z + span_z,
        ]

    summed = 3.0 * STENCIL[0] * window(0, 0, 0)
    for reach in range(1, 5):
        beside_all = (
            window(reach, 0, 0)
            + window(-reach, 0, 0)
            + window(0, reach, 0)
            + window(0, -reach, 0)
            + window(0, 0, reach)
            + window(0, 0, -reach)
        )
        summed = summed + STENCIL[reach] * beside_all
    return summed


def pad_sides(field):
    return jnp.pad(field, ((4, 4), (0, 0), (4, 4)))


ROWS = 1
BLOCK = 8


def step_kernel(moment, cur_ref, prev_ref, lo_ref, hi_ref, vel_ref, fwd_ref, src_ref, img_ref,
                next_ref, img_out_ref, first_ref, last_ref, pad_ref):
    cells_y, cells_x, cells_z = cur_ref.shape
    width = lo_ref.shape[1]
    block = pl.program_id(0)

    @pl.when(block == 0)
    def _():
        zeros = jnp.zeros((4, pad_ref.shape[1], cells_z), jnp.float32)
        pad_ref[0:4] = zeros
        pad_ref[4 + cells_y : 8 + cells_y] = zeros
        pad_ref[4 : 4 + cells_y, 8 - width : 8] = lo_ref[...]
        pad_ref[4 : 4 + cells_y, 8 : 8 + cells_x] = cur_ref[...]
        pad_ref[4 : 4 + cells_y, 8 + cells_x : 8 + cells_x + width] = hi_ref[...]

    def body(chunk, carry):
        y0 = pl.multiple_of(chunk * ROWS, ROWS)
        base = block * BLOCK + y0 + 4

        def window(shift_y, shift_x):
            return pad_ref[pl.ds(base + shift_y, ROWS), 8 + shift_x : 8 + shift_x + cells_x, :]

        center = window(0, 0)
        depth = lax.broadcasted_iota(jnp.int32, center.shape, 2)
        half = cells_z // 2
        low, high = center[..., :half], center[..., half:]
        lane = lax.broadcasted_iota(jnp.int32, low.shape, 2)

        def along_z(reach):
            low_up = pltpu.roll(low, half - reach, 2)
            high_up = pltpu.roll(high, half - reach, 2)
            low_down = pltpu.roll(low, reach, 2)
            high_down = pltpu.roll(high, reach, 2)
            head = lane < half - reach
            tail = lane >= reach
            up = jnp.concatenate(
                [jnp.where(head, low_up, high_up), jnp.where(head, high_up, 0.0)], axis=2
            )
            down = jnp.concatenate(
                [jnp.where(tail, low_down, 0.0), jnp.where(tail, high_down, low_down)], axis=2
            )
            return up, down

        summed = 3.0 * STENCIL[0] * center
        for reach in range(1, 5):
            z_up, z_down = along_z(reach)
            beside_all = (
                window(reach, 0)
                + window(-reach, 0)
                + window(0, reach)
                + window(0, -reach)
                + z_up
                + z_down
            )
            summed = summed + STENCIL[reach] * beside_all
        rows = pl.ds(y0, ROWS)
        advanced = 2.0 * center - prev_ref[rows] + vel_ref[rows] * summed
        source_rows = pl.ds(block * BLOCK + y0, ROWS)
        source = jnp.broadcast_to(src_ref[source_rows, :, pl.ds(moment, 1)], advanced.shape)
        advanced = jnp.where(depth == 0, advanced + source, advanced)
        next_ref[rows] = advanced
        img_out_ref[rows] = img_ref[rows] + fwd_ref[rows].astype(jnp.float32) * advanced
        first_ref[rows] = advanced[:, :width]
        last_ref[rows] = advanced[:, cells_x - width :]
        return carry

    lax.fori_loop(0, BLOCK // ROWS, body, 0, unroll=4)


def step_call(moment, current, previous, lo, hi, speed_sq, forward, source, imaging):
    cells_y, cells_x, cells_z = current.shape
    width = lo.shape[1]
    whole = pl.BlockSpec((cells_y, cells_x, cells_z), lambda i: (0, 0, 0))
    whole_rim = pl.BlockSpec((cells_y, width, cells_z), lambda i: (0, 0, 0))
    field = pl.BlockSpec((BLOCK, cells_x, cells_z), lambda i: (i, 0, 0))
    rim = pl.BlockSpec((BLOCK, width, cells_z), lambda i: (i, 0, 0))
    fwd_spec = pl.BlockSpec((None, BLOCK, cells_x, cells_z), lambda i: (moment, i, 0, 0))
    src_spec = pl.BlockSpec(source.shape, lambda i: (0, 0, 0))
    f32 = jnp.float32
    return pl.pallas_call(
        functools.partial(step_kernel, moment),
        grid=(cells_y // BLOCK,),
        out_shape=(
            jax.ShapeDtypeStruct(current.shape, f32),
            jax.ShapeDtypeStruct(current.shape, f32),
            jax.ShapeDtypeStruct(lo.shape, f32),
            jax.ShapeDtypeStruct(lo.shape, f32),
        ),
        in_specs=[whole, field, whole_rim, whole_rim, field, fwd_spec, src_spec, field],
        out_specs=(field, field, rim, rim),
        scratch_shapes=[pltpu.VMEM((cells_y + 8, cells_x + 16, cells_z), f32)],
        input_output_aliases={7: 1},
        compiler_params=pltpu.CompilerParams(
            dimension_semantics=("arbitrary",), vmem_limit_bytes=48 * 1024 * 1024
        ),
    )(current, previous, lo, hi, speed_sq, forward, source, imaging)


def tile_kernel(moment, tile_ref, cur_ref, prev_ref, halo_ref, vel_ref, fwd_ref, src_ref, img_ref,
                chain_ref, next_ref, img_out_ref, edge_ref, pad_ref):
    del chain_ref
    cells_y, cells_x, cells_z = cur_ref.shape
    width = halo_ref.shape[1]
    part = cells_x // 2
    zeros = jnp.zeros((4, pad_ref.shape[1], cells_z), jnp.float32)
    pad_ref[0:4] = zeros
    pad_ref[4 + cells_y : 8 + cells_y] = zeros
    pad_ref[4 : 4 + cells_y, 8 : 8 + cells_x] = cur_ref[...]

    def compute(tile):
        if tile == 0:
            pad_ref[4 : 4 + cells_y, 8 - width : 8] = halo_ref[...]
        else:
            pad_ref[4 : 4 + cells_y, 8 + cells_x : 8 + cells_x + width] = halo_ref[...]
        start = 8 + tile * part

        def body(chunk, carry):
            y0 = chunk * ROWS
            base = y0 + 4

            def window(shift_y, shift_x):
                return pad_ref[
                    pl.ds(base + shift_y, ROWS), start + shift_x : start + shift_x + part, :
                ]

            center = window(0, 0)
            depth = lax.broadcasted_iota(jnp.int32, center.shape, 2)

            def along_z(reach):
                up = pltpu.roll(center, cells_z - reach, 2)
                down = pltpu.roll(center, reach, 2)
                return (
                    jnp.where(depth + reach < cells_z, up, 0.0),
                    jnp.where(depth - reach >= 0, down, 0.0),
                )

            summed = 3.0 * STENCIL[0] * center
            for reach in range(1, 5):
                z_up, z_down = along_z(reach)
                beside_all = (
                    window(reach, 0)
                    + window(-reach, 0)
                    + window(0, reach)
                    + window(0, -reach)
                    + z_up
                    + z_down
                )
                summed = summed + STENCIL[reach] * beside_all
            rows = pl.ds(y0, ROWS)
            advanced = 2.0 * center - prev_ref[rows] + vel_ref[rows] * summed
            source = src_ref[rows, tile * part : (tile + 1) * part, pl.ds(moment, 1)]
            source = jnp.broadcast_to(source, advanced.shape)
            advanced = jnp.where(depth == 0, advanced + source, advanced)
            next_ref[rows] = advanced
            accel = fwd_ref[rows].astype(jnp.float32)[:, tile * part : (tile + 1) * part]
            img_out_ref[rows] = img_ref[rows] + accel * advanced
            if tile == 0:
                edge_ref[rows] = advanced[:, :width]
            else:
                edge_ref[rows] = advanced[:, part - width :]
            return carry

        lax.fori_loop(0, cells_y // ROWS, body, 0, unroll=4)

    for tile in range(2):
        pl.when(tile_ref[0] == tile)(functools.partial(compute, tile))


def tile_call(moment, tile, current, previous, halo_rim, speed_sq, forward, source, imaging, chain):
    cells_y, cells_x, cells_z = current.shape
    width = halo_rim.shape[1]
    part = cells_x // 2
    whole = pl.BlockSpec((cells_y, cells_x, cells_z), lambda i, t: (0, 0, 0))
    rim = pl.BlockSpec((cells_y, width, cells_z), lambda i, t: (0, 0, 0))
    half = pl.BlockSpec((cells_y, part, cells_z), lambda i, t: (0, t[0], 0))
    fwd_spec = pl.BlockSpec((None, cells_y, cells_x, cells_z), lambda i, t: (moment, 0, 0, 0))
    src_spec = pl.BlockSpec(source.shape, lambda i, t: (0, 0, 0))
    f32 = jnp.float32
    cells = cells_y * part * cells_z
    return pl.pallas_call(
        functools.partial(tile_kernel, moment),
        grid_spec=pltpu.PrefetchScalarGridSpec(
            num_scalar_prefetch=1,
            grid=(1,),
            in_specs=[whole, half, rim, half, fwd_spec, src_spec, half,
                      pl.BlockSpec(memory_space=pl.ANY)],
            out_specs=(half, half, rim),
            scratch_shapes=[pltpu.VMEM((cells_y + 8, cells_x + 16, cells_z), f32)],
        ),
        out_shape=(
            jax.ShapeDtypeStruct(current.shape, f32),
            jax.ShapeDtypeStruct(current.shape, f32),
            jax.ShapeDtypeStruct(halo_rim.shape, f32),
        ),
        input_output_aliases={7: 1, 8: 0},
        cost_estimate=pl.CostEstimate(
            flops=60 * cells, bytes_accessed=28 * cells, transcendentals=0
        ),
        compiler_params=pltpu.CompilerParams(vmem_limit_bytes=48 * 1024 * 1024),
    )(tile, current, previous, halo_rim, speed_sq, forward, source, imaging, chain)


def halo(first, last):
    axis = "space"
    devices = lax.axis_size(axis)
    even = lax.axis_index(axis) % 2 == 0
    within = [(i, i ^ 1) for i in range(devices)]
    across = [(i, i + 1 - 2 * ((i + 1) % 2)) for i in range(1, devices - 1)]
    got_within = lax.ppermute(jnp.where(even, last, first), axis, within)
    got_across = lax.ppermute(jnp.where(even, first, last), axis, across)
    lo = jnp.where(even, got_across, got_within)
    hi = jnp.where(even, got_within, got_across)
    return lo, hi


def local(
    residual,
    record_tile,
    record_cell,
    time_filter,
    offsets,
    velocity,
    adjoint_prev,
    adjoint_now,
    forward_accel,
):
    tiles_count = lax.axis_size("space")
    record_count = residual.shape[1]
    cells_y = velocity.shape[1]
    cells_x = velocity.shape[2]
    step_count = forward_accel.shape[1]
    slot_count = record_count * 3 // 16
    surface = cells_y * cells_x
    block_rows = (cells_y + cells_y // 4) // lax.axis_size("shot")
    trace_rows = residual[0]
    tile_ids = record_tile[0, :, 0]
    cell_ids = record_cell[0]
    one_hot = (tile_ids[:, None] == jnp.arange(tiles_count, dtype=jnp.int32)[None, :]).astype(
        jnp.int32
    )
    order_rank = jnp.sum((jnp.cumsum(one_hot, axis=0) - 1) * one_hot, axis=1)
    slot_index = tile_ids * slot_count + order_rank
    filtered = jnp.dot(trace_rows, time_filter.T, preferred_element_type=jnp.float32)
    payload = jnp.concatenate(
        [filtered, (cell_ids + 1).astype(jnp.float32)[:, None]], axis=1
    )
    slots = tiles_count * slot_count
    placing = (
        slot_index[None, :] == jnp.arange(slots, dtype=jnp.int32)[:, None]
    ).astype(jnp.float32)
    buffer = jnp.dot(placing, payload, precision=lax.Precision.HIGHEST)
    buffer = buffer.reshape(tiles_count, slot_count, step_count + 1)
    arrived = lax.all_to_all(buffer, "space", split_axis=0, concat_axis=0, tiled=True)
    arrived = arrived.reshape(slots, step_count + 1)
    cell_of = arrived[:, step_count].astype(jnp.int32)
    gathering = (
        cell_of[:, None] == jnp.arange(1, surface + 1, dtype=jnp.int32)[None, :]
    ).astype(jnp.float32)
    source = lax.dot_general(
        gathering,
        arrived[:, :step_count],
        (((0,), (0,)), ((), ())),
        precision=lax.Precision.HIGHEST,
    )
    source = source.reshape(cells_y, cells_x, step_count)
    shift_rows = offsets[0]
    speed_sq = velocity[0]
    previous = adjoint_prev[0]
    current = adjoint_now[0]
    forward = forward_accel[0]
    imaging = jnp.zeros_like(current)
    width = 4
    odd = lax.axis_index("space") % 2
    tile_near = (1 - odd).reshape(1).astype(jnp.int32)
    tile_far = odd.reshape(1).astype(jnp.int32)
    devices = lax.axis_size("space")
    within = [(i, i ^ 1) for i in range(devices)]
    across = [(i, i + 1 - 2 * ((i + 1) % 2)) for i in range(1, devices - 1)]
    first = current[:, :width]
    last = current[:, cells_x - width :]
    even = odd == 0
    near_edge = jnp.where(even, last, first)
    far_edge = jnp.where(even, first, last)
    for moment in range(step_count):
        near_halo = lax.ppermute(near_edge, "space", within)
        far_halo = lax.ppermute(far_edge, "space", across)
        partial_next, imaging, near_edge = tile_call(
            moment, tile_near, current, previous, near_halo, speed_sq, forward, source,
            imaging, jnp.zeros_like(current),
        )
        advanced, imaging, far_edge = tile_call(
            moment, tile_far, current, previous, far_halo, speed_sq, forward, source,
            imaging, partial_next,
        )
        previous, current = (current, advanced)
    row_index = jnp.arange(lax.axis_size("shot") * block_rows, dtype=jnp.int32) - shift_rows
    inside = (row_index >= 0) & (row_index < cells_y)
    chosen = jnp.take(imaging, jnp.clip(row_index, 0, cells_y - 1), axis=0)
    placed = jnp.where(inside[:, None, None], chosen, 0.0)
    shots = lax.axis_size("shot")
    placed = placed.reshape((shots, block_rows) + placed.shape[1:])
    arrived = lax.all_to_all(placed, "shot", split_axis=0, concat_axis=0, tiled=True)
    gradient = jnp.sum(arrived, axis=0)
    return (gradient, current[None])


def solution(mesh):
    in_specs = (
        P("shot", "space", None),
        P("shot", "space", None),
        P("shot", "space"),
        P(),
        P("shot"),
        P("shot", None, "space", None),
        P("shot", None, "space", None),
        P("shot", None, "space", None),
        P("shot", None, None, "space", None),
    )
    out_specs = (P("shot", "space", None), P("shot", None, "space", None))
    return jax.shard_map(local, mesh=mesh, in_specs=in_specs, out_specs=out_specs, check_vma=False)
```

```python
import functools

import jax
import jax.numpy as jnp
from jax import lax
from jax.sharding import PartitionSpec as P
from jax.experimental import pallas as pl
from jax.experimental.pallas import tpu as pltpu

STENCIL = (-205.0 / 72.0, 8.0 / 5.0, -1.0 / 5.0, 8.0 / 315.0, -1.0 / 560.0)


def extended(shard, sides, width):
    for axis, dim in sides:
        devices, length = (lax.axis_size(axis), shard.shape[dim])
        up = [(i, (i + 1) % devices) for i in range(devices - 1)]
        down = [(j, i) for i, j in up]
        last = lax.slice_in_dim(shard, length - width, length, axis=dim)
        leading = lax.slice_in_dim(shard, 0, width, axis=dim)
        before = lax.ppermute(last, axis, up)
        after = lax.ppermute(leading, axis, down)
        shard = jnp.concatenate([before, shard, after], axis=dim)
    return shard


def laplace(padded):
    span_y = padded.shape[0] - 8
    span_x = padded.shape[1] - 8
    span_z = padded.shape[2] - 8

    def window(shift_y, shift_x, shift_z):
        return padded[
            4 + shift_y : 4 + shift_y + span_y,
            4 + shift_x : 4 + shift_x + span_x,
            4 + shift_z : 4 + shift_z + span_z,
        ]

    summed = 3.0 * STENCIL[0] * window(0, 0, 0)
    for reach in range(1, 5):
        beside_all = (
            window(reach, 0, 0)
            + window(-reach, 0, 0)
            + window(0, reach, 0)
            + window(0, -reach, 0)
            + window(0, 0, reach)
            + window(0, 0, -reach)
        )
        summed = summed + STENCIL[reach] * beside_all
    return summed


def pad_sides(field):
    return jnp.pad(field, ((4, 4), (0, 0), (4, 4)))


ROWS = 1
BLOCK = 8
SLAB_ROWS = 4
SLAB_UNROLL = 2


def step_kernel(moment, cur_ref, prev_ref, lo_ref, hi_ref, vel_ref, fwd_ref, src_ref, img_ref,
                next_ref, img_out_ref, first_ref, last_ref, pad_ref):
    cells_y, cells_x, cells_z = cur_ref.shape
    width = lo_ref.shape[1]
    block = pl.program_id(0)

    @pl.when(block == 0)
    def _():
        zeros = jnp.zeros((4, pad_ref.shape[1], cells_z), jnp.float32)
        pad_ref[0:4] = zeros
        pad_ref[4 + cells_y : 8 + cells_y] = zeros
        pad_ref[4 : 4 + cells_y, 8 - width : 8] = lo_ref[...]
        pad_ref[4 : 4 + cells_y, 8 : 8 + cells_x] = cur_ref[...]
        pad_ref[4 : 4 + cells_y, 8 + cells_x : 8 + cells_x + width] = hi_ref[...]

    def body(chunk, carry):
        y0 = pl.multiple_of(chunk * ROWS, ROWS)
        base = block * BLOCK + y0 + 4

        def window(shift_y, shift_x):
            return pad_ref[pl.ds(base + shift_y, ROWS), 8 + shift_x : 8 + shift_x + cells_x, :]

        center = window(0, 0)
        depth = lax.broadcasted_iota(jnp.int32, center.shape, 2)
        half = cells_z // 2
        low, high = center[..., :half], center[..., half:]
        lane = lax.broadcasted_iota(jnp.int32, low.shape, 2)

        def along_z(reach):
            low_up = pltpu.roll(low, half - reach, 2)
            high_up = pltpu.roll(high, half - reach, 2)
            low_down = pltpu.roll(low, reach, 2)
            high_down = pltpu.roll(high, reach, 2)
            head = lane < half - reach
            tail = lane >= reach
            up = jnp.concatenate(
                [jnp.where(head, low_up, high_up), jnp.where(head, high_up, 0.0)], axis=2
            )
            down = jnp.concatenate(
                [jnp.where(tail, low_down, 0.0), jnp.where(tail, high_down, low_down)], axis=2
            )
            return up, down

        summed = 3.0 * STENCIL[0] * center
        for reach in range(1, 5):
            z_up, z_down = along_z(reach)
            beside_all = (
                window(reach, 0)
                + window(-reach, 0)
                + window(0, reach)
                + window(0, -reach)
                + z_up
                + z_down
            )
            summed = summed + STENCIL[reach] * beside_all
        rows = pl.ds(y0, ROWS)
        advanced = 2.0 * center - prev_ref[rows] + vel_ref[rows] * summed
        source_rows = pl.ds(block * BLOCK + y0, ROWS)
        source = jnp.broadcast_to(src_ref[source_rows, :, pl.ds(moment, 1)], advanced.shape)
        advanced = jnp.where(depth == 0, advanced + source, advanced)
        next_ref[rows] = advanced
        img_out_ref[rows] = img_ref[rows] + fwd_ref[rows].astype(jnp.float32) * advanced
        first_ref[rows] = advanced[:, :width]
        last_ref[rows] = advanced[:, cells_x - width :]
        return carry

    lax.fori_loop(0, BLOCK // ROWS, body, 0, unroll=4)


def step_call(moment, current, previous, lo, hi, speed_sq, forward, source, imaging):
    cells_y, cells_x, cells_z = current.shape
    width = lo.shape[1]
    whole = pl.BlockSpec((cells_y, cells_x, cells_z), lambda i: (0, 0, 0))
    whole_rim = pl.BlockSpec((cells_y, width, cells_z), lambda i: (0, 0, 0))
    field = pl.BlockSpec((BLOCK, cells_x, cells_z), lambda i: (i, 0, 0))
    rim = pl.BlockSpec((BLOCK, width, cells_z), lambda i: (i, 0, 0))
    fwd_spec = pl.BlockSpec((None, BLOCK, cells_x, cells_z), lambda i: (moment, i, 0, 0))
    src_spec = pl.BlockSpec(source.shape, lambda i: (0, 0, 0))
    f32 = jnp.float32
    return pl.pallas_call(
        functools.partial(step_kernel, moment),
        grid=(cells_y // BLOCK,),
        out_shape=(
            jax.ShapeDtypeStruct(current.shape, f32),
            jax.ShapeDtypeStruct(current.shape, f32),
            jax.ShapeDtypeStruct(lo.shape, f32),
            jax.ShapeDtypeStruct(lo.shape, f32),
        ),
        in_specs=[whole, field, whole_rim, whole_rim, field, fwd_spec, src_spec, field],
        out_specs=(field, field, rim, rim),
        scratch_shapes=[pltpu.VMEM((cells_y + 8, cells_x + 16, cells_z), f32)],
        input_output_aliases={7: 1},
        compiler_params=pltpu.CompilerParams(
            dimension_semantics=("arbitrary",), vmem_limit_bytes=48 * 1024 * 1024
        ),
    )(current, previous, lo, hi, speed_sq, forward, source, imaging)


def tile_kernel(moment, tile_ref, cur_ref, prev_ref, halo_ref, vel_ref, fwd_ref, src_ref, img_ref,
                chain_ref, next_ref, img_out_ref, edge_ref, pad_ref):
    del chain_ref
    cells_y, cells_x, cells_z = cur_ref.shape
    width = halo_ref.shape[1]
    part = cells_x // 2
    zeros = jnp.zeros((4, pad_ref.shape[1], cells_z), jnp.float32)
    pad_ref[0:4] = zeros
    pad_ref[4 + cells_y : 8 + cells_y] = zeros
    pad_ref[4 : 4 + cells_y, 8 : 8 + cells_x] = cur_ref[...]

    def compute(tile):
        if tile == 0:
            pad_ref[4 : 4 + cells_y, 8 - width : 8] = halo_ref[...]
        else:
            pad_ref[4 : 4 + cells_y, 8 + cells_x : 8 + cells_x + width] = halo_ref[...]
        start = 8 + tile * part

        def body(chunk, carry):
            y0 = chunk * SLAB_ROWS
            base = y0 + 4
            slab = pad_ref[pl.ds(base - 4, SLAB_ROWS + 8), start : start + part, :]

            def window(shift_y, shift_x):
                if shift_x == 0:
                    return slab[4 + shift_y : 4 + shift_y + SLAB_ROWS]
                return pad_ref[
                    pl.ds(base + shift_y, SLAB_ROWS), start + shift_x : start + shift_x + part, :
                ]

            center = window(0, 0)
            depth = lax.broadcasted_iota(jnp.int32, center.shape, 2)

            def along_z(reach):
                up = pltpu.roll(center, cells_z - reach, 2)
                down = pltpu.roll(center, reach, 2)
                return (
                    jnp.where(depth + reach < cells_z, up, 0.0),
                    jnp.where(depth - reach >= 0, down, 0.0),
                )

            summed = 3.0 * STENCIL[0] * center
            for reach in range(1, 5):
                z_up, z_down = along_z(reach)
                beside_all = (
                    window(reach, 0)
                    + window(-reach, 0)
                    + window(0, reach)
                    + window(0, -reach)
                    + z_up
                    + z_down
                )
                summed = summed + STENCIL[reach] * beside_all
            rows = pl.ds(y0, SLAB_ROWS)
            advanced = 2.0 * center - prev_ref[rows] + vel_ref[rows] * summed
            source = src_ref[rows, tile * part : (tile + 1) * part, pl.ds(moment, 1)]
            source = jnp.broadcast_to(source, advanced.shape)
            advanced = jnp.where(depth == 0, advanced + source, advanced)
            next_ref[rows] = advanced
            accel = fwd_ref[rows].astype(jnp.float32)[:, tile * part : (tile + 1) * part]
            img_out_ref[rows] = img_ref[rows] + accel * advanced
            if tile == 0:
                edge_ref[rows] = advanced[:, :width]
            else:
                edge_ref[rows] = advanced[:, part - width :]
            return carry

        lax.fori_loop(0, cells_y // SLAB_ROWS, body, 0, unroll=SLAB_UNROLL)

    for tile in range(2):
        pl.when(tile_ref[0] == tile)(functools.partial(compute, tile))


def tile_call(moment, tile, current, previous, halo_rim, speed_sq, forward, source, imaging, chain):
    cells_y, cells_x, cells_z = current.shape
    width = halo_rim.shape[1]
    part = cells_x // 2
    whole = pl.BlockSpec((cells_y, cells_x, cells_z), lambda i, t: (0, 0, 0))
    rim = pl.BlockSpec((cells_y, width, cells_z), lambda i, t: (0, 0, 0))
    half = pl.BlockSpec((cells_y, part, cells_z), lambda i, t: (0, t[0], 0))
    fwd_spec = pl.BlockSpec((None, cells_y, cells_x, cells_z), lambda i, t: (moment, 0, 0, 0))
    src_spec = pl.BlockSpec(source.shape, lambda i, t: (0, 0, 0))
    f32 = jnp.float32
    cells = cells_y * part * cells_z
    return pl.pallas_call(
        functools.partial(tile_kernel, moment),
        grid_spec=pltpu.PrefetchScalarGridSpec(
            num_scalar_prefetch=1,
            grid=(1,),
            in_specs=[whole, half, rim, half, fwd_spec, src_spec, half,
                      pl.BlockSpec(memory_space=pl.ANY)],
            out_specs=(half, half, rim),
            scratch_shapes=[pltpu.VMEM((cells_y + 8, cells_x + 16, cells_z), f32)],
        ),
        out_shape=(
            jax.ShapeDtypeStruct(current.shape, f32),
            jax.ShapeDtypeStruct(current.shape, f32),
            jax.ShapeDtypeStruct(halo_rim.shape, f32),
        ),
        input_output_aliases={7: 1, 8: 0},
        cost_estimate=pl.CostEstimate(
            flops=60 * cells, bytes_accessed=28 * cells, transcendentals=0
        ),
        compiler_params=pltpu.CompilerParams(vmem_limit_bytes=48 * 1024 * 1024),
    )(tile, current, previous, halo_rim, speed_sq, forward, source, imaging, chain)


def halo(first, last):
    axis = "space"
    devices = lax.axis_size(axis)
    even = lax.axis_index(axis) % 2 == 0
    within = [(i, i ^ 1) for i in range(devices)]
    across = [(i, i + 1 - 2 * ((i + 1) % 2)) for i in range(1, devices - 1)]
    got_within = lax.ppermute(jnp.where(even, last, first), axis, within)
    got_across = lax.ppermute(jnp.where(even, first, last), axis, across)
    lo = jnp.where(even, got_across, got_within)
    hi = jnp.where(even, got_within, got_across)
    return lo, hi


def local(
    residual,
    record_tile,
    record_cell,
    time_filter,
    offsets,
    velocity,
    adjoint_prev,
    adjoint_now,
    forward_accel,
):
    tiles_count = lax.axis_size("space")
    record_count = residual.shape[1]
    cells_y = velocity.shape[1]
    cells_x = velocity.shape[2]
    step_count = forward_accel.shape[1]
    slot_count = record_count * 3 // 16
    surface = cells_y * cells_x
    block_rows = (cells_y + cells_y // 4) // lax.axis_size("shot")
    trace_rows = residual[0]
    tile_ids = record_tile[0, :, 0]
    cell_ids = record_cell[0]
    one_hot = (tile_ids[:, None] == jnp.arange(tiles_count, dtype=jnp.int32)[None, :]).astype(
        jnp.int32
    )
    order_rank = jnp.sum((jnp.cumsum(one_hot, axis=0) - 1) * one_hot, axis=1)
    slot_index = tile_ids * slot_count + order_rank
    filtered = jnp.dot(trace_rows, time_filter.T, preferred_element_type=jnp.float32)
    payload = jnp.concatenate(
        [filtered, (cell_ids + 1).astype(jnp.float32)[:, None]], axis=1
    )
    slots = tiles_count * slot_count
    placing = (
        slot_index[None, :] == jnp.arange(slots, dtype=jnp.int32)[:, None]
    ).astype(jnp.float32)
    buffer = jnp.dot(placing, payload, precision=lax.Precision.HIGHEST)
    buffer = buffer.reshape(tiles_count, slot_count, step_count + 1)
    arrived = lax.all_to_all(buffer, "space", split_axis=0, concat_axis=0, tiled=True)
    arrived = arrived.reshape(slots, step_count + 1)
    cell_of = arrived[:, step_count].astype(jnp.int32)
    gathering = (
        cell_of[:, None] == jnp.arange(1, surface + 1, dtype=jnp.int32)[None, :]
    ).astype(jnp.float32)
    source = lax.dot_general(
        gathering,
        arrived[:, :step_count],
        (((0,), (0,)), ((), ())),
        precision=lax.Precision.HIGHEST,
    )
    source = source.reshape(cells_y, cells_x, step_count)
    shift_rows = offsets[0]
    speed_sq = velocity[0]
    previous = adjoint_prev[0]
    current = adjoint_now[0]
    forward = forward_accel[0]
    imaging = jnp.zeros_like(current)
    width = 4
    odd = lax.axis_index("space") % 2
    tile_near = (1 - odd).reshape(1).astype(jnp.int32)
    tile_far = odd.reshape(1).astype(jnp.int32)
    devices = lax.axis_size("space")
    within = [(i, i ^ 1) for i in range(devices)]
    across = [(i, i + 1 - 2 * ((i + 1) % 2)) for i in range(1, devices - 1)]
    first = current[:, :width]
    last = current[:, cells_x - width :]
    even = odd == 0
    near_edge = jnp.where(even, last, first)
    far_edge = jnp.where(even, first, last)
    for moment in range(step_count):
        near_halo = lax.ppermute(near_edge, "space", within)
        far_halo = lax.ppermute(far_edge, "space", across)
        partial_next, imaging, near_edge = tile_call(
            moment, tile_near, current, previous, near_halo, speed_sq, forward, source,
            imaging, jnp.zeros_like(current),
        )
        advanced, imaging, far_edge = tile_call(
            moment, tile_far, current, previous, far_halo, speed_sq, forward, source,
            imaging, partial_next,
        )
        previous, current = (current, advanced)
    row_index = jnp.arange(lax.axis_size("shot") * block_rows, dtype=jnp.int32) - shift_rows
    inside = (row_index >= 0) & (row_index < cells_y)
    chosen = jnp.take(imaging, jnp.clip(row_index, 0, cells_y - 1), axis=0)
    placed = jnp.where(inside[:, None, None], chosen, 0.0)
    shots = lax.axis_size("shot")
    placed = placed.reshape((shots, block_rows) + placed.shape[1:])
    arrived = lax.all_to_all(placed, "shot", split_axis=0, concat_axis=0, tiled=True)
    gradient = jnp.sum(arrived, axis=0)
    return (gradient, current[None])


def solution(mesh):
    in_specs = (
        P("shot", "space", None),
        P("shot", "space", None),
        P("shot", "space"),
        P(),
        P("shot"),
        P("shot", None, "space", None),
        P("shot", None, "space", None),
        P("shot", None, "space", None),
        P("shot", None, None, "space", None),
    )
    out_specs = (P("shot", "space", None), P("shot", None, "space", None))
    return jax.shard_map(local, mesh=mesh, in_specs=in_specs, out_specs=out_specs, check_vma=False)
```

```python
import functools

import jax
import jax.numpy as jnp
from jax import lax
from jax.sharding import PartitionSpec as P
from jax.experimental import pallas as pl
from jax.experimental.pallas import tpu as pltpu

STENCIL = (-205.0 / 72.0, 8.0 / 5.0, -1.0 / 5.0, 8.0 / 315.0, -1.0 / 560.0)


def extended(shard, sides, width):
    for axis, dim in sides:
        devices, length = (lax.axis_size(axis), shard.shape[dim])
        up = [(i, (i + 1) % devices) for i in range(devices - 1)]
        down = [(j, i) for i, j in up]
        last = lax.slice_in_dim(shard, length - width, length, axis=dim)
        leading = lax.slice_in_dim(shard, 0, width, axis=dim)
        before = lax.ppermute(last, axis, up)
        after = lax.ppermute(leading, axis, down)
        shard = jnp.concatenate([before, shard, after], axis=dim)
    return shard


def laplace(padded):
    span_y = padded.shape[0] - 8
    span_x = padded.shape[1] - 8
    span_z = padded.shape[2] - 8

    def window(shift_y, shift_x, shift_z):
        return padded[
            4 + shift_y : 4 + shift_y + span_y,
            4 + shift_x : 4 + shift_x + span_x,
            4 + shift_z : 4 + shift_z + span_z,
        ]

    summed = 3.0 * STENCIL[0] * window(0, 0, 0)
    for reach in range(1, 5):
        beside_all = (
            window(reach, 0, 0)
            + window(-reach, 0, 0)
            + window(0, reach, 0)
            + window(0, -reach, 0)
            + window(0, 0, reach)
            + window(0, 0, -reach)
        )
        summed = summed + STENCIL[reach] * beside_all
    return summed


def pad_sides(field):
    return jnp.pad(field, ((4, 4), (0, 0), (4, 4)))


ROWS = 1
BLOCK = 8
SLAB_ROWS = 4
SLAB_UNROLL = 2


def step_kernel(moment, cur_ref, prev_ref, lo_ref, hi_ref, vel_ref, fwd_ref, src_ref, img_ref,
                next_ref, img_out_ref, first_ref, last_ref, pad_ref):
    cells_y, cells_x, cells_z = cur_ref.shape
    width = lo_ref.shape[1]
    block = pl.program_id(0)

    @pl.when(block == 0)
    def _():
        zeros = jnp.zeros((4, pad_ref.shape[1], cells_z), jnp.float32)
        pad_ref[0:4] = zeros
        pad_ref[4 + cells_y : 8 + cells_y] = zeros
        pad_ref[4 : 4 + cells_y, 8 - width : 8] = lo_ref[...]
        pad_ref[4 : 4 + cells_y, 8 : 8 + cells_x] = cur_ref[...]
        pad_ref[4 : 4 + cells_y, 8 + cells_x : 8 + cells_x + width] = hi_ref[...]

    def body(chunk, carry):
        y0 = pl.multiple_of(chunk * ROWS, ROWS)
        base = block * BLOCK + y0 + 4

        def window(shift_y, shift_x):
            return pad_ref[pl.ds(base + shift_y, ROWS), 8 + shift_x : 8 + shift_x + cells_x, :]

        center = window(0, 0)
        depth = lax.broadcasted_iota(jnp.int32, center.shape, 2)
        half = cells_z // 2
        low, high = center[..., :half], center[..., half:]
        lane = lax.broadcasted_iota(jnp.int32, low.shape, 2)

        def along_z(reach):
            low_up = pltpu.roll(low, half - reach, 2)
            high_up = pltpu.roll(high, half - reach, 2)
            low_down = pltpu.roll(low, reach, 2)
            high_down = pltpu.roll(high, reach, 2)
            head = lane < half - reach
            tail = lane >= reach
            up = jnp.concatenate(
                [jnp.where(head, low_up, high_up), jnp.where(head, high_up, 0.0)], axis=2
            )
            down = jnp.concatenate(
                [jnp.where(tail, low_down, 0.0), jnp.where(tail, high_down, low_down)], axis=2
            )
            return up, down

        summed = 3.0 * STENCIL[0] * center
        for reach in range(1, 5):
            z_up, z_down = along_z(reach)
            beside_all = (
                window(reach, 0)
                + window(-reach, 0)
                + window(0, reach)
                + window(0, -reach)
                + z_up
                + z_down
            )
            summed = summed + STENCIL[reach] * beside_all
        rows = pl.ds(y0, ROWS)
        advanced = 2.0 * center - prev_ref[rows] + vel_ref[rows] * summed
        source_rows = pl.ds(block * BLOCK + y0, ROWS)
        source = jnp.broadcast_to(src_ref[source_rows, :, pl.ds(moment, 1)], advanced.shape)
        advanced = jnp.where(depth == 0, advanced + source, advanced)
        next_ref[rows] = advanced
        img_out_ref[rows] = img_ref[rows] + fwd_ref[rows].astype(jnp.float32) * advanced
        first_ref[rows] = advanced[:, :width]
        last_ref[rows] = advanced[:, cells_x - width :]
        return carry

    lax.fori_loop(0, BLOCK // ROWS, body, 0, unroll=4)


def step_call(moment, current, previous, lo, hi, speed_sq, forward, source, imaging):
    cells_y, cells_x, cells_z = current.shape
    width = lo.shape[1]
    whole = pl.BlockSpec((cells_y, cells_x, cells_z), lambda i: (0, 0, 0))
    whole_rim = pl.BlockSpec((cells_y, width, cells_z), lambda i: (0, 0, 0))
    field = pl.BlockSpec((BLOCK, cells_x, cells_z), lambda i: (i, 0, 0))
    rim = pl.BlockSpec((BLOCK, width, cells_z), lambda i: (i, 0, 0))
    fwd_spec = pl.BlockSpec((None, BLOCK, cells_x, cells_z), lambda i: (moment, i, 0, 0))
    src_spec = pl.BlockSpec(source.shape, lambda i: (0, 0, 0))
    f32 = jnp.float32
    return pl.pallas_call(
        functools.partial(step_kernel, moment),
        grid=(cells_y // BLOCK,),
        out_shape=(
            jax.ShapeDtypeStruct(current.shape, f32),
            jax.ShapeDtypeStruct(current.shape, f32),
            jax.ShapeDtypeStruct(lo.shape, f32),
            jax.ShapeDtypeStruct(lo.shape, f32),
        ),
        in_specs=[whole, field, whole_rim, whole_rim, field, fwd_spec, src_spec, field],
        out_specs=(field, field, rim, rim),
        scratch_shapes=[pltpu.VMEM((cells_y + 8, cells_x + 16, cells_z), f32)],
        input_output_aliases={7: 1},
        compiler_params=pltpu.CompilerParams(
            dimension_semantics=("arbitrary",), vmem_limit_bytes=48 * 1024 * 1024
        ),
    )(current, previous, lo, hi, speed_sq, forward, source, imaging)


def tile_kernel(moment, chained, tile_ref, cur_ref, prev_ref, halo_ref, vel_ref, fwd_ref, src_ref,
                img_ref, *rest):
    if chained:
        rest = rest[1:]
    next_ref, img_out_ref, edge_ref, pad_ref = rest
    cells_y, cells_x, cells_z = cur_ref.shape
    width = halo_ref.shape[1]
    part = cells_x // 2
    zeros = jnp.zeros((4, pad_ref.shape[1], cells_z), jnp.float32)
    pad_ref[0:4] = zeros
    pad_ref[4 + cells_y : 8 + cells_y] = zeros
    pad_ref[4 : 4 + cells_y, 8 : 8 + cells_x] = cur_ref[...]

    def compute(tile):
        if tile == 0:
            pad_ref[4 : 4 + cells_y, 8 - width : 8] = halo_ref[...]
        else:
            pad_ref[4 : 4 + cells_y, 8 + cells_x : 8 + cells_x + width] = halo_ref[...]
        start = 8 + tile * part

        def body(chunk, carry):
            y0 = chunk * SLAB_ROWS
            base = y0 + 4
            slab = pad_ref[pl.ds(base - 4, SLAB_ROWS + 8), start : start + part, :]

            def window(shift_y, shift_x):
                if shift_x == 0:
                    return slab[4 + shift_y : 4 + shift_y + SLAB_ROWS]
                return pad_ref[
                    pl.ds(base + shift_y, SLAB_ROWS), start + shift_x : start + shift_x + part, :
                ]

            center = window(0, 0)
            depth = lax.broadcasted_iota(jnp.int32, center.shape, 2)

            def along_z(reach):
                up = pltpu.roll(center, cells_z - reach, 2)
                down = pltpu.roll(center, reach, 2)
                return (
                    jnp.where(depth + reach < cells_z, up, 0.0),
                    jnp.where(depth - reach >= 0, down, 0.0),
                )

            summed = 3.0 * STENCIL[0] * center
            for reach in range(1, 5):
                z_up, z_down = along_z(reach)
                beside_all = (
                    window(reach, 0)
                    + window(-reach, 0)
                    + window(0, reach)
                    + window(0, -reach)
                    + z_up
                    + z_down
                )
                summed = summed + STENCIL[reach] * beside_all
            rows = pl.ds(y0, SLAB_ROWS)
            advanced = 2.0 * center - prev_ref[rows] + vel_ref[rows] * summed
            source = src_ref[rows, tile * part : (tile + 1) * part, pl.ds(moment, 1)]
            source = jnp.broadcast_to(source, advanced.shape)
            advanced = jnp.where(depth == 0, advanced + source, advanced)
            next_ref[rows] = advanced
            accel = fwd_ref[rows].astype(jnp.float32)[:, tile * part : (tile + 1) * part]
            img_out_ref[rows] = img_ref[rows] + accel * advanced
            if tile == 0:
                edge_ref[rows] = advanced[:, :width]
            else:
                edge_ref[rows] = advanced[:, part - width :]
            return carry

        lax.fori_loop(0, cells_y // SLAB_ROWS, body, 0, unroll=SLAB_UNROLL)

    for tile in range(2):
        pl.when(tile_ref[0] == tile)(functools.partial(compute, tile))


def tile_call(moment, tile, current, previous, halo_rim, speed_sq, forward, source, imaging, chain):
    cells_y, cells_x, cells_z = current.shape
    width = halo_rim.shape[1]
    part = cells_x // 2
    whole = pl.BlockSpec((cells_y, cells_x, cells_z), lambda i, t: (0, 0, 0))
    rim = pl.BlockSpec((cells_y, width, cells_z), lambda i, t: (0, 0, 0))
    half = pl.BlockSpec((cells_y, part, cells_z), lambda i, t: (0, t[0], 0))
    fwd_spec = pl.BlockSpec((None, cells_y, cells_x, cells_z), lambda i, t: (moment, 0, 0, 0))
    src_spec = pl.BlockSpec(source.shape, lambda i, t: (0, 0, 0))
    f32 = jnp.float32
    cells = cells_y * part * cells_z
    chained = chain is not None
    in_specs = [whole, half, rim, half, fwd_spec, src_spec, half]
    operands = [tile, current, previous, halo_rim, speed_sq, forward, source, imaging]
    aliases = {7: 1}
    if chained:
        in_specs.append(pl.BlockSpec(memory_space=pl.ANY))
        operands.append(chain)
        aliases[8] = 0
    return pl.pallas_call(
        functools.partial(tile_kernel, moment, chained),
        grid_spec=pltpu.PrefetchScalarGridSpec(
            num_scalar_prefetch=1,
            grid=(1,),
            in_specs=in_specs,
            out_specs=(half, half, rim),
            scratch_shapes=[pltpu.VMEM((cells_y + 8, cells_x + 16, cells_z), f32)],
        ),
        out_shape=(
            jax.ShapeDtypeStruct(current.shape, f32),
            jax.ShapeDtypeStruct(current.shape, f32),
            jax.ShapeDtypeStruct(halo_rim.shape, f32),
        ),
        input_output_aliases=aliases,
        cost_estimate=pl.CostEstimate(
            flops=60 * cells, bytes_accessed=28 * cells, transcendentals=0
        ),
        compiler_params=pltpu.CompilerParams(vmem_limit_bytes=48 * 1024 * 1024),
    )(*operands)


def halo(first, last):
    axis = "space"
    devices = lax.axis_size(axis)
    even = lax.axis_index(axis) % 2 == 0
    within = [(i, i ^ 1) for i in range(devices)]
    across = [(i, i + 1 - 2 * ((i + 1) % 2)) for i in range(1, devices - 1)]
    got_within = lax.ppermute(jnp.where(even, last, first), axis, within)
    got_across = lax.ppermute(jnp.where(even, first, last), axis, across)
    lo = jnp.where(even, got_across, got_within)
    hi = jnp.where(even, got_within, got_across)
    return lo, hi


def local(
    residual,
    record_tile,
    record_cell,
    time_filter,
    offsets,
    velocity,
    adjoint_prev,
    adjoint_now,
    forward_accel,
):
    tiles_count = lax.axis_size("space")
    record_count = residual.shape[1]
    cells_y = velocity.shape[1]
    cells_x = velocity.shape[2]
    step_count = forward_accel.shape[1]
    slot_count = record_count * 3 // 16
    surface = cells_y * cells_x
    block_rows = (cells_y + cells_y // 4) // lax.axis_size("shot")
    trace_rows = residual[0]
    tile_ids = record_tile[0, :, 0]
    cell_ids = record_cell[0]
    one_hot = (tile_ids[:, None] == jnp.arange(tiles_count, dtype=jnp.int32)[None, :]).astype(
        jnp.int32
    )
    order_rank = jnp.sum((jnp.cumsum(one_hot, axis=0) - 1) * one_hot, axis=1)
    slot_index = tile_ids * slot_count + order_rank
    filtered = jnp.dot(trace_rows, time_filter.T, preferred_element_type=jnp.float32)
    payload = jnp.concatenate(
        [filtered, (cell_ids + 1).astype(jnp.float32)[:, None]], axis=1
    )
    slots = tiles_count * slot_count
    placing = (
        slot_index[None, :] == jnp.arange(slots, dtype=jnp.int32)[:, None]
    ).astype(jnp.float32)
    buffer = jnp.dot(placing, payload, precision=lax.Precision.HIGHEST)
    buffer = buffer.reshape(tiles_count, slot_count, step_count + 1)
    arrived = lax.all_to_all(buffer, "space", split_axis=0, concat_axis=0, tiled=True)
    arrived = arrived.reshape(slots, step_count + 1)
    cell_of = arrived[:, step_count].astype(jnp.int32)
    gathering = (
        cell_of[:, None] == jnp.arange(1, surface + 1, dtype=jnp.int32)[None, :]
    ).astype(jnp.float32)
    source = lax.dot_general(
        gathering,
        arrived[:, :step_count],
        (((0,), (0,)), ((), ())),
        precision=lax.Precision.HIGHEST,
    )
    source = source.reshape(cells_y, cells_x, step_count)
    shift_rows = offsets[0]
    speed_sq = velocity[0]
    previous = adjoint_prev[0]
    current = adjoint_now[0]
    forward = forward_accel[0]
    imaging = jnp.zeros_like(current)
    width = 4
    odd = lax.axis_index("space") % 2
    tile_near = (1 - odd).reshape(1).astype(jnp.int32)
    tile_far = odd.reshape(1).astype(jnp.int32)
    devices = lax.axis_size("space")
    within = [(i, i ^ 1) for i in range(devices)]
    across = [(i, i + 1 - 2 * ((i + 1) % 2)) for i in range(1, devices - 1)]
    first = current[:, :width]
    last = current[:, cells_x - width :]
    even = odd == 0
    near_edge = jnp.where(even, last, first)
    far_edge = jnp.where(even, first, last)
    for moment in range(step_count):
        near_halo = lax.ppermute(near_edge, "space", within)
        far_halo = lax.ppermute(far_edge, "space", across)
        partial_next, imaging, near_edge = tile_call(
            moment, tile_near, current, previous, near_halo, speed_sq, forward, source,
            imaging, None,
        )
        advanced, imaging, far_edge = tile_call(
            moment, tile_far, current, previous, far_halo, speed_sq, forward, source,
            imaging, partial_next,
        )
        previous, current = (current, advanced)
    row_index = jnp.arange(lax.axis_size("shot") * block_rows, dtype=jnp.int32) - shift_rows
    inside = (row_index >= 0) & (row_index < cells_y)
    chosen = jnp.take(imaging, jnp.clip(row_index, 0, cells_y - 1), axis=0)
    placed = jnp.where(inside[:, None, None], chosen, 0.0)
    shots = lax.axis_size("shot")
    placed = placed.reshape((shots, block_rows) + placed.shape[1:])
    arrived = lax.all_to_all(placed, "shot", split_axis=0, concat_axis=0, tiled=True)
    gradient = jnp.sum(arrived, axis=0)
    return (gradient, current[None])


def solution(mesh):
    in_specs = (
        P("shot", "space", None),
        P("shot", "space", None),
        P("shot", "space"),
        P(),
        P("shot"),
        P("shot", None, "space", None),
        P("shot", None, "space", None),
        P("shot", None, "space", None),
        P("shot", None, None, "space", None),
    )
    out_specs = (P("shot", "space", None), P("shot", None, "space", None))
    return jax.shard_map(local, mesh=mesh, in_specs=in_specs, out_specs=out_specs, check_vma=False)
```

```python
import functools

import jax
import jax.numpy as jnp
from jax import lax
from jax.sharding import PartitionSpec as P
from jax.experimental import pallas as pl
from jax.experimental.pallas import tpu as pltpu

STENCIL = (-205.0 / 72.0, 8.0 / 5.0, -1.0 / 5.0, 8.0 / 315.0, -1.0 / 560.0)


def extended(shard, sides, width):
    for axis, dim in sides:
        devices, length = (lax.axis_size(axis), shard.shape[dim])
        up = [(i, (i + 1) % devices) for i in range(devices - 1)]
        down = [(j, i) for i, j in up]
        last = lax.slice_in_dim(shard, length - width, length, axis=dim)
        leading = lax.slice_in_dim(shard, 0, width, axis=dim)
        before = lax.ppermute(last, axis, up)
        after = lax.ppermute(leading, axis, down)
        shard = jnp.concatenate([before, shard, after], axis=dim)
    return shard


def laplace(padded):
    span_y = padded.shape[0] - 8
    span_x = padded.shape[1] - 8
    span_z = padded.shape[2] - 8

    def window(shift_y, shift_x, shift_z):
        return padded[
            4 + shift_y : 4 + shift_y + span_y,
            4 + shift_x : 4 + shift_x + span_x,
            4 + shift_z : 4 + shift_z + span_z,
        ]

    summed = 3.0 * STENCIL[0] * window(0, 0, 0)
    for reach in range(1, 5):
        beside_all = (
            window(reach, 0, 0)
            + window(-reach, 0, 0)
            + window(0, reach, 0)
            + window(0, -reach, 0)
            + window(0, 0, reach)
            + window(0, 0, -reach)
        )
        summed = summed + STENCIL[reach] * beside_all
    return summed


def pad_sides(field):
    return jnp.pad(field, ((4, 4), (0, 0), (4, 4)))


ROWS = 1
BLOCK = 8
SLAB_ROWS = 4
SLAB_UNROLL = 2


def step_kernel(moment, cur_ref, prev_ref, lo_ref, hi_ref, vel_ref, fwd_ref, src_ref, img_ref,
                next_ref, img_out_ref, first_ref, last_ref, pad_ref):
    cells_y, cells_x, cells_z = cur_ref.shape
    width = lo_ref.shape[1]
    block = pl.program_id(0)

    @pl.when(block == 0)
    def _():
        zeros = jnp.zeros((4, pad_ref.shape[1], cells_z), jnp.float32)
        pad_ref[0:4] = zeros
        pad_ref[4 + cells_y : 8 + cells_y] = zeros
        pad_ref[4 : 4 + cells_y, 8 - width : 8] = lo_ref[...]
        pad_ref[4 : 4 + cells_y, 8 : 8 + cells_x] = cur_ref[...]
        pad_ref[4 : 4 + cells_y, 8 + cells_x : 8 + cells_x + width] = hi_ref[...]

    def body(chunk, carry):
        y0 = pl.multiple_of(chunk * ROWS, ROWS)
        base = block * BLOCK + y0 + 4

        def window(shift_y, shift_x):
            return pad_ref[pl.ds(base + shift_y, ROWS), 8 + shift_x : 8 + shift_x + cells_x, :]

        center = window(0, 0)
        depth = lax.broadcasted_iota(jnp.int32, center.shape, 2)
        half = cells_z // 2
        low, high = center[..., :half], center[..., half:]
        lane = lax.broadcasted_iota(jnp.int32, low.shape, 2)

        def along_z(reach):
            low_up = pltpu.roll(low, half - reach, 2)
            high_up = pltpu.roll(high, half - reach, 2)
            low_down = pltpu.roll(low, reach, 2)
            high_down = pltpu.roll(high, reach, 2)
            head = lane < half - reach
            tail = lane >= reach
            up = jnp.concatenate(
                [jnp.where(head, low_up, high_up), jnp.where(head, high_up, 0.0)], axis=2
            )
            down = jnp.concatenate(
                [jnp.where(tail, low_down, 0.0), jnp.where(tail, high_down, low_down)], axis=2
            )
            return up, down

        summed = 3.0 * STENCIL[0] * center
        for reach in range(1, 5):
            z_up, z_down = along_z(reach)
            beside_all = (
                window(reach, 0)
                + window(-reach, 0)
                + window(0, reach)
                + window(0, -reach)
                + z_up
                + z_down
            )
            summed = summed + STENCIL[reach] * beside_all
        rows = pl.ds(y0, ROWS)
        advanced = 2.0 * center - prev_ref[rows] + vel_ref[rows] * summed
        source_rows = pl.ds(block * BLOCK + y0, ROWS)
        source = jnp.broadcast_to(src_ref[source_rows, :, pl.ds(moment, 1)], advanced.shape)
        advanced = jnp.where(depth == 0, advanced + source, advanced)
        next_ref[rows] = advanced
        img_out_ref[rows] = img_ref[rows] + fwd_ref[rows].astype(jnp.float32) * advanced
        first_ref[rows] = advanced[:, :width]
        last_ref[rows] = advanced[:, cells_x - width :]
        return carry

    lax.fori_loop(0, BLOCK // ROWS, body, 0, unroll=4)


def step_call(moment, current, previous, lo, hi, speed_sq, forward, source, imaging):
    cells_y, cells_x, cells_z = current.shape
    width = lo.shape[1]
    whole = pl.BlockSpec((cells_y, cells_x, cells_z), lambda i: (0, 0, 0))
    whole_rim = pl.BlockSpec((cells_y, width, cells_z), lambda i: (0, 0, 0))
    field = pl.BlockSpec((BLOCK, cells_x, cells_z), lambda i: (i, 0, 0))
    rim = pl.BlockSpec((BLOCK, width, cells_z), lambda i: (i, 0, 0))
    fwd_spec = pl.BlockSpec((None, BLOCK, cells_x, cells_z), lambda i: (moment, i, 0, 0))
    src_spec = pl.BlockSpec(source.shape, lambda i: (0, 0, 0))
    f32 = jnp.float32
    return pl.pallas_call(
        functools.partial(step_kernel, moment),
        grid=(cells_y // BLOCK,),
        out_shape=(
            jax.ShapeDtypeStruct(current.shape, f32),
            jax.ShapeDtypeStruct(current.shape, f32),
            jax.ShapeDtypeStruct(lo.shape, f32),
            jax.ShapeDtypeStruct(lo.shape, f32),
        ),
        in_specs=[whole, field, whole_rim, whole_rim, field, fwd_spec, src_spec, field],
        out_specs=(field, field, rim, rim),
        scratch_shapes=[pltpu.VMEM((cells_y + 8, cells_x + 16, cells_z), f32)],
        input_output_aliases={7: 1},
        compiler_params=pltpu.CompilerParams(
            dimension_semantics=("arbitrary",), vmem_limit_bytes=48 * 1024 * 1024
        ),
    )(current, previous, lo, hi, speed_sq, forward, source, imaging)


def tile_kernel(moment, chained, tile_ref, cur_ref, prev_ref, halo_ref, vel_ref, fwd_ref, src_ref,
                img_ref, *rest):
    if chained:
        rest = rest[1:]
    next_ref, img_out_ref, edge_ref, pad_ref = rest
    cells_y, cells_x, cells_z = cur_ref.shape
    width = halo_ref.shape[1]
    part = cells_x // 2
    zeros = jnp.zeros((4, pad_ref.shape[1], cells_z), jnp.float32)
    pad_ref[0:4] = zeros
    pad_ref[4 + cells_y : 8 + cells_y] = zeros
    pad_ref[4 : 4 + cells_y, 8 : 8 + cells_x] = cur_ref[...]

    def compute(tile):
        if tile == 0:
            pad_ref[4 : 4 + cells_y, 8 - width : 8] = halo_ref[...]
        else:
            pad_ref[4 : 4 + cells_y, 8 + cells_x : 8 + cells_x + width] = halo_ref[...]
        start = 8 + tile * part

        def body(chunk, carry):
            y0 = chunk * SLAB_ROWS
            base = y0 + 4
            slab = pad_ref[pl.ds(base - 4, SLAB_ROWS + 8), start : start + part, :]

            def window(shift_y, shift_x):
                if shift_x == 0:
                    return slab[4 + shift_y : 4 + shift_y + SLAB_ROWS]
                return pad_ref[
                    pl.ds(base + shift_y, SLAB_ROWS), start + shift_x : start + shift_x + part, :
                ]

            center = window(0, 0)
            depth = lax.broadcasted_iota(jnp.int32, center.shape, 2)

            def along_z(reach):
                up = pltpu.roll(center, cells_z - reach, 2)
                down = pltpu.roll(center, reach, 2)
                return (
                    jnp.where(depth + reach < cells_z, up, 0.0),
                    jnp.where(depth - reach >= 0, down, 0.0),
                )

            summed = 3.0 * STENCIL[0] * center
            for reach in range(1, 5):
                z_up, z_down = along_z(reach)
                beside_all = (
                    window(reach, 0)
                    + window(-reach, 0)
                    + window(0, reach)
                    + window(0, -reach)
                    + z_up
                    + z_down
                )
                summed = summed + STENCIL[reach] * beside_all
            rows = pl.ds(y0, SLAB_ROWS)
            advanced = 2.0 * center - prev_ref[rows] + vel_ref[rows] * summed
            source = src_ref[rows, tile * part : (tile + 1) * part, pl.ds(moment, 1)]
            source = jnp.broadcast_to(source, advanced.shape)
            advanced = jnp.where(depth == 0, advanced + source, advanced)
            next_ref[rows] = advanced
            accel = fwd_ref[rows].astype(jnp.float32)[:, tile * part : (tile + 1) * part]
            img_out_ref[rows] = img_ref[rows] + accel * advanced
            if tile == 0:
                edge_ref[rows] = advanced[:, :width]
            else:
                edge_ref[rows] = advanced[:, part - width :]
            return carry

        lax.fori_loop(0, cells_y // SLAB_ROWS, body, 0, unroll=SLAB_UNROLL)

    for tile in range(2):
        pl.when(tile_ref[0] == tile)(functools.partial(compute, tile))


def tile_call(moment, tile, current, previous, halo_rim, speed_sq, forward, source, imaging, chain):
    cells_y, cells_x, cells_z = current.shape
    width = halo_rim.shape[1]
    part = cells_x // 2
    whole = pl.BlockSpec((cells_y, cells_x, cells_z), lambda i, t: (0, 0, 0))
    rim = pl.BlockSpec((cells_y, width, cells_z), lambda i, t: (0, 0, 0))
    half = pl.BlockSpec((cells_y, part, cells_z), lambda i, t: (0, t[0], 0))
    fwd_spec = pl.BlockSpec((None, cells_y, cells_x, cells_z), lambda i, t: (moment, 0, 0, 0))
    src_spec = pl.BlockSpec(source.shape, lambda i, t: (0, 0, 0))
    f32 = jnp.float32
    cells = cells_y * part * cells_z
    chained = chain is not None
    in_specs = [whole, half, rim, half, fwd_spec, src_spec, half]
    operands = [tile, current, previous, halo_rim, speed_sq, forward, source, imaging]
    aliases = {7: 1}
    if chained:
        in_specs.append(pl.BlockSpec(memory_space=pl.ANY))
        operands.append(chain)
        aliases[8] = 0
    return pl.pallas_call(
        functools.partial(tile_kernel, moment, chained),
        grid_spec=pltpu.PrefetchScalarGridSpec(
            num_scalar_prefetch=1,
            grid=(1,),
            in_specs=in_specs,
            out_specs=(half, half, rim),
            scratch_shapes=[pltpu.VMEM((cells_y + 8, cells_x + 16, cells_z), f32)],
        ),
        out_shape=(
            jax.ShapeDtypeStruct(current.shape, f32),
            jax.ShapeDtypeStruct(current.shape, f32),
            jax.ShapeDtypeStruct(halo_rim.shape, f32),
        ),
        input_output_aliases=aliases,
        cost_estimate=pl.CostEstimate(
            flops=60 * cells, bytes_accessed=28 * cells, transcendentals=0
        ),
        compiler_params=pltpu.CompilerParams(vmem_limit_bytes=48 * 1024 * 1024),
    )(*operands)


def split_dot(select, table):
    high = table.astype(jnp.bfloat16)
    rest = table - high.astype(jnp.float32)
    middle = rest.astype(jnp.bfloat16)
    low = (rest - middle.astype(jnp.float32)).astype(jnp.bfloat16)
    total = jnp.dot(select, high, preferred_element_type=jnp.float32)
    total = total + jnp.dot(select, middle, preferred_element_type=jnp.float32)
    return total + jnp.dot(select, low, preferred_element_type=jnp.float32)


def route_kernel(slot_count, traces_ref, filter_ref, tile_col_ref, tile_row_ref, cell_ref, out_ref):
    records = traces_ref.shape[0]
    columns = filter_ref.shape[0]
    values = lax.dot_general(
        traces_ref[...], filter_ref[...], (((1,), (1,)), ((), ())),
        preferred_element_type=jnp.float32,
    )
    lane = lax.broadcasted_iota(jnp.int32, (records, columns), 1)
    cell = jnp.broadcast_to((cell_ref[...] + 1).astype(jnp.float32), (records, columns))
    payload = jnp.where(lane == columns - 2, cell, values)
    earlier = lax.broadcasted_iota(jnp.int32, (records, records), 0)
    later = lax.broadcasted_iota(jnp.int32, (records, records), 1)
    same = (tile_col_ref[...] == tile_row_ref[...]) & (earlier < later)
    rank = jnp.sum(same.astype(jnp.int32), axis=0, keepdims=True)
    slot = tile_row_ref[...] * slot_count + rank
    slots = out_ref.shape[0]
    placing = (lax.broadcasted_iota(jnp.int32, (slots, records), 0) == slot).astype(jnp.bfloat16)
    out_ref[...] = split_dot(placing, payload)


def gather_kernel(cells_ref, arrived_ref, out_ref):
    surface = out_ref.shape[0]
    slots = arrived_ref.shape[0]
    cell_index = lax.broadcasted_iota(jnp.int32, (surface, slots), 0) + 1
    gathering = (cell_index == cells_ref[...]).astype(jnp.bfloat16)
    out_ref[...] = split_dot(gathering, arrived_ref[...])


def halo(first, last):
    axis = "space"
    devices = lax.axis_size(axis)
    even = lax.axis_index(axis) % 2 == 0
    within = [(i, i ^ 1) for i in range(devices)]
    across = [(i, i + 1 - 2 * ((i + 1) % 2)) for i in range(1, devices - 1)]
    got_within = lax.ppermute(jnp.where(even, last, first), axis, within)
    got_across = lax.ppermute(jnp.where(even, first, last), axis, across)
    lo = jnp.where(even, got_across, got_within)
    hi = jnp.where(even, got_within, got_across)
    return lo, hi


def local(
    residual,
    record_tile,
    record_cell,
    time_filter,
    offsets,
    velocity,
    adjoint_prev,
    adjoint_now,
    forward_accel,
):
    tiles_count = lax.axis_size("space")
    record_count = residual.shape[1]
    cells_y = velocity.shape[1]
    cells_x = velocity.shape[2]
    step_count = forward_accel.shape[1]
    slot_count = record_count * 3 // 16
    surface = cells_y * cells_x
    block_rows = (cells_y + cells_y // 4) // lax.axis_size("shot")
    trace_rows = residual[0]
    tile_ids = record_tile[0, :, 0]
    cell_ids = record_cell[0]
    slots = tiles_count * slot_count
    columns = step_count + 2
    filter_rows = jnp.concatenate(
        [time_filter, jnp.zeros((columns - step_count,) + time_filter.shape[1:], time_filter.dtype)]
    )
    vmem = pl.BlockSpec(memory_space=pltpu.VMEM)
    buffer = pl.pallas_call(
        functools.partial(route_kernel, slot_count),
        out_shape=jax.ShapeDtypeStruct((slots, columns), jnp.float32),
        in_specs=[vmem] * 5,
        out_specs=vmem,
    )(
        trace_rows,
        filter_rows,
        tile_ids.reshape(record_count, 1),
        tile_ids.reshape(1, record_count),
        cell_ids.reshape(record_count, 1),
    )
    buffer = buffer.reshape(tiles_count, slot_count, columns)
    arrived = lax.all_to_all(buffer, "space", split_axis=0, concat_axis=0, tiled=True)
    arrived = arrived.reshape(slots, columns)
    cells_row = arrived[:, step_count].astype(jnp.int32).reshape(1, slots)
    source = pl.pallas_call(
        gather_kernel,
        out_shape=jax.ShapeDtypeStruct((surface, columns), jnp.float32),
        in_specs=[vmem] * 2,
        out_specs=vmem,
    )(cells_row, arrived)
    source = source.reshape(cells_y, cells_x, columns)
    shift_rows = offsets[0]
    speed_sq = velocity[0]
    previous = adjoint_prev[0]
    current = adjoint_now[0]
    forward = forward_accel[0]
    imaging = jnp.zeros_like(current)
    width = 4
    odd = lax.axis_index("space") % 2
    tile_near = (1 - odd).reshape(1).astype(jnp.int32)
    tile_far = odd.reshape(1).astype(jnp.int32)
    devices = lax.axis_size("space")
    within = [(i, i ^ 1) for i in range(devices)]
    across = [(i, i + 1 - 2 * ((i + 1) % 2)) for i in range(1, devices - 1)]
    first = current[:, :width]
    last = current[:, cells_x - width :]
    even = odd == 0
    near_edge = jnp.where(even, last, first)
    far_edge = jnp.where(even, first, last)
    for moment in range(step_count):
        near_halo = lax.ppermute(near_edge, "space", within)
        far_halo = lax.ppermute(far_edge, "space", across)
        partial_next, imaging, near_edge = tile_call(
            moment, tile_near, current, previous, near_halo, speed_sq, forward, source,
            imaging, None,
        )
        advanced, imaging, far_edge = tile_call(
            moment, tile_far, current, previous, far_halo, speed_sq, forward, source,
            imaging, partial_next,
        )
        previous, current = (current, advanced)
    row_index = jnp.arange(lax.axis_size("shot") * block_rows, dtype=jnp.int32) - shift_rows
    inside = (row_index >= 0) & (row_index < cells_y)
    chosen = jnp.take(imaging, jnp.clip(row_index, 0, cells_y - 1), axis=0)
    placed = jnp.where(inside[:, None, None], chosen, 0.0)
    shots = lax.axis_size("shot")
    placed = placed.reshape((shots, block_rows) + placed.shape[1:])
    arrived = lax.all_to_all(placed, "shot", split_axis=0, concat_axis=0, tiled=True)
    gradient = jnp.sum(arrived, axis=0)
    return (gradient, current[None])


def solution(mesh):
    in_specs = (
        P("shot", "space", None),
        P("shot", "space", None),
        P("shot", "space"),
        P(),
        P("shot"),
        P("shot", None, "space", None),
        P("shot", None, "space", None),
        P("shot", None, "space", None),
        P("shot", None, None, "space", None),
    )
    out_specs = (P("shot", "space", None), P("shot", None, "space", None))
    return jax.shard_map(local, mesh=mesh, in_specs=in_specs, out_specs=out_specs, check_vma=False)
```

```python
import functools

import jax
import jax.numpy as jnp
from jax import lax
from jax.sharding import PartitionSpec as P
from jax.experimental import pallas as pl
from jax.experimental.pallas import tpu as pltpu

STENCIL = (-205.0 / 72.0, 8.0 / 5.0, -1.0 / 5.0, 8.0 / 315.0, -1.0 / 560.0)


def extended(shard, sides, width):
    for axis, dim in sides:
        devices, length = (lax.axis_size(axis), shard.shape[dim])
        up = [(i, (i + 1) % devices) for i in range(devices - 1)]
        down = [(j, i) for i, j in up]
        last = lax.slice_in_dim(shard, length - width, length, axis=dim)
        leading = lax.slice_in_dim(shard, 0, width, axis=dim)
        before = lax.ppermute(last, axis, up)
        after = lax.ppermute(leading, axis, down)
        shard = jnp.concatenate([before, shard, after], axis=dim)
    return shard


def laplace(padded):
    span_y = padded.shape[0] - 8
    span_x = padded.shape[1] - 8
    span_z = padded.shape[2] - 8

    def window(shift_y, shift_x, shift_z):
        return padded[
            4 + shift_y : 4 + shift_y + span_y,
            4 + shift_x : 4 + shift_x + span_x,
            4 + shift_z : 4 + shift_z + span_z,
        ]

    summed = 3.0 * STENCIL[0] * window(0, 0, 0)
    for reach in range(1, 5):
        beside_all = (
            window(reach, 0, 0)
            + window(-reach, 0, 0)
            + window(0, reach, 0)
            + window(0, -reach, 0)
            + window(0, 0, reach)
            + window(0, 0, -reach)
        )
        summed = summed + STENCIL[reach] * beside_all
    return summed


def pad_sides(field):
    return jnp.pad(field, ((4, 4), (0, 0), (4, 4)))


ROWS = 1
BLOCK = 8
SLAB_ROWS = 4
SLAB_UNROLL = 2


def step_kernel(moment, cur_ref, prev_ref, lo_ref, hi_ref, vel_ref, fwd_ref, src_ref, img_ref,
                next_ref, img_out_ref, first_ref, last_ref, pad_ref):
    cells_y, cells_x, cells_z = cur_ref.shape
    width = lo_ref.shape[1]
    block = pl.program_id(0)

    @pl.when(block == 0)
    def _():
        zeros = jnp.zeros((4, pad_ref.shape[1], cells_z), jnp.float32)
        pad_ref[0:4] = zeros
        pad_ref[4 + cells_y : 8 + cells_y] = zeros
        pad_ref[4 : 4 + cells_y, 8 - width : 8] = lo_ref[...]
        pad_ref[4 : 4 + cells_y, 8 : 8 + cells_x] = cur_ref[...]
        pad_ref[4 : 4 + cells_y, 8 + cells_x : 8 + cells_x + width] = hi_ref[...]

    def body(chunk, carry):
        y0 = pl.multiple_of(chunk * ROWS, ROWS)
        base = block * BLOCK + y0 + 4

        def window(shift_y, shift_x):
            return pad_ref[pl.ds(base + shift_y, ROWS), 8 + shift_x : 8 + shift_x + cells_x, :]

        center = window(0, 0)
        depth = lax.broadcasted_iota(jnp.int32, center.shape, 2)
        half = cells_z // 2
        low, high = center[..., :half], center[..., half:]
        lane = lax.broadcasted_iota(jnp.int32, low.shape, 2)

        def along_z(reach):
            low_up = pltpu.roll(low, half - reach, 2)
            high_up = pltpu.roll(high, half - reach, 2)
            low_down = pltpu.roll(low, reach, 2)
            high_down = pltpu.roll(high, reach, 2)
            head = lane < half - reach
            tail = lane >= reach
            up = jnp.concatenate(
                [jnp.where(head, low_up, high_up), jnp.where(head, high_up, 0.0)], axis=2
            )
            down = jnp.concatenate(
                [jnp.where(tail, low_down, 0.0), jnp.where(tail, high_down, low_down)], axis=2
            )
            return up, down

        summed = 3.0 * STENCIL[0] * center
        for reach in range(1, 5):
            z_up, z_down = along_z(reach)
            beside_all = (
                window(reach, 0)
                + window(-reach, 0)
                + window(0, reach)
                + window(0, -reach)
                + z_up
                + z_down
            )
            summed = summed + STENCIL[reach] * beside_all
        rows = pl.ds(y0, ROWS)
        advanced = 2.0 * center - prev_ref[rows] + vel_ref[rows] * summed
        source_rows = pl.ds(block * BLOCK + y0, ROWS)
        source = jnp.broadcast_to(src_ref[source_rows, :, pl.ds(moment, 1)], advanced.shape)
        advanced = jnp.where(depth == 0, advanced + source, advanced)
        next_ref[rows] = advanced
        img_out_ref[rows] = img_ref[rows] + fwd_ref[rows].astype(jnp.float32) * advanced
        first_ref[rows] = advanced[:, :width]
        last_ref[rows] = advanced[:, cells_x - width :]
        return carry

    lax.fori_loop(0, BLOCK // ROWS, body, 0, unroll=4)


def step_call(moment, current, previous, lo, hi, speed_sq, forward, source, imaging):
    cells_y, cells_x, cells_z = current.shape
    width = lo.shape[1]
    whole = pl.BlockSpec((cells_y, cells_x, cells_z), lambda i: (0, 0, 0))
    whole_rim = pl.BlockSpec((cells_y, width, cells_z), lambda i: (0, 0, 0))
    field = pl.BlockSpec((BLOCK, cells_x, cells_z), lambda i: (i, 0, 0))
    rim = pl.BlockSpec((BLOCK, width, cells_z), lambda i: (i, 0, 0))
    fwd_spec = pl.BlockSpec((None, BLOCK, cells_x, cells_z), lambda i: (moment, i, 0, 0))
    src_spec = pl.BlockSpec(source.shape, lambda i: (0, 0, 0))
    f32 = jnp.float32
    return pl.pallas_call(
        functools.partial(step_kernel, moment),
        grid=(cells_y // BLOCK,),
        out_shape=(
            jax.ShapeDtypeStruct(current.shape, f32),
            jax.ShapeDtypeStruct(current.shape, f32),
            jax.ShapeDtypeStruct(lo.shape, f32),
            jax.ShapeDtypeStruct(lo.shape, f32),
        ),
        in_specs=[whole, field, whole_rim, whole_rim, field, fwd_spec, src_spec, field],
        out_specs=(field, field, rim, rim),
        scratch_shapes=[pltpu.VMEM((cells_y + 8, cells_x + 16, cells_z), f32)],
        input_output_aliases={7: 1},
        compiler_params=pltpu.CompilerParams(
            dimension_semantics=("arbitrary",), vmem_limit_bytes=48 * 1024 * 1024
        ),
    )(current, previous, lo, hi, speed_sq, forward, source, imaging)


def tile_kernel(moment, chained, tile_ref, cur_ref, prev_ref, halo_ref, vel_ref, fwd_ref, src_ref,
                img_ref, *rest):
    if chained:
        rest = rest[1:]
    next_ref, img_out_ref, edge_ref, pad_ref = rest
    cells_y, cells_x, cells_z = cur_ref.shape
    width = halo_ref.shape[1]
    part = cells_x // 2
    zeros = jnp.zeros((4, pad_ref.shape[1], cells_z), jnp.float32)
    pad_ref[0:4] = zeros
    pad_ref[4 + cells_y : 8 + cells_y] = zeros
    pad_ref[4 : 4 + cells_y, 8 : 8 + cells_x] = cur_ref[...]

    def compute(tile):
        if tile == 0:
            pad_ref[4 : 4 + cells_y, 8 - width : 8] = halo_ref[...]
        else:
            pad_ref[4 : 4 + cells_y, 8 + cells_x : 8 + cells_x + width] = halo_ref[...]
        start = 8 + tile * part

        def body(chunk, carry):
            y0 = chunk * SLAB_ROWS
            base = y0 + 4
            slab = pad_ref[pl.ds(base - 4, SLAB_ROWS + 8), start : start + part, :]

            def window(shift_y, shift_x):
                if shift_x == 0:
                    return slab[4 + shift_y : 4 + shift_y + SLAB_ROWS]
                return pad_ref[
                    pl.ds(base + shift_y, SLAB_ROWS), start + shift_x : start + shift_x + part, :
                ]

            center = window(0, 0)
            depth = lax.broadcasted_iota(jnp.int32, center.shape, 2)

            def along_z(reach):
                up = pltpu.roll(center, cells_z - reach, 2)
                down = pltpu.roll(center, reach, 2)
                return (
                    jnp.where(depth + reach < cells_z, up, 0.0),
                    jnp.where(depth - reach >= 0, down, 0.0),
                )

            summed = 3.0 * STENCIL[0] * center
            for reach in range(1, 5):
                z_up, z_down = along_z(reach)
                beside_all = (
                    window(reach, 0)
                    + window(-reach, 0)
                    + window(0, reach)
                    + window(0, -reach)
                    + z_up
                    + z_down
                )
                summed = summed + STENCIL[reach] * beside_all
            rows = pl.ds(y0, SLAB_ROWS)
            advanced = 2.0 * center - prev_ref[rows] + vel_ref[rows] * summed
            source = src_ref[rows, tile * part : (tile + 1) * part, pl.ds(moment, 1)]
            source = jnp.broadcast_to(source, advanced.shape)
            advanced = jnp.where(depth == 0, advanced + source, advanced)
            next_ref[rows] = advanced
            accel = fwd_ref[rows].astype(jnp.float32)[:, tile * part : (tile + 1) * part]
            img_out_ref[rows] = img_ref[rows] + accel * advanced
            if tile == 0:
                edge_ref[rows] = advanced[:, :width]
            else:
                edge_ref[rows] = advanced[:, part - width :]
            return carry

        lax.fori_loop(0, cells_y // SLAB_ROWS, body, 0, unroll=SLAB_UNROLL)

    for tile in range(2):
        pl.when(tile_ref[0] == tile)(functools.partial(compute, tile))


def tile_call(moment, tile, current, previous, halo_rim, speed_sq, forward, source, imaging, chain):
    cells_y, cells_x, cells_z = current.shape
    width = halo_rim.shape[1]
    part = cells_x // 2
    whole = pl.BlockSpec((cells_y, cells_x, cells_z), lambda i, t: (0, 0, 0))
    rim = pl.BlockSpec((cells_y, width, cells_z), lambda i, t: (0, 0, 0))
    half = pl.BlockSpec((cells_y, part, cells_z), lambda i, t: (0, t[0], 0))
    fwd_spec = pl.BlockSpec((None, cells_y, cells_x, cells_z), lambda i, t: (moment, 0, 0, 0))
    src_spec = pl.BlockSpec(source.shape, lambda i, t: (0, 0, 0))
    f32 = jnp.float32
    cells = cells_y * part * cells_z
    chained = chain is not None
    in_specs = [whole, half, rim, half, fwd_spec, src_spec, half]
    operands = [tile, current, previous, halo_rim, speed_sq, forward, source, imaging]
    aliases = {7: 1}
    if chained:
        in_specs.append(pl.BlockSpec(memory_space=pl.ANY))
        operands.append(chain)
        aliases[8] = 0
    return pl.pallas_call(
        functools.partial(tile_kernel, moment, chained),
        grid_spec=pltpu.PrefetchScalarGridSpec(
            num_scalar_prefetch=1,
            grid=(1,),
            in_specs=in_specs,
            out_specs=(half, half, rim),
            scratch_shapes=[pltpu.VMEM((cells_y + 8, cells_x + 16, cells_z), f32)],
        ),
        out_shape=(
            jax.ShapeDtypeStruct(current.shape, f32),
            jax.ShapeDtypeStruct(current.shape, f32),
            jax.ShapeDtypeStruct(halo_rim.shape, f32),
        ),
        input_output_aliases=aliases,
        cost_estimate=pl.CostEstimate(
            flops=60 * cells, bytes_accessed=28 * cells, transcendentals=0
        ),
        compiler_params=pltpu.CompilerParams(vmem_limit_bytes=48 * 1024 * 1024),
    )(*operands)


def halo(first, last):
    axis = "space"
    devices = lax.axis_size(axis)
    even = lax.axis_index(axis) % 2 == 0
    within = [(i, i ^ 1) for i in range(devices)]
    across = [(i, i + 1 - 2 * ((i + 1) % 2)) for i in range(1, devices - 1)]
    got_within = lax.ppermute(jnp.where(even, last, first), axis, within)
    got_across = lax.ppermute(jnp.where(even, first, last), axis, across)
    lo = jnp.where(even, got_across, got_within)
    hi = jnp.where(even, got_within, got_across)
    return lo, hi


def local(
    residual,
    record_tile,
    record_cell,
    time_filter,
    offsets,
    velocity,
    adjoint_prev,
    adjoint_now,
    forward_accel,
):
    tiles_count = lax.axis_size("space")
    record_count = residual.shape[1]
    cells_y = velocity.shape[1]
    cells_x = velocity.shape[2]
    cells_z = velocity.shape[3]
    step_count = forward_accel.shape[1]
    slot_count = record_count * 3 // 16
    surface = cells_y * cells_x
    block_rows = (cells_y + cells_y // 4) // lax.axis_size("shot")
    trace_rows = residual[0]
    tile_ids = record_tile[0, :, 0]
    cell_ids = record_cell[0]
    record_order = jnp.arange(record_count, dtype=jnp.int32)
    same_before = (tile_ids[:, None] == tile_ids[None, :]) & (
        record_order[:, None] < record_order[None, :]
    )
    order_rank = jnp.sum(same_before.astype(jnp.int32), axis=0)
    slot_index = tile_ids * slot_count + order_rank
    filtered = jnp.dot(trace_rows, time_filter.T, preferred_element_type=jnp.float32)
    payload = jnp.concatenate(
        [filtered, (cell_ids + 1).astype(jnp.float32)[:, None]], axis=1
    )
    slots = tiles_count * slot_count
    placing = (
        slot_index[None, :] == jnp.arange(slots, dtype=jnp.int32)[:, None]
    ).astype(jnp.float32)
    buffer = jnp.dot(placing, payload, precision=lax.Precision.HIGHEST)
    buffer = buffer.reshape(tiles_count, slot_count, step_count + 1)
    arrived = lax.all_to_all(buffer, "space", split_axis=0, concat_axis=0, tiled=True)
    arrived = arrived.reshape(slots, step_count + 1)
    cell_of = arrived[:, step_count].astype(jnp.int32)
    gathering = (
        cell_of[:, None] == jnp.arange(1, surface + 1, dtype=jnp.int32)[None, :]
    ).astype(jnp.float32)
    source = lax.dot_general(
        gathering,
        arrived[:, :step_count],
        (((0,), (0,)), ((), ())),
        precision=lax.Precision.HIGHEST,
    )
    source = source.reshape(cells_y, cells_x, step_count)
    shift_rows = offsets[0]
    speed_sq = velocity[0]
    previous = adjoint_prev[0]
    current = adjoint_now[0]
    forward = forward_accel[0]
    imaging = jnp.zeros_like(current)
    width = 4
    odd = lax.axis_index("space") % 2
    tile_near = (1 - odd).reshape(1).astype(jnp.int32)
    tile_far = odd.reshape(1).astype(jnp.int32)
    devices = lax.axis_size("space")
    within = [(i, i ^ 1) for i in range(devices)]
    across = [(i, i + 1 - 2 * ((i + 1) % 2)) for i in range(1, devices - 1)]
    zero = jnp.zeros((), jnp.int32)
    near_start = (1 - odd) * (cells_x - width)
    near_edge = lax.dynamic_slice(current, (zero, near_start, zero), (cells_y, width, cells_z))
    far_start = odd * (cells_x - width)
    far_edge = lax.dynamic_slice(current, (zero, far_start, zero), (cells_y, width, cells_z))
    for moment in range(step_count):
        near_halo = lax.ppermute(near_edge, "space", within)
        far_halo = lax.ppermute(far_edge, "space", across)
        partial_next, imaging, near_edge = tile_call(
            moment, tile_near, current, previous, near_halo, speed_sq, forward, source,
            imaging, None,
        )
        advanced, imaging, far_edge = tile_call(
            moment, tile_far, current, previous, far_halo, speed_sq, forward, source,
            imaging, partial_next,
        )
        previous, current = (current, advanced)
    row_index = jnp.arange(lax.axis_size("shot") * block_rows, dtype=jnp.int32) - shift_rows
    inside = (row_index >= 0) & (row_index < cells_y)
    chosen = jnp.take(imaging, jnp.clip(row_index, 0, cells_y - 1), axis=0)
    placed = jnp.where(inside[:, None, None], chosen, 0.0)
    shots = lax.axis_size("shot")
    placed = placed.reshape((shots, block_rows) + placed.shape[1:])
    arrived = lax.all_to_all(placed, "shot", split_axis=0, concat_axis=0, tiled=True)
    gradient = jnp.sum(arrived, axis=0)
    return (gradient, current[None])


def solution(mesh):
    in_specs = (
        P("shot", "space", None),
        P("shot", "space", None),
        P("shot", "space"),
        P(),
        P("shot"),
        P("shot", None, "space", None),
        P("shot", None, "space", None),
        P("shot", None, "space", None),
        P("shot", None, None, "space", None),
    )
    out_specs = (P("shot", "space", None), P("shot", None, "space", None))
    return jax.shard_map(local, mesh=mesh, in_specs=in_specs, out_specs=out_specs, check_vma=False)
```

```python
import functools

import jax
import jax.numpy as jnp
from jax import lax
from jax.sharding import PartitionSpec as P
from jax.experimental import pallas as pl
from jax.experimental.pallas import tpu as pltpu

STENCIL = (-205.0 / 72.0, 8.0 / 5.0, -1.0 / 5.0, 8.0 / 315.0, -1.0 / 560.0)


def extended(shard, sides, width):
    for axis, dim in sides:
        devices, length = (lax.axis_size(axis), shard.shape[dim])
        up = [(i, (i + 1) % devices) for i in range(devices - 1)]
        down = [(j, i) for i, j in up]
        last = lax.slice_in_dim(shard, length - width, length, axis=dim)
        leading = lax.slice_in_dim(shard, 0, width, axis=dim)
        before = lax.ppermute(last, axis, up)
        after = lax.ppermute(leading, axis, down)
        shard = jnp.concatenate([before, shard, after], axis=dim)
    return shard


def laplace(padded):
    span_y = padded.shape[0] - 8
    span_x = padded.shape[1] - 8
    span_z = padded.shape[2] - 8

    def window(shift_y, shift_x, shift_z):
        return padded[
            4 + shift_y : 4 + shift_y + span_y,
            4 + shift_x : 4 + shift_x + span_x,
            4 + shift_z : 4 + shift_z + span_z,
        ]

    summed = 3.0 * STENCIL[0] * window(0, 0, 0)
    for reach in range(1, 5):
        beside_all = (
            window(reach, 0, 0)
            + window(-reach, 0, 0)
            + window(0, reach, 0)
            + window(0, -reach, 0)
            + window(0, 0, reach)
            + window(0, 0, -reach)
        )
        summed = summed + STENCIL[reach] * beside_all
    return summed


def pad_sides(field):
    return jnp.pad(field, ((4, 4), (0, 0), (4, 4)))


ROWS = 1
BLOCK = 8
SLAB_ROWS = 4
SLAB_UNROLL = 2


def step_kernel(moment, cur_ref, prev_ref, lo_ref, hi_ref, vel_ref, fwd_ref, src_ref, img_ref,
                next_ref, img_out_ref, first_ref, last_ref, pad_ref):
    cells_y, cells_x, cells_z = cur_ref.shape
    width = lo_ref.shape[1]
    block = pl.program_id(0)

    @pl.when(block == 0)
    def _():
        zeros = jnp.zeros((4, pad_ref.shape[1], cells_z), jnp.float32)
        pad_ref[0:4] = zeros
        pad_ref[4 + cells_y : 8 + cells_y] = zeros
        pad_ref[4 : 4 + cells_y, 8 - width : 8] = lo_ref[...]
        pad_ref[4 : 4 + cells_y, 8 : 8 + cells_x] = cur_ref[...]
        pad_ref[4 : 4 + cells_y, 8 + cells_x : 8 + cells_x + width] = hi_ref[...]

    def body(chunk, carry):
        y0 = pl.multiple_of(chunk * ROWS, ROWS)
        base = block * BLOCK + y0 + 4

        def window(shift_y, shift_x):
            return pad_ref[pl.ds(base + shift_y, ROWS), 8 + shift_x : 8 + shift_x + cells_x, :]

        center = window(0, 0)
        depth = lax.broadcasted_iota(jnp.int32, center.shape, 2)
        half = cells_z // 2
        low, high = center[..., :half], center[..., half:]
        lane = lax.broadcasted_iota(jnp.int32, low.shape, 2)

        def along_z(reach):
            low_up = pltpu.roll(low, half - reach, 2)
            high_up = pltpu.roll(high, half - reach, 2)
            low_down = pltpu.roll(low, reach, 2)
            high_down = pltpu.roll(high, reach, 2)
            head = lane < half - reach
            tail = lane >= reach
            up = jnp.concatenate(
                [jnp.where(head, low_up, high_up), jnp.where(head, high_up, 0.0)], axis=2
            )
            down = jnp.concatenate(
                [jnp.where(tail, low_down, 0.0), jnp.where(tail, high_down, low_down)], axis=2
            )
            return up, down

        summed = 3.0 * STENCIL[0] * center
        for reach in range(1, 5):
            z_up, z_down = along_z(reach)
            beside_all = (
                window(reach, 0)
                + window(-reach, 0)
                + window(0, reach)
                + window(0, -reach)
                + z_up
                + z_down
            )
            summed = summed + STENCIL[reach] * beside_all
        rows = pl.ds(y0, ROWS)
        advanced = 2.0 * center - prev_ref[rows] + vel_ref[rows] * summed
        source_rows = pl.ds(block * BLOCK + y0, ROWS)
        source = jnp.broadcast_to(src_ref[source_rows, :, pl.ds(moment, 1)], advanced.shape)
        advanced = jnp.where(depth == 0, advanced + source, advanced)
        next_ref[rows] = advanced
        img_out_ref[rows] = img_ref[rows] + fwd_ref[rows].astype(jnp.float32) * advanced
        first_ref[rows] = advanced[:, :width]
        last_ref[rows] = advanced[:, cells_x - width :]
        return carry

    lax.fori_loop(0, BLOCK // ROWS, body, 0, unroll=4)


def step_call(moment, current, previous, lo, hi, speed_sq, forward, source, imaging):
    cells_y, cells_x, cells_z = current.shape
    width = lo.shape[1]
    whole = pl.BlockSpec((cells_y, cells_x, cells_z), lambda i: (0, 0, 0))
    whole_rim = pl.BlockSpec((cells_y, width, cells_z), lambda i: (0, 0, 0))
    field = pl.BlockSpec((BLOCK, cells_x, cells_z), lambda i: (i, 0, 0))
    rim = pl.BlockSpec((BLOCK, width, cells_z), lambda i: (i, 0, 0))
    fwd_spec = pl.BlockSpec((None, BLOCK, cells_x, cells_z), lambda i: (moment, i, 0, 0))
    src_spec = pl.BlockSpec(source.shape, lambda i: (0, 0, 0))
    f32 = jnp.float32
    return pl.pallas_call(
        functools.partial(step_kernel, moment),
        grid=(cells_y // BLOCK,),
        out_shape=(
            jax.ShapeDtypeStruct(current.shape, f32),
            jax.ShapeDtypeStruct(current.shape, f32),
            jax.ShapeDtypeStruct(lo.shape, f32),
            jax.ShapeDtypeStruct(lo.shape, f32),
        ),
        in_specs=[whole, field, whole_rim, whole_rim, field, fwd_spec, src_spec, field],
        out_specs=(field, field, rim, rim),
        scratch_shapes=[pltpu.VMEM((cells_y + 8, cells_x + 16, cells_z), f32)],
        input_output_aliases={7: 1},
        compiler_params=pltpu.CompilerParams(
            dimension_semantics=("arbitrary",), vmem_limit_bytes=48 * 1024 * 1024
        ),
    )(current, previous, lo, hi, speed_sq, forward, source, imaging)


def tile_kernel(moment, chained, tile_ref, cur_ref, prev_ref, halo_ref, vel_ref, fwd_ref, src_ref,
                img_ref, *rest):
    if chained:
        rest = rest[1:]
    next_ref, img_out_ref, edge_ref, pad_ref = rest
    cells_y, cells_x, cells_z = cur_ref.shape
    width = halo_ref.shape[1]
    part = cells_x // 2
    zeros = jnp.zeros((4, pad_ref.shape[1], cells_z), jnp.float32)
    pad_ref[0:4] = zeros
    pad_ref[4 + cells_y : 8 + cells_y] = zeros
    pad_ref[4 : 4 + cells_y, 8 : 8 + cells_x] = cur_ref[...]

    def compute(tile):
        if tile == 0:
            pad_ref[4 : 4 + cells_y, 8 - width : 8] = halo_ref[...]
        else:
            pad_ref[4 : 4 + cells_y, 8 + cells_x : 8 + cells_x + width] = halo_ref[...]
        start = 8 + tile * part

        def body(chunk, carry):
            y0 = chunk * SLAB_ROWS
            base = y0 + 4
            slab = pad_ref[pl.ds(base - 4, SLAB_ROWS + 8), start : start + part, :]

            def window(shift_y, shift_x):
                if shift_x == 0:
                    return slab[4 + shift_y : 4 + shift_y + SLAB_ROWS]
                return pad_ref[
                    pl.ds(base + shift_y, SLAB_ROWS), start + shift_x : start + shift_x + part, :
                ]

            center = window(0, 0)
            depth = lax.broadcasted_iota(jnp.int32, center.shape, 2)

            def along_z(reach):
                up = pltpu.roll(center, cells_z - reach, 2)
                down = pltpu.roll(center, reach, 2)
                return (
                    jnp.where(depth + reach < cells_z, up, 0.0),
                    jnp.where(depth - reach >= 0, down, 0.0),
                )

            summed = 3.0 * STENCIL[0] * center
            for reach in range(1, 5):
                z_up, z_down = along_z(reach)
                beside_all = (
                    window(reach, 0)
                    + window(-reach, 0)
                    + window(0, reach)
                    + window(0, -reach)
                    + z_up
                    + z_down
                )
                summed = summed + STENCIL[reach] * beside_all
            rows = pl.ds(y0, SLAB_ROWS)
            advanced = 2.0 * center - prev_ref[rows] + vel_ref[rows] * summed
            source = src_ref[rows, tile * part : (tile + 1) * part, pl.ds(moment, 1)]
            source = jnp.broadcast_to(source, advanced.shape)
            advanced = jnp.where(depth == 0, advanced + source, advanced)
            next_ref[rows] = advanced
            accel = fwd_ref[rows].astype(jnp.float32)[:, tile * part : (tile + 1) * part]
            img_out_ref[rows] = img_ref[rows] + accel * advanced
            if tile == 0:
                edge_ref[rows] = advanced[:, :width]
            else:
                edge_ref[rows] = advanced[:, part - width :]
            return carry

        lax.fori_loop(0, cells_y // SLAB_ROWS, body, 0, unroll=SLAB_UNROLL)

    for tile in range(2):
        pl.when(tile_ref[0] == tile)(functools.partial(compute, tile))


def tile_call(moment, tile, current, previous, halo_rim, speed_sq, forward, source, imaging, chain):
    cells_y, cells_x, cells_z = current.shape
    width = halo_rim.shape[1]
    part = cells_x // 2
    whole = pl.BlockSpec((cells_y, cells_x, cells_z), lambda i, t: (0, 0, 0))
    rim = pl.BlockSpec((cells_y, width, cells_z), lambda i, t: (0, 0, 0))
    half = pl.BlockSpec((cells_y, part, cells_z), lambda i, t: (0, t[0], 0))
    fwd_spec = pl.BlockSpec((None, cells_y, cells_x, cells_z), lambda i, t: (moment, 0, 0, 0))
    src_spec = pl.BlockSpec(source.shape, lambda i, t: (0, 0, 0))
    f32 = jnp.float32
    cells = cells_y * part * cells_z
    chained = chain is not None
    in_specs = [whole, half, rim, half, fwd_spec, src_spec, half]
    operands = [tile, current, previous, halo_rim, speed_sq, forward, source, imaging]
    aliases = {7: 1}
    if chained:
        in_specs.append(pl.BlockSpec(memory_space=pl.ANY))
        operands.append(chain)
        aliases[8] = 0
    return pl.pallas_call(
        functools.partial(tile_kernel, moment, chained),
        grid_spec=pltpu.PrefetchScalarGridSpec(
            num_scalar_prefetch=1,
            grid=(1,),
            in_specs=in_specs,
            out_specs=(half, half, rim),
            scratch_shapes=[pltpu.VMEM((cells_y + 8, cells_x + 16, cells_z), f32)],
        ),
        out_shape=(
            jax.ShapeDtypeStruct(current.shape, f32),
            jax.ShapeDtypeStruct(current.shape, f32),
            jax.ShapeDtypeStruct(halo_rim.shape, f32),
        ),
        input_output_aliases=aliases,
        cost_estimate=pl.CostEstimate(
            flops=60 * cells, bytes_accessed=28 * cells, transcendentals=0
        ),
        compiler_params=pltpu.CompilerParams(vmem_limit_bytes=48 * 1024 * 1024),
    )(*operands)


def edge_kernel(odd_ref, cur_ref, near_ref, far_ref):
    width = near_ref.shape[1]
    cells_x = cur_ref.shape[1]

    @pl.when(odd_ref[0] == 0)
    def _():
        near_ref[...] = cur_ref[:, cells_x - width :, :]
        far_ref[...] = cur_ref[:, :width, :]

    @pl.when(odd_ref[0] == 1)
    def _():
        near_ref[...] = cur_ref[:, :width, :]
        far_ref[...] = cur_ref[:, cells_x - width :, :]


def edges_of(current, odd, width):
    cells_y, cells_x, cells_z = current.shape
    rim = jax.ShapeDtypeStruct((cells_y, width, cells_z), current.dtype)
    whole = pl.BlockSpec((cells_y, cells_x, cells_z), lambda i, t: (0, 0, 0))
    rim_spec = pl.BlockSpec((cells_y, width, cells_z), lambda i, t: (0, 0, 0))
    return pl.pallas_call(
        edge_kernel,
        grid_spec=pltpu.PrefetchScalarGridSpec(
            num_scalar_prefetch=1,
            grid=(1,),
            in_specs=[whole],
            out_specs=(rim_spec, rim_spec),
        ),
        out_shape=(rim, rim),
    )(odd, current)


def halo(first, last):
    axis = "space"
    devices = lax.axis_size(axis)
    even = lax.axis_index(axis) % 2 == 0
    within = [(i, i ^ 1) for i in range(devices)]
    across = [(i, i + 1 - 2 * ((i + 1) % 2)) for i in range(1, devices - 1)]
    got_within = lax.ppermute(jnp.where(even, last, first), axis, within)
    got_across = lax.ppermute(jnp.where(even, first, last), axis, across)
    lo = jnp.where(even, got_across, got_within)
    hi = jnp.where(even, got_within, got_across)
    return lo, hi


def local(
    residual,
    record_tile,
    record_cell,
    time_filter,
    offsets,
    velocity,
    adjoint_prev,
    adjoint_now,
    forward_accel,
):
    tiles_count = lax.axis_size("space")
    record_count = residual.shape[1]
    cells_y = velocity.shape[1]
    cells_x = velocity.shape[2]
    cells_z = velocity.shape[3]
    step_count = forward_accel.shape[1]
    slot_count = record_count * 3 // 16
    surface = cells_y * cells_x
    block_rows = (cells_y + cells_y // 4) // lax.axis_size("shot")
    trace_rows = residual[0]
    tile_ids = record_tile[0, :, 0]
    cell_ids = record_cell[0]
    record_order = jnp.arange(record_count, dtype=jnp.int32)
    same_before = (tile_ids[:, None] == tile_ids[None, :]) & (
        record_order[:, None] < record_order[None, :]
    )
    order_rank = jnp.sum(same_before.astype(jnp.int32), axis=0)
    slot_index = tile_ids * slot_count + order_rank
    filtered = jnp.dot(trace_rows, time_filter.T, preferred_element_type=jnp.float32)
    payload = jnp.concatenate(
        [filtered, (cell_ids + 1).astype(jnp.float32)[:, None]], axis=1
    )
    slots = tiles_count * slot_count
    placing = (
        slot_index[None, :] == jnp.arange(slots, dtype=jnp.int32)[:, None]
    ).astype(jnp.float32)
    buffer = jnp.dot(placing, payload, precision=lax.Precision.HIGHEST)
    buffer = buffer.reshape(tiles_count, slot_count, step_count + 1)
    arrived = lax.all_to_all(buffer, "space", split_axis=0, concat_axis=0, tiled=True)
    arrived = arrived.reshape(slots, step_count + 1)
    cell_of = arrived[:, step_count].astype(jnp.int32)
    gathering = (
        cell_of[:, None] == jnp.arange(1, surface + 1, dtype=jnp.int32)[None, :]
    ).astype(jnp.float32)
    source = lax.dot_general(
        gathering,
        arrived[:, :step_count],
        (((0,), (0,)), ((), ())),
        precision=lax.Precision.HIGHEST,
    )
    source = source.reshape(cells_y, cells_x, step_count)
    shift_rows = offsets[0]
    speed_sq = velocity[0]
    previous = adjoint_prev[0]
    current = adjoint_now[0]
    forward = forward_accel[0]
    imaging = jnp.zeros_like(current)
    width = 4
    odd = lax.axis_index("space") % 2
    tile_near = (1 - odd).reshape(1).astype(jnp.int32)
    tile_far = odd.reshape(1).astype(jnp.int32)
    devices = lax.axis_size("space")
    within = [(i, i ^ 1) for i in range(devices)]
    across = [(i, i + 1 - 2 * ((i + 1) % 2)) for i in range(1, devices - 1)]
    near_edge, far_edge = edges_of(current, tile_far, width)
    for moment in range(step_count):
        near_halo = lax.ppermute(near_edge, "space", within)
        far_halo = lax.ppermute(far_edge, "space", across)
        partial_next, imaging, near_edge = tile_call(
            moment, tile_near, current, previous, near_halo, speed_sq, forward, source,
            imaging, None,
        )
        advanced, imaging, far_edge = tile_call(
            moment, tile_far, current, previous, far_halo, speed_sq, forward, source,
            imaging, partial_next,
        )
        previous, current = (current, advanced)
    row_index = jnp.arange(lax.axis_size("shot") * block_rows, dtype=jnp.int32) - shift_rows
    inside = (row_index >= 0) & (row_index < cells_y)
    chosen = jnp.take(imaging, jnp.clip(row_index, 0, cells_y - 1), axis=0)
    placed = jnp.where(inside[:, None, None], chosen, 0.0)
    shots = lax.axis_size("shot")
    placed = placed.reshape((shots, block_rows) + placed.shape[1:])
    arrived = lax.all_to_all(placed, "shot", split_axis=0, concat_axis=0, tiled=True)
    gradient = jnp.sum(arrived, axis=0)
    return (gradient, current[None])


def solution(mesh):
    in_specs = (
        P("shot", "space", None),
        P("shot", "space", None),
        P("shot", "space"),
        P(),
        P("shot"),
        P("shot", None, "space", None),
        P("shot", None, "space", None),
        P("shot", None, "space", None),
        P("shot", None, None, "space", None),
    )
    out_specs = (P("shot", "space", None), P("shot", None, "space", None))
    return jax.shard_map(local, mesh=mesh, in_specs=in_specs, out_specs=out_specs, check_vma=False)
```

```python
import functools

import jax
import jax.numpy as jnp
from jax import lax
from jax.sharding import PartitionSpec as P
from jax.experimental import pallas as pl
from jax.experimental.pallas import tpu as pltpu

STENCIL = (-205.0 / 72.0, 8.0 / 5.0, -1.0 / 5.0, 8.0 / 315.0, -1.0 / 560.0)


def extended(shard, sides, width):
    for axis, dim in sides:
        devices, length = (lax.axis_size(axis), shard.shape[dim])
        up = [(i, (i + 1) % devices) for i in range(devices - 1)]
        down = [(j, i) for i, j in up]
        last = lax.slice_in_dim(shard, length - width, length, axis=dim)
        leading = lax.slice_in_dim(shard, 0, width, axis=dim)
        before = lax.ppermute(last, axis, up)
        after = lax.ppermute(leading, axis, down)
        shard = jnp.concatenate([before, shard, after], axis=dim)
    return shard


def laplace(padded):
    span_y = padded.shape[0] - 8
    span_x = padded.shape[1] - 8
    span_z = padded.shape[2] - 8

    def window(shift_y, shift_x, shift_z):
        return padded[
            4 + shift_y : 4 + shift_y + span_y,
            4 + shift_x : 4 + shift_x + span_x,
            4 + shift_z : 4 + shift_z + span_z,
        ]

    summed = 3.0 * STENCIL[0] * window(0, 0, 0)
    for reach in range(1, 5):
        beside_all = (
            window(reach, 0, 0)
            + window(-reach, 0, 0)
            + window(0, reach, 0)
            + window(0, -reach, 0)
            + window(0, 0, reach)
            + window(0, 0, -reach)
        )
        summed = summed + STENCIL[reach] * beside_all
    return summed


def pad_sides(field):
    return jnp.pad(field, ((4, 4), (0, 0), (4, 4)))


ROWS = 1
BLOCK = 8
SLAB_ROWS = 4
SLAB_UNROLL = 2


def step_kernel(moment, cur_ref, prev_ref, lo_ref, hi_ref, vel_ref, fwd_ref, src_ref, img_ref,
                next_ref, img_out_ref, first_ref, last_ref, pad_ref):
    cells_y, cells_x, cells_z = cur_ref.shape
    width = lo_ref.shape[1]
    block = pl.program_id(0)

    @pl.when(block == 0)
    def _():
        zeros = jnp.zeros((4, pad_ref.shape[1], cells_z), jnp.float32)
        pad_ref[0:4] = zeros
        pad_ref[4 + cells_y : 8 + cells_y] = zeros
        pad_ref[4 : 4 + cells_y, 8 - width : 8] = lo_ref[...]
        pad_ref[4 : 4 + cells_y, 8 : 8 + cells_x] = cur_ref[...]
        pad_ref[4 : 4 + cells_y, 8 + cells_x : 8 + cells_x + width] = hi_ref[...]

    def body(chunk, carry):
        y0 = pl.multiple_of(chunk * ROWS, ROWS)
        base = block * BLOCK + y0 + 4

        def window(shift_y, shift_x):
            return pad_ref[pl.ds(base + shift_y, ROWS), 8 + shift_x : 8 + shift_x + cells_x, :]

        center = window(0, 0)
        depth = lax.broadcasted_iota(jnp.int32, center.shape, 2)
        half = cells_z // 2
        low, high = center[..., :half], center[..., half:]
        lane = lax.broadcasted_iota(jnp.int32, low.shape, 2)

        def along_z(reach):
            low_up = pltpu.roll(low, half - reach, 2)
            high_up = pltpu.roll(high, half - reach, 2)
            low_down = pltpu.roll(low, reach, 2)
            high_down = pltpu.roll(high, reach, 2)
            head = lane < half - reach
            tail = lane >= reach
            up = jnp.concatenate(
                [jnp.where(head, low_up, high_up), jnp.where(head, high_up, 0.0)], axis=2
            )
            down = jnp.concatenate(
                [jnp.where(tail, low_down, 0.0), jnp.where(tail, high_down, low_down)], axis=2
            )
            return up, down

        summed = 3.0 * STENCIL[0] * center
        for reach in range(1, 5):
            z_up, z_down = along_z(reach)
            beside_all = (
                window(reach, 0)
                + window(-reach, 0)
                + window(0, reach)
                + window(0, -reach)
                + z_up
                + z_down
            )
            summed = summed + STENCIL[reach] * beside_all
        rows = pl.ds(y0, ROWS)
        advanced = 2.0 * center - prev_ref[rows] + vel_ref[rows] * summed
        source_rows = pl.ds(block * BLOCK + y0, ROWS)
        source = jnp.broadcast_to(src_ref[source_rows, :, pl.ds(moment, 1)], advanced.shape)
        advanced = jnp.where(depth == 0, advanced + source, advanced)
        next_ref[rows] = advanced
        img_out_ref[rows] = img_ref[rows] + fwd_ref[rows].astype(jnp.float32) * advanced
        first_ref[rows] = advanced[:, :width]
        last_ref[rows] = advanced[:, cells_x - width :]
        return carry

    lax.fori_loop(0, BLOCK // ROWS, body, 0, unroll=4)


def step_call(moment, current, previous, lo, hi, speed_sq, forward, source, imaging):
    cells_y, cells_x, cells_z = current.shape
    width = lo.shape[1]
    whole = pl.BlockSpec((cells_y, cells_x, cells_z), lambda i: (0, 0, 0))
    whole_rim = pl.BlockSpec((cells_y, width, cells_z), lambda i: (0, 0, 0))
    field = pl.BlockSpec((BLOCK, cells_x, cells_z), lambda i: (i, 0, 0))
    rim = pl.BlockSpec((BLOCK, width, cells_z), lambda i: (i, 0, 0))
    fwd_spec = pl.BlockSpec((None, BLOCK, cells_x, cells_z), lambda i: (moment, i, 0, 0))
    src_spec = pl.BlockSpec(source.shape, lambda i: (0, 0, 0))
    f32 = jnp.float32
    return pl.pallas_call(
        functools.partial(step_kernel, moment),
        grid=(cells_y // BLOCK,),
        out_shape=(
            jax.ShapeDtypeStruct(current.shape, f32),
            jax.ShapeDtypeStruct(current.shape, f32),
            jax.ShapeDtypeStruct(lo.shape, f32),
            jax.ShapeDtypeStruct(lo.shape, f32),
        ),
        in_specs=[whole, field, whole_rim, whole_rim, field, fwd_spec, src_spec, field],
        out_specs=(field, field, rim, rim),
        scratch_shapes=[pltpu.VMEM((cells_y + 8, cells_x + 16, cells_z), f32)],
        input_output_aliases={7: 1},
        compiler_params=pltpu.CompilerParams(
            dimension_semantics=("arbitrary",), vmem_limit_bytes=48 * 1024 * 1024
        ),
    )(current, previous, lo, hi, speed_sq, forward, source, imaging)


def tile_kernel(moment, chained, tile_ref, cur_ref, prev_ref, halo_ref, vel_ref, fwd_ref, src_ref,
                img_ref, *rest):
    if chained:
        rest = rest[1:]
    next_ref, img_out_ref, edge_ref, pad_ref = rest
    cells_y, cells_x, cells_z = cur_ref.shape
    width = halo_ref.shape[1]
    part = cells_x // 2
    zeros = jnp.zeros((4, pad_ref.shape[1], cells_z), jnp.float32)
    pad_ref[0:4] = zeros
    pad_ref[4 + cells_y : 8 + cells_y] = zeros
    pad_ref[4 : 4 + cells_y, 8 : 8 + cells_x] = cur_ref[...]

    def compute(tile):
        if tile == 0:
            pad_ref[4 : 4 + cells_y, 8 - width : 8] = halo_ref[...]
        else:
            pad_ref[4 : 4 + cells_y, 8 + cells_x : 8 + cells_x + width] = halo_ref[...]
        start = 8 + tile * part

        def body(chunk, carry):
            y0 = chunk * SLAB_ROWS
            base = y0 + 4
            slab = pad_ref[pl.ds(base - 4, SLAB_ROWS + 8), start : start + part, :]

            def window(shift_y, shift_x):
                if shift_x == 0:
                    return slab[4 + shift_y : 4 + shift_y + SLAB_ROWS]
                return pad_ref[
                    pl.ds(base + shift_y, SLAB_ROWS), start + shift_x : start + shift_x + part, :
                ]

            center = window(0, 0)
            depth = lax.broadcasted_iota(jnp.int32, center.shape, 2)

            def along_z(reach):
                up = pltpu.roll(center, cells_z - reach, 2)
                down = pltpu.roll(center, reach, 2)
                return (
                    jnp.where(depth + reach < cells_z, up, 0.0),
                    jnp.where(depth - reach >= 0, down, 0.0),
                )

            summed = 3.0 * STENCIL[0] * center
            for reach in range(1, 5):
                z_up, z_down = along_z(reach)
                beside_all = (
                    window(reach, 0)
                    + window(-reach, 0)
                    + window(0, reach)
                    + window(0, -reach)
                    + z_up
                    + z_down
                )
                summed = summed + STENCIL[reach] * beside_all
            rows = pl.ds(y0, SLAB_ROWS)
            advanced = 2.0 * center - prev_ref[rows] + vel_ref[rows] * summed
            source = src_ref[rows, tile * part : (tile + 1) * part, pl.ds(moment, 1)]
            source = jnp.broadcast_to(source, advanced.shape)
            advanced = jnp.where(depth == 0, advanced + source, advanced)
            next_ref[rows] = advanced
            accel = fwd_ref[rows].astype(jnp.float32)[:, tile * part : (tile + 1) * part]
            img_out_ref[rows] = img_ref[rows] + accel * advanced
            if tile == 0:
                edge_ref[rows] = advanced[:, :width]
            else:
                edge_ref[rows] = advanced[:, part - width :]
            return carry

        lax.fori_loop(0, cells_y // SLAB_ROWS, body, 0, unroll=SLAB_UNROLL)

    for tile in range(2):
        pl.when(tile_ref[0] == tile)(functools.partial(compute, tile))


def tile_call(moment, tile, current, previous, halo_rim, speed_sq, forward, source, imaging, chain):
    cells_y, cells_x, cells_z = current.shape
    width = halo_rim.shape[1]
    part = cells_x // 2
    whole = pl.BlockSpec((cells_y, cells_x, cells_z), lambda i, t: (0, 0, 0))
    rim = pl.BlockSpec((cells_y, width, cells_z), lambda i, t: (0, 0, 0))
    half = pl.BlockSpec((cells_y, part, cells_z), lambda i, t: (0, t[0], 0))
    fwd_spec = pl.BlockSpec((None, cells_y, cells_x, cells_z), lambda i, t: (moment, 0, 0, 0))
    src_spec = pl.BlockSpec(source.shape, lambda i, t: (0, 0, 0))
    f32 = jnp.float32
    cells = cells_y * part * cells_z
    chained = chain is not None
    in_specs = [whole, half, rim, half, fwd_spec, src_spec, half]
    operands = [tile, current, previous, halo_rim, speed_sq, forward, source, imaging]
    aliases = {7: 1}
    if chained:
        in_specs.append(pl.BlockSpec(memory_space=pl.ANY))
        operands.append(chain)
        aliases[8] = 0
    return pl.pallas_call(
        functools.partial(tile_kernel, moment, chained),
        grid_spec=pltpu.PrefetchScalarGridSpec(
            num_scalar_prefetch=1,
            grid=(1,),
            in_specs=in_specs,
            out_specs=(half, half, rim),
            scratch_shapes=[pltpu.VMEM((cells_y + 8, cells_x + 16, cells_z), f32)],
        ),
        out_shape=(
            jax.ShapeDtypeStruct(current.shape, f32),
            jax.ShapeDtypeStruct(current.shape, f32),
            jax.ShapeDtypeStruct(halo_rim.shape, f32),
        ),
        input_output_aliases=aliases,
        cost_estimate=pl.CostEstimate(
            flops=60 * cells, bytes_accessed=28 * cells, transcendentals=0
        ),
        compiler_params=pltpu.CompilerParams(vmem_limit_bytes=48 * 1024 * 1024),
    )(*operands)


def halo(first, last):
    axis = "space"
    devices = lax.axis_size(axis)
    even = lax.axis_index(axis) % 2 == 0
    within = [(i, i ^ 1) for i in range(devices)]
    across = [(i, i + 1 - 2 * ((i + 1) % 2)) for i in range(1, devices - 1)]
    got_within = lax.ppermute(jnp.where(even, last, first), axis, within)
    got_across = lax.ppermute(jnp.where(even, first, last), axis, across)
    lo = jnp.where(even, got_across, got_within)
    hi = jnp.where(even, got_within, got_across)
    return lo, hi


def local(
    residual,
    record_tile,
    record_cell,
    time_filter,
    offsets,
    velocity,
    adjoint_prev,
    adjoint_now,
    forward_accel,
):
    tiles_count = lax.axis_size("space")
    record_count = residual.shape[1]
    cells_y = velocity.shape[1]
    cells_x = velocity.shape[2]
    cells_z = velocity.shape[3]
    step_count = forward_accel.shape[1]
    slot_count = record_count * 3 // 16
    surface = cells_y * cells_x
    block_rows = (cells_y + cells_y // 4) // lax.axis_size("shot")
    trace_rows = residual[0]
    tile_ids = record_tile[0, :, 0]
    cell_ids = record_cell[0]
    record_order = jnp.arange(record_count, dtype=jnp.int32)
    same_before = (tile_ids[:, None] == tile_ids[None, :]) & (
        record_order[:, None] < record_order[None, :]
    )
    order_rank = jnp.sum(same_before.astype(jnp.int32), axis=0)
    slot_index = tile_ids * slot_count + order_rank
    filtered = jnp.dot(trace_rows, time_filter.T, preferred_element_type=jnp.float32)
    payload = jnp.concatenate(
        [filtered, (cell_ids + 1).astype(jnp.float32)[:, None]], axis=1
    )
    slots = tiles_count * slot_count
    placing = (
        slot_index[None, :] == jnp.arange(slots, dtype=jnp.int32)[:, None]
    ).astype(jnp.float32)
    buffer = jnp.dot(placing, payload, precision=lax.Precision.HIGHEST)
    buffer = buffer.reshape(tiles_count, slot_count, step_count + 1)
    arrived = lax.all_to_all(buffer, "space", split_axis=0, concat_axis=0, tiled=True)
    arrived = arrived.reshape(slots, step_count + 1)
    cell_of = arrived[:, step_count].astype(jnp.int32)
    gathering = (
        cell_of[:, None] == jnp.arange(1, surface + 1, dtype=jnp.int32)[None, :]
    ).astype(jnp.float32)
    source = lax.dot_general(
        gathering,
        arrived[:, :step_count],
        (((0,), (0,)), ((), ())),
        precision=lax.Precision.HIGHEST,
    )
    source = source.reshape(cells_y, cells_x, step_count)
    shift_rows = offsets[0]
    speed_sq = velocity[0]
    previous = adjoint_prev[0]
    current = adjoint_now[0]
    forward = forward_accel[0]
    imaging = jnp.zeros_like(current)
    width = 4
    odd = lax.axis_index("space") % 2
    tile_near = (1 - odd).reshape(1).astype(jnp.int32)
    tile_far = odd.reshape(1).astype(jnp.int32)
    devices = lax.axis_size("space")
    within = [(i, i ^ 1) for i in range(devices)]
    across = [(i, i + 1 - 2 * ((i + 1) % 2)) for i in range(1, devices - 1)]
    zero = jnp.zeros((), jnp.int32)
    near_start = (1 - odd) * (cells_x - width)
    near_edge = lax.dynamic_slice(current, (zero, near_start, zero), (cells_y, width, cells_z))
    far_start = odd * (cells_x - width)
    far_edge = lax.dynamic_slice(current, (zero, far_start, zero), (cells_y, width, cells_z))
    for moment in range(step_count):
        near_halo = lax.ppermute(near_edge, "space", within)
        partial_next, imaging, near_edge = tile_call(
            moment, tile_near, current, previous, near_halo, speed_sq, forward, source,
            imaging, None,
        )
        far_edge, partial_next = lax.optimization_barrier((far_edge, partial_next))
        far_halo = lax.ppermute(far_edge, "space", across)
        advanced, imaging, far_edge = tile_call(
            moment, tile_far, current, previous, far_halo, speed_sq, forward, source,
            imaging, partial_next,
        )
        previous, current = (current, advanced)
    row_index = jnp.arange(lax.axis_size("shot") * block_rows, dtype=jnp.int32) - shift_rows
    inside = (row_index >= 0) & (row_index < cells_y)
    chosen = jnp.take(imaging, jnp.clip(row_index, 0, cells_y - 1), axis=0)
    placed = jnp.where(inside[:, None, None], chosen, 0.0)
    shots = lax.axis_size("shot")
    placed = placed.reshape((shots, block_rows) + placed.shape[1:])
    arrived = lax.all_to_all(placed, "shot", split_axis=0, concat_axis=0, tiled=True)
    gradient = jnp.sum(arrived, axis=0)
    return (gradient, current[None])


def solution(mesh):
    in_specs = (
        P("shot", "space", None),
        P("shot", "space", None),
        P("shot", "space"),
        P(),
        P("shot"),
        P("shot", None, "space", None),
        P("shot", None, "space", None),
        P("shot", None, "space", None),
        P("shot", None, None, "space", None),
    )
    out_specs = (P("shot", "space", None), P("shot", None, "space", None))
    return jax.shard_map(local, mesh=mesh, in_specs=in_specs, out_specs=out_specs, check_vma=False)
```

```python
import functools

import jax
import jax.numpy as jnp
from jax import lax
from jax.sharding import PartitionSpec as P
from jax.experimental import pallas as pl
from jax.experimental.pallas import tpu as pltpu

STENCIL = (-205.0 / 72.0, 8.0 / 5.0, -1.0 / 5.0, 8.0 / 315.0, -1.0 / 560.0)


def extended(shard, sides, width):
    for axis, dim in sides:
        devices, length = (lax.axis_size(axis), shard.shape[dim])
        up = [(i, (i + 1) % devices) for i in range(devices - 1)]
        down = [(j, i) for i, j in up]
        last = lax.slice_in_dim(shard, length - width, length, axis=dim)
        leading = lax.slice_in_dim(shard, 0, width, axis=dim)
        before = lax.ppermute(last, axis, up)
        after = lax.ppermute(leading, axis, down)
        shard = jnp.concatenate([before, shard, after], axis=dim)
    return shard


def laplace(padded):
    span_y = padded.shape[0] - 8
    span_x = padded.shape[1] - 8
    span_z = padded.shape[2] - 8

    def window(shift_y, shift_x, shift_z):
        return padded[
            4 + shift_y : 4 + shift_y + span_y,
            4 + shift_x : 4 + shift_x + span_x,
            4 + shift_z : 4 + shift_z + span_z,
        ]

    summed = 3.0 * STENCIL[0] * window(0, 0, 0)
    for reach in range(1, 5):
        beside_all = (
            window(reach, 0, 0)
            + window(-reach, 0, 0)
            + window(0, reach, 0)
            + window(0, -reach, 0)
            + window(0, 0, reach)
            + window(0, 0, -reach)
        )
        summed = summed + STENCIL[reach] * beside_all
    return summed


def pad_sides(field):
    return jnp.pad(field, ((4, 4), (0, 0), (4, 4)))


ROWS = 1
BLOCK = 8
SLAB_ROWS = 4
SLAB_UNROLL = 2


def step_kernel(moment, cur_ref, prev_ref, lo_ref, hi_ref, vel_ref, fwd_ref, src_ref, img_ref,
                next_ref, img_out_ref, first_ref, last_ref, pad_ref):
    cells_y, cells_x, cells_z = cur_ref.shape
    width = lo_ref.shape[1]
    block = pl.program_id(0)

    @pl.when(block == 0)
    def _():
        zeros = jnp.zeros((4, pad_ref.shape[1], cells_z), jnp.float32)
        pad_ref[0:4] = zeros
        pad_ref[4 + cells_y : 8 + cells_y] = zeros
        pad_ref[4 : 4 + cells_y, 8 - width : 8] = lo_ref[...]
        pad_ref[4 : 4 + cells_y, 8 : 8 + cells_x] = cur_ref[...]
        pad_ref[4 : 4 + cells_y, 8 + cells_x : 8 + cells_x + width] = hi_ref[...]

    def body(chunk, carry):
        y0 = pl.multiple_of(chunk * ROWS, ROWS)
        base = block * BLOCK + y0 + 4

        def window(shift_y, shift_x):
            return pad_ref[pl.ds(base + shift_y, ROWS), 8 + shift_x : 8 + shift_x + cells_x, :]

        center = window(0, 0)
        depth = lax.broadcasted_iota(jnp.int32, center.shape, 2)
        half = cells_z // 2
        low, high = center[..., :half], center[..., half:]
        lane = lax.broadcasted_iota(jnp.int32, low.shape, 2)

        def along_z(reach):
            low_up = pltpu.roll(low, half - reach, 2)
            high_up = pltpu.roll(high, half - reach, 2)
            low_down = pltpu.roll(low, reach, 2)
            high_down = pltpu.roll(high, reach, 2)
            head = lane < half - reach
            tail = lane >= reach
            up = jnp.concatenate(
                [jnp.where(head, low_up, high_up), jnp.where(head, high_up, 0.0)], axis=2
            )
            down = jnp.concatenate(
                [jnp.where(tail, low_down, 0.0), jnp.where(tail, high_down, low_down)], axis=2
            )
            return up, down

        summed = 3.0 * STENCIL[0] * center
        for reach in range(1, 5):
            z_up, z_down = along_z(reach)
            beside_all = (
                window(reach, 0)
                + window(-reach, 0)
                + window(0, reach)
                + window(0, -reach)
                + z_up
                + z_down
            )
            summed = summed + STENCIL[reach] * beside_all
        rows = pl.ds(y0, ROWS)
        advanced = 2.0 * center - prev_ref[rows] + vel_ref[rows] * summed
        source_rows = pl.ds(block * BLOCK + y0, ROWS)
        source = jnp.broadcast_to(src_ref[source_rows, :, pl.ds(moment, 1)], advanced.shape)
        advanced = jnp.where(depth == 0, advanced + source, advanced)
        next_ref[rows] = advanced
        img_out_ref[rows] = img_ref[rows] + fwd_ref[rows].astype(jnp.float32) * advanced
        first_ref[rows] = advanced[:, :width]
        last_ref[rows] = advanced[:, cells_x - width :]
        return carry

    lax.fori_loop(0, BLOCK // ROWS, body, 0, unroll=4)


def step_call(moment, current, previous, lo, hi, speed_sq, forward, source, imaging):
    cells_y, cells_x, cells_z = current.shape
    width = lo.shape[1]
    whole = pl.BlockSpec((cells_y, cells_x, cells_z), lambda i: (0, 0, 0))
    whole_rim = pl.BlockSpec((cells_y, width, cells_z), lambda i: (0, 0, 0))
    field = pl.BlockSpec((BLOCK, cells_x, cells_z), lambda i: (i, 0, 0))
    rim = pl.BlockSpec((BLOCK, width, cells_z), lambda i: (i, 0, 0))
    fwd_spec = pl.BlockSpec((None, BLOCK, cells_x, cells_z), lambda i: (moment, i, 0, 0))
    src_spec = pl.BlockSpec(source.shape, lambda i: (0, 0, 0))
    f32 = jnp.float32
    return pl.pallas_call(
        functools.partial(step_kernel, moment),
        grid=(cells_y // BLOCK,),
        out_shape=(
            jax.ShapeDtypeStruct(current.shape, f32),
            jax.ShapeDtypeStruct(current.shape, f32),
            jax.ShapeDtypeStruct(lo.shape, f32),
            jax.ShapeDtypeStruct(lo.shape, f32),
        ),
        in_specs=[whole, field, whole_rim, whole_rim, field, fwd_spec, src_spec, field],
        out_specs=(field, field, rim, rim),
        scratch_shapes=[pltpu.VMEM((cells_y + 8, cells_x + 16, cells_z), f32)],
        input_output_aliases={7: 1},
        compiler_params=pltpu.CompilerParams(
            dimension_semantics=("arbitrary",), vmem_limit_bytes=48 * 1024 * 1024
        ),
    )(current, previous, lo, hi, speed_sq, forward, source, imaging)


def tile_kernel(moment, chained, tile_ref, cur_ref, prev_ref, halo_ref, vel_ref, fwd_ref, src_ref,
                img_ref, *rest):
    if chained:
        rest = rest[1:]
    next_ref, img_out_ref, edge_ref, pad_ref = rest
    cells_y, cells_x, cells_z = cur_ref.shape
    width = halo_ref.shape[1]
    part = cells_x // 2
    zeros = jnp.zeros((4, pad_ref.shape[1], cells_z), jnp.float32)
    pad_ref[0:4] = zeros
    pad_ref[4 + cells_y : 8 + cells_y] = zeros
    pad_ref[4 : 4 + cells_y, 8 : 8 + cells_x] = cur_ref[...]

    def compute(tile):
        if tile == 0:
            pad_ref[4 : 4 + cells_y, 8 - width : 8] = halo_ref[...]
        else:
            pad_ref[4 : 4 + cells_y, 8 + cells_x : 8 + cells_x + width] = halo_ref[...]
        start = 8 + tile * part

        def body(chunk, carry):
            y0 = chunk * SLAB_ROWS
            base = y0 + 4
            slab = pad_ref[pl.ds(base - 4, SLAB_ROWS + 8), start : start + part, :]

            def window(shift_y, shift_x):
                if shift_x == 0:
                    return slab[4 + shift_y : 4 + shift_y + SLAB_ROWS]
                return pad_ref[
                    pl.ds(base + shift_y, SLAB_ROWS), start + shift_x : start + shift_x + part, :
                ]

            center = window(0, 0)
            depth = lax.broadcasted_iota(jnp.int32, center.shape, 2)

            def along_z(reach):
                up = pltpu.roll(center, cells_z - reach, 2)
                down = pltpu.roll(center, reach, 2)
                return (
                    jnp.where(depth + reach < cells_z, up, 0.0),
                    jnp.where(depth - reach >= 0, down, 0.0),
                )

            summed = 3.0 * STENCIL[0] * center
            for reach in range(1, 5):
                z_up, z_down = along_z(reach)
                beside_all = (
                    window(reach, 0)
                    + window(-reach, 0)
                    + window(0, reach)
                    + window(0, -reach)
                    + z_up
                    + z_down
                )
                summed = summed + STENCIL[reach] * beside_all
            rows = pl.ds(y0, SLAB_ROWS)
            advanced = 2.0 * center - prev_ref[rows] + vel_ref[rows] * summed
            source = src_ref[rows, tile * part : (tile + 1) * part, pl.ds(moment, 1)]
            source = jnp.broadcast_to(source, advanced.shape)
            advanced = jnp.where(depth == 0, advanced + source, advanced)
            next_ref[rows] = advanced
            accel = fwd_ref[rows].astype(jnp.float32)[:, tile * part : (tile + 1) * part]
            img_out_ref[rows] = img_ref[rows] + accel * advanced
            if tile == 0:
                edge_ref[rows] = advanced[:, :width]
            else:
                edge_ref[rows] = advanced[:, part - width :]
            return carry

        lax.fori_loop(0, cells_y // SLAB_ROWS, body, 0, unroll=SLAB_UNROLL)

    for tile in range(2):
        pl.when(tile_ref[0] == tile)(functools.partial(compute, tile))


def tile_call(moment, tile, current, previous, halo_rim, speed_sq, forward, source, imaging, chain):
    cells_y, cells_x, cells_z = current.shape
    width = halo_rim.shape[1]
    part = cells_x // 2
    whole = pl.BlockSpec((cells_y, cells_x, cells_z), lambda i, t: (0, 0, 0))
    rim = pl.BlockSpec((cells_y, width, cells_z), lambda i, t: (0, 0, 0))
    half = pl.BlockSpec((cells_y, part, cells_z), lambda i, t: (0, t[0], 0))
    fwd_spec = pl.BlockSpec((None, cells_y, cells_x, cells_z), lambda i, t: (moment, 0, 0, 0))
    src_spec = pl.BlockSpec(source.shape, lambda i, t: (0, 0, 0))
    f32 = jnp.float32
    cells = cells_y * part * cells_z
    chained = chain is not None
    in_specs = [whole, half, rim, half, fwd_spec, src_spec, half]
    operands = [tile, current, previous, halo_rim, speed_sq, forward, source, imaging]
    aliases = {7: 1}
    if chained:
        in_specs.append(pl.BlockSpec(memory_space=pl.ANY))
        operands.append(chain)
        aliases[8] = 0
    return pl.pallas_call(
        functools.partial(tile_kernel, moment, chained),
        grid_spec=pltpu.PrefetchScalarGridSpec(
            num_scalar_prefetch=1,
            grid=(1,),
            in_specs=in_specs,
            out_specs=(half, half, rim),
            scratch_shapes=[pltpu.VMEM((cells_y + 8, cells_x + 16, cells_z), f32)],
        ),
        out_shape=(
            jax.ShapeDtypeStruct(current.shape, f32),
            jax.ShapeDtypeStruct(current.shape, f32),
            jax.ShapeDtypeStruct(halo_rim.shape, f32),
        ),
        input_output_aliases=aliases,
        cost_estimate=pl.CostEstimate(
            flops=60 * cells, bytes_accessed=28 * cells, transcendentals=0
        ),
        compiler_params=pltpu.CompilerParams(vmem_limit_bytes=48 * 1024 * 1024),
    )(*operands)


def exact_select(select, table, dimension_numbers):
    high = lax.reduce_precision(table, exponent_bits=8, mantissa_bits=7)
    rest = table - high
    middle = lax.reduce_precision(rest, exponent_bits=8, mantissa_bits=7)
    low = rest - middle
    select = select.astype(jnp.bfloat16)
    parts = [
        lax.dot_general(
            select, part.astype(jnp.bfloat16), dimension_numbers,
            preferred_element_type=jnp.float32,
        )
        for part in (high, middle, low)
    ]
    return (parts[0] + parts[1]) + parts[2]


def halo(first, last):
    axis = "space"
    devices = lax.axis_size(axis)
    even = lax.axis_index(axis) % 2 == 0
    within = [(i, i ^ 1) for i in range(devices)]
    across = [(i, i + 1 - 2 * ((i + 1) % 2)) for i in range(1, devices - 1)]
    got_within = lax.ppermute(jnp.where(even, last, first), axis, within)
    got_across = lax.ppermute(jnp.where(even, first, last), axis, across)
    lo = jnp.where(even, got_across, got_within)
    hi = jnp.where(even, got_within, got_across)
    return lo, hi


def local(
    residual,
    record_tile,
    record_cell,
    time_filter,
    offsets,
    velocity,
    adjoint_prev,
    adjoint_now,
    forward_accel,
):
    tiles_count = lax.axis_size("space")
    record_count = residual.shape[1]
    cells_y = velocity.shape[1]
    cells_x = velocity.shape[2]
    cells_z = velocity.shape[3]
    step_count = forward_accel.shape[1]
    slot_count = record_count * 3 // 16
    surface = cells_y * cells_x
    block_rows = (cells_y + cells_y // 4) // lax.axis_size("shot")
    trace_rows = residual[0]
    tile_ids = record_tile[0, :, 0]
    cell_ids = record_cell[0]
    record_order = jnp.arange(record_count, dtype=jnp.int32)
    same_before = (tile_ids[:, None] == tile_ids[None, :]) & (
        record_order[:, None] < record_order[None, :]
    )
    order_rank = jnp.sum(same_before.astype(jnp.int32), axis=0)
    slot_index = tile_ids * slot_count + order_rank
    filtered = jnp.dot(trace_rows, time_filter.T, preferred_element_type=jnp.float32)
    payload = jnp.concatenate(
        [filtered, (cell_ids + 1).astype(jnp.float32)[:, None]], axis=1
    )
    slots = tiles_count * slot_count
    placing = (
        slot_index[None, :] == jnp.arange(slots, dtype=jnp.int32)[:, None]
    ).astype(jnp.float32)
    buffer = exact_select(placing, payload, (((1,), (0,)), ((), ())))
    buffer = buffer.reshape(tiles_count, slot_count, step_count + 1)
    arrived = lax.all_to_all(buffer, "space", split_axis=0, concat_axis=0, tiled=True)
    arrived = arrived.reshape(slots, step_count + 1)
    cell_of = arrived[:, step_count].astype(jnp.int32)
    gathering = (
        cell_of[:, None] == jnp.arange(1, surface + 1, dtype=jnp.int32)[None, :]
    ).astype(jnp.float32)
    source = exact_select(gathering, arrived[:, :step_count], (((0,), (0,)), ((), ())))
    source = source.reshape(cells_y, cells_x, step_count)
    shift_rows = offsets[0]
    speed_sq = velocity[0]
    previous = adjoint_prev[0]
    current = adjoint_now[0]
    forward = forward_accel[0]
    imaging = jnp.zeros_like(current)
    width = 4
    odd = lax.axis_index("space") % 2
    tile_near = (1 - odd).reshape(1).astype(jnp.int32)
    tile_far = odd.reshape(1).astype(jnp.int32)
    devices = lax.axis_size("space")
    within = [(i, i ^ 1) for i in range(devices)]
    across = [(i, i + 1 - 2 * ((i + 1) % 2)) for i in range(1, devices - 1)]
    zero = jnp.zeros((), jnp.int32)
    near_start = (1 - odd) * (cells_x - width)
    near_edge = lax.dynamic_slice(current, (zero, near_start, zero), (cells_y, width, cells_z))
    far_start = odd * (cells_x - width)
    far_edge = lax.dynamic_slice(current, (zero, far_start, zero), (cells_y, width, cells_z))
    for moment in range(step_count):
        near_halo = lax.ppermute(near_edge, "space", within)
        far_halo = lax.ppermute(far_edge, "space", across)
        partial_next, imaging, near_edge = tile_call(
            moment, tile_near, current, previous, near_halo, speed_sq, forward, source,
            imaging, None,
        )
        advanced, imaging, far_edge = tile_call(
            moment, tile_far, current, previous, far_halo, speed_sq, forward, source,
            imaging, partial_next,
        )
        previous, current = (current, advanced)
    row_index = jnp.arange(lax.axis_size("shot") * block_rows, dtype=jnp.int32) - shift_rows
    inside = (row_index >= 0) & (row_index < cells_y)
    chosen = jnp.take(imaging, jnp.clip(row_index, 0, cells_y - 1), axis=0)
    placed = jnp.where(inside[:, None, None], chosen, 0.0)
    shots = lax.axis_size("shot")
    placed = placed.reshape((shots, block_rows) + placed.shape[1:])
    arrived = lax.all_to_all(placed, "shot", split_axis=0, concat_axis=0, tiled=True)
    gradient = jnp.sum(arrived, axis=0)
    return (gradient, current[None])


def solution(mesh):
    in_specs = (
        P("shot", "space", None),
        P("shot", "space", None),
        P("shot", "space"),
        P(),
        P("shot"),
        P("shot", None, "space", None),
        P("shot", None, "space", None),
        P("shot", None, "space", None),
        P("shot", None, None, "space", None),
    )
    out_specs = (P("shot", "space", None), P("shot", None, "space", None))
    return jax.shard_map(local, mesh=mesh, in_specs=in_specs, out_specs=out_specs, check_vma=False)
```

```python
import functools

import jax
import jax.numpy as jnp
from jax import lax
from jax.sharding import PartitionSpec as P
from jax.experimental import pallas as pl
from jax.experimental.pallas import tpu as pltpu

STENCIL = (-205.0 / 72.0, 8.0 / 5.0, -1.0 / 5.0, 8.0 / 315.0, -1.0 / 560.0)


def extended(shard, sides, width):
    for axis, dim in sides:
        devices, length = (lax.axis_size(axis), shard.shape[dim])
        up = [(i, (i + 1) % devices) for i in range(devices - 1)]
        down = [(j, i) for i, j in up]
        last = lax.slice_in_dim(shard, length - width, length, axis=dim)
        leading = lax.slice_in_dim(shard, 0, width, axis=dim)
        before = lax.ppermute(last, axis, up)
        after = lax.ppermute(leading, axis, down)
        shard = jnp.concatenate([before, shard, after], axis=dim)
    return shard


def laplace(padded):
    span_y = padded.shape[0] - 8
    span_x = padded.shape[1] - 8
    span_z = padded.shape[2] - 8

    def window(shift_y, shift_x, shift_z):
        return padded[
            4 + shift_y : 4 + shift_y + span_y,
            4 + shift_x : 4 + shift_x + span_x,
            4 + shift_z : 4 + shift_z + span_z,
        ]

    summed = 3.0 * STENCIL[0] * window(0, 0, 0)
    for reach in range(1, 5):
        beside_all = (
            window(reach, 0, 0)
            + window(-reach, 0, 0)
            + window(0, reach, 0)
            + window(0, -reach, 0)
            + window(0, 0, reach)
            + window(0, 0, -reach)
        )
        summed = summed + STENCIL[reach] * beside_all
    return summed


def pad_sides(field):
    return jnp.pad(field, ((4, 4), (0, 0), (4, 4)))


ROWS = 1
BLOCK = 8
SLAB_ROWS = 4
SLAB_UNROLL = 2


def step_kernel(moment, cur_ref, prev_ref, lo_ref, hi_ref, vel_ref, fwd_ref, src_ref, img_ref,
                next_ref, img_out_ref, first_ref, last_ref, pad_ref):
    cells_y, cells_x, cells_z = cur_ref.shape
    width = lo_ref.shape[1]
    block = pl.program_id(0)

    @pl.when(block == 0)
    def _():
        zeros = jnp.zeros((4, pad_ref.shape[1], cells_z), jnp.float32)
        pad_ref[0:4] = zeros
        pad_ref[4 + cells_y : 8 + cells_y] = zeros
        pad_ref[4 : 4 + cells_y, 8 - width : 8] = lo_ref[...]
        pad_ref[4 : 4 + cells_y, 8 : 8 + cells_x] = cur_ref[...]
        pad_ref[4 : 4 + cells_y, 8 + cells_x : 8 + cells_x + width] = hi_ref[...]

    def body(chunk, carry):
        y0 = pl.multiple_of(chunk * ROWS, ROWS)
        base = block * BLOCK + y0 + 4

        def window(shift_y, shift_x):
            return pad_ref[pl.ds(base + shift_y, ROWS), 8 + shift_x : 8 + shift_x + cells_x, :]

        center = window(0, 0)
        depth = lax.broadcasted_iota(jnp.int32, center.shape, 2)
        half = cells_z // 2
        low, high = center[..., :half], center[..., half:]
        lane = lax.broadcasted_iota(jnp.int32, low.shape, 2)

        def along_z(reach):
            low_up = pltpu.roll(low, half - reach, 2)
            high_up = pltpu.roll(high, half - reach, 2)
            low_down = pltpu.roll(low, reach, 2)
            high_down = pltpu.roll(high, reach, 2)
            head = lane < half - reach
            tail = lane >= reach
            up = jnp.concatenate(
                [jnp.where(head, low_up, high_up), jnp.where(head, high_up, 0.0)], axis=2
            )
            down = jnp.concatenate(
                [jnp.where(tail, low_down, 0.0), jnp.where(tail, high_down, low_down)], axis=2
            )
            return up, down

        summed = 3.0 * STENCIL[0] * center
        for reach in range(1, 5):
            z_up, z_down = along_z(reach)
            beside_all = (
                window(reach, 0)
                + window(-reach, 0)
                + window(0, reach)
                + window(0, -reach)
                + z_up
                + z_down
            )
            summed = summed + STENCIL[reach] * beside_all
        rows = pl.ds(y0, ROWS)
        advanced = 2.0 * center - prev_ref[rows] + vel_ref[rows] * summed
        source_rows = pl.ds(block * BLOCK + y0, ROWS)
        source = jnp.broadcast_to(src_ref[source_rows, :, pl.ds(moment, 1)], advanced.shape)
        advanced = jnp.where(depth == 0, advanced + source, advanced)
        next_ref[rows] = advanced
        img_out_ref[rows] = img_ref[rows] + fwd_ref[rows].astype(jnp.float32) * advanced
        first_ref[rows] = advanced[:, :width]
        last_ref[rows] = advanced[:, cells_x - width :]
        return carry

    lax.fori_loop(0, BLOCK // ROWS, body, 0, unroll=4)


def step_call(moment, current, previous, lo, hi, speed_sq, forward, source, imaging):
    cells_y, cells_x, cells_z = current.shape
    width = lo.shape[1]
    whole = pl.BlockSpec((cells_y, cells_x, cells_z), lambda i: (0, 0, 0))
    whole_rim = pl.BlockSpec((cells_y, width, cells_z), lambda i: (0, 0, 0))
    field = pl.BlockSpec((BLOCK, cells_x, cells_z), lambda i: (i, 0, 0))
    rim = pl.BlockSpec((BLOCK, width, cells_z), lambda i: (i, 0, 0))
    fwd_spec = pl.BlockSpec((None, BLOCK, cells_x, cells_z), lambda i: (moment, i, 0, 0))
    src_spec = pl.BlockSpec(source.shape, lambda i: (0, 0, 0))
    f32 = jnp.float32
    return pl.pallas_call(
        functools.partial(step_kernel, moment),
        grid=(cells_y // BLOCK,),
        out_shape=(
            jax.ShapeDtypeStruct(current.shape, f32),
            jax.ShapeDtypeStruct(current.shape, f32),
            jax.ShapeDtypeStruct(lo.shape, f32),
            jax.ShapeDtypeStruct(lo.shape, f32),
        ),
        in_specs=[whole, field, whole_rim, whole_rim, field, fwd_spec, src_spec, field],
        out_specs=(field, field, rim, rim),
        scratch_shapes=[pltpu.VMEM((cells_y + 8, cells_x + 16, cells_z), f32)],
        input_output_aliases={7: 1},
        compiler_params=pltpu.CompilerParams(
            dimension_semantics=("arbitrary",), vmem_limit_bytes=48 * 1024 * 1024
        ),
    )(current, previous, lo, hi, speed_sq, forward, source, imaging)


def tile_kernel(moment, chained, tile_ref, cur_ref, prev_ref, halo_ref, vel_ref, fwd_ref, src_ref,
                img_ref, *rest):
    if chained:
        rest = rest[1:]
    next_ref, img_out_ref, edge_ref, pad_ref = rest
    cells_y, cells_x, cells_z = cur_ref.shape
    width = halo_ref.shape[1]
    part = cells_x // 2
    zeros = jnp.zeros((4, pad_ref.shape[1], cells_z), jnp.float32)
    pad_ref[0:4] = zeros
    pad_ref[4 + cells_y : 8 + cells_y] = zeros
    pad_ref[4 : 4 + cells_y, 8 : 8 + cells_x] = cur_ref[...]

    def compute(tile):
        if tile == 0:
            pad_ref[4 : 4 + cells_y, 8 - width : 8] = halo_ref[...]
        else:
            pad_ref[4 : 4 + cells_y, 8 + cells_x : 8 + cells_x + width] = halo_ref[...]
        start = 8 + tile * part

        def body(chunk, carry):
            y0 = chunk * SLAB_ROWS
            base = y0 + 4
            slab = pad_ref[pl.ds(base - 4, SLAB_ROWS + 8), start : start + part, :]

            def window(shift_y, shift_x):
                if shift_x == 0:
                    return slab[4 + shift_y : 4 + shift_y + SLAB_ROWS]
                return pad_ref[
                    pl.ds(base + shift_y, SLAB_ROWS), start + shift_x : start + shift_x + part, :
                ]

            center = window(0, 0)
            depth = lax.broadcasted_iota(jnp.int32, center.shape, 2)

            def along_z(reach):
                up = pltpu.roll(center, cells_z - reach, 2)
                down = pltpu.roll(center, reach, 2)
                return (
                    jnp.where(depth + reach < cells_z, up, 0.0),
                    jnp.where(depth - reach >= 0, down, 0.0),
                )

            summed = 3.0 * STENCIL[0] * center
            for reach in range(1, 5):
                z_up, z_down = along_z(reach)
                beside_all = (
                    window(reach, 0)
                    + window(-reach, 0)
                    + window(0, reach)
                    + window(0, -reach)
                    + z_up
                    + z_down
                )
                summed = summed + STENCIL[reach] * beside_all
            rows = pl.ds(y0, SLAB_ROWS)
            advanced = 2.0 * center - prev_ref[rows] + vel_ref[rows] * summed
            source = src_ref[rows, tile * part : (tile + 1) * part, pl.ds(moment, 1)]
            source = jnp.broadcast_to(source, advanced.shape)
            advanced = jnp.where(depth == 0, advanced + source, advanced)
            next_ref[rows] = advanced
            accel = fwd_ref[rows].astype(jnp.float32)[:, tile * part : (tile + 1) * part]
            img_out_ref[rows] = img_ref[rows] + accel * advanced
            if tile == 0:
                edge_ref[rows] = advanced[:, :width]
            else:
                edge_ref[rows] = advanced[:, part - width :]
            return carry

        lax.fori_loop(0, cells_y // SLAB_ROWS, body, 0, unroll=SLAB_UNROLL)

    for tile in range(2):
        pl.when(tile_ref[0] == tile)(functools.partial(compute, tile))


def tile_call(moment, tile, current, previous, halo_rim, speed_sq, forward, source, imaging, chain):
    cells_y, cells_x, cells_z = current.shape
    width = halo_rim.shape[1]
    part = cells_x // 2
    whole = pl.BlockSpec((cells_y, cells_x, cells_z), lambda i, t: (0, 0, 0))
    rim = pl.BlockSpec((cells_y, width, cells_z), lambda i, t: (0, 0, 0))
    half = pl.BlockSpec((cells_y, part, cells_z), lambda i, t: (0, t[0], 0))
    fwd_spec = pl.BlockSpec((None, cells_y, cells_x, cells_z), lambda i, t: (moment, 0, 0, 0))
    src_spec = pl.BlockSpec(source.shape, lambda i, t: (0, 0, 0))
    f32 = jnp.float32
    cells = cells_y * part * cells_z
    chained = chain is not None
    in_specs = [whole, half, rim, half, fwd_spec, src_spec, half]
    operands = [tile, current, previous, halo_rim, speed_sq, forward, source, imaging]
    aliases = {7: 1}
    if chained:
        in_specs.append(pl.BlockSpec(memory_space=pl.ANY))
        operands.append(chain)
        aliases[8] = 0
    return pl.pallas_call(
        functools.partial(tile_kernel, moment, chained),
        grid_spec=pltpu.PrefetchScalarGridSpec(
            num_scalar_prefetch=1,
            grid=(1,),
            in_specs=in_specs,
            out_specs=(half, half, rim),
            scratch_shapes=[pltpu.VMEM((cells_y + 8, cells_x + 16, cells_z), f32)],
        ),
        out_shape=(
            jax.ShapeDtypeStruct(current.shape, f32),
            jax.ShapeDtypeStruct(current.shape, f32),
            jax.ShapeDtypeStruct(halo_rim.shape, f32),
        ),
        input_output_aliases=aliases,
        cost_estimate=pl.CostEstimate(
            flops=60 * cells, bytes_accessed=28 * cells, transcendentals=0
        ),
        compiler_params=pltpu.CompilerParams(vmem_limit_bytes=48 * 1024 * 1024),
    )(*operands)


def exact_select(select, table, dimension_numbers):
    high = lax.reduce_precision(table, exponent_bits=8, mantissa_bits=7)
    rest = table - high
    middle = lax.reduce_precision(rest, exponent_bits=8, mantissa_bits=7)
    low = rest - middle
    select = select.astype(jnp.bfloat16)
    parts = [
        lax.dot_general(
            select, part.astype(jnp.bfloat16), dimension_numbers,
            preferred_element_type=jnp.float32,
        )
        for part in (high, middle, low)
    ]
    return (parts[0] + parts[1]) + parts[2]


def halo(first, last):
    axis = "space"
    devices = lax.axis_size(axis)
    even = lax.axis_index(axis) % 2 == 0
    within = [(i, i ^ 1) for i in range(devices)]
    across = [(i, i + 1 - 2 * ((i + 1) % 2)) for i in range(1, devices - 1)]
    got_within = lax.ppermute(jnp.where(even, last, first), axis, within)
    got_across = lax.ppermute(jnp.where(even, first, last), axis, across)
    lo = jnp.where(even, got_across, got_within)
    hi = jnp.where(even, got_within, got_across)
    return lo, hi


def local(
    residual,
    record_tile,
    record_cell,
    time_filter,
    offsets,
    velocity,
    adjoint_prev,
    adjoint_now,
    forward_accel,
):
    tiles_count = lax.axis_size("space")
    record_count = residual.shape[1]
    cells_y = velocity.shape[1]
    cells_x = velocity.shape[2]
    cells_z = velocity.shape[3]
    step_count = forward_accel.shape[1]
    slot_count = record_count * 3 // 16
    surface = cells_y * cells_x
    block_rows = (cells_y + cells_y // 4) // lax.axis_size("shot")
    trace_rows = residual[0]
    tile_ids = record_tile[0, :, 0]
    cell_ids = record_cell[0]
    record_order = jnp.arange(record_count, dtype=jnp.int32)
    same_before = (tile_ids[:, None] == tile_ids[None, :]) & (
        record_order[:, None] < record_order[None, :]
    )
    order_rank = jnp.sum(same_before.astype(jnp.int32), axis=0)
    slot_index = tile_ids * slot_count + order_rank
    filtered = jnp.dot(trace_rows, time_filter.T, preferred_element_type=jnp.float32)
    payload = jnp.concatenate(
        [filtered, (cell_ids + 1).astype(jnp.float32)[:, None]], axis=1
    )
    slots = tiles_count * slot_count
    placing = (
        slot_index[None, :] == jnp.arange(slots, dtype=jnp.int32)[:, None]
    ).astype(jnp.float32)
    buffer = exact_select(placing, payload, (((1,), (0,)), ((), ())))
    buffer = buffer.reshape(tiles_count, slot_count, step_count + 1)
    arrived = lax.all_to_all(buffer, "space", split_axis=0, concat_axis=0, tiled=True)
    arrived = arrived.reshape(slots, step_count + 1)
    cell_of = arrived[:, step_count].astype(jnp.int32)
    gathering = (
        cell_of[:, None] == jnp.arange(1, surface + 1, dtype=jnp.int32)[None, :]
    ).astype(jnp.float32)
    source = exact_select(gathering, arrived[:, :step_count], (((0,), (0,)), ((), ())))
    source = source.reshape(cells_y, cells_x, step_count)
    shift_rows = offsets[0]
    speed_sq = velocity[0]
    previous = adjoint_prev[0]
    current = adjoint_now[0]
    forward = forward_accel[0]
    imaging = jnp.zeros_like(current)
    width = 4
    odd = lax.axis_index("space") % 2
    tile_near = (1 - odd).reshape(1).astype(jnp.int32)
    tile_far = odd.reshape(1).astype(jnp.int32)
    devices = lax.axis_size("space")
    within = [(i, i ^ 1) for i in range(devices)]
    across = [(i, i + 1 - 2 * ((i + 1) % 2)) for i in range(1, devices - 1)]
    first = current[:, :width]
    last = current[:, cells_x - width :]
    even = odd == 0
    near_edge = jnp.where(even, last, first)
    far_edge = jnp.where(even, first, last)
    for moment in range(step_count):
        near_halo = lax.ppermute(near_edge, "space", within)
        far_halo = lax.ppermute(far_edge, "space", across)
        partial_next, imaging, near_edge = tile_call(
            moment, tile_near, current, previous, near_halo, speed_sq, forward, source,
            imaging, None,
        )
        advanced, imaging, far_edge = tile_call(
            moment, tile_far, current, previous, far_halo, speed_sq, forward, source,
            imaging, partial_next,
        )
        previous, current = (current, advanced)
    row_index = jnp.arange(lax.axis_size("shot") * block_rows, dtype=jnp.int32) - shift_rows
    inside = (row_index >= 0) & (row_index < cells_y)
    chosen = jnp.take(imaging, jnp.clip(row_index, 0, cells_y - 1), axis=0)
    placed = jnp.where(inside[:, None, None], chosen, 0.0)
    shots = lax.axis_size("shot")
    placed = placed.reshape((shots, block_rows) + placed.shape[1:])
    arrived = lax.all_to_all(placed, "shot", split_axis=0, concat_axis=0, tiled=True)
    gradient = jnp.sum(arrived, axis=0)
    return (gradient, current[None])


def solution(mesh):
    in_specs = (
        P("shot", "space", None),
        P("shot", "space", None),
        P("shot", "space"),
        P(),
        P("shot"),
        P("shot", None, "space", None),
        P("shot", None, "space", None),
        P("shot", None, "space", None),
        P("shot", None, None, "space", None),
    )
    out_specs = (P("shot", "space", None), P("shot", None, "space", None))
    return jax.shard_map(local, mesh=mesh, in_specs=in_specs, out_specs=out_specs, check_vma=False)
```

```python
import functools

import jax
import jax.numpy as jnp
from jax import lax
from jax.sharding import PartitionSpec as P
from jax.experimental import pallas as pl
from jax.experimental.pallas import tpu as pltpu

STENCIL = (-205.0 / 72.0, 8.0 / 5.0, -1.0 / 5.0, 8.0 / 315.0, -1.0 / 560.0)


def extended(shard, sides, width):
    for axis, dim in sides:
        devices, length = (lax.axis_size(axis), shard.shape[dim])
        up = [(i, (i + 1) % devices) for i in range(devices - 1)]
        down = [(j, i) for i, j in up]
        last = lax.slice_in_dim(shard, length - width, length, axis=dim)
        leading = lax.slice_in_dim(shard, 0, width, axis=dim)
        before = lax.ppermute(last, axis, up)
        after = lax.ppermute(leading, axis, down)
        shard = jnp.concatenate([before, shard, after], axis=dim)
    return shard


def laplace(padded):
    span_y = padded.shape[0] - 8
    span_x = padded.shape[1] - 8
    span_z = padded.shape[2] - 8

    def window(shift_y, shift_x, shift_z):
        return padded[
            4 + shift_y : 4 + shift_y + span_y,
            4 + shift_x : 4 + shift_x + span_x,
            4 + shift_z : 4 + shift_z + span_z,
        ]

    summed = 3.0 * STENCIL[0] * window(0, 0, 0)
    for reach in range(1, 5):
        beside_all = (
            window(reach, 0, 0)
            + window(-reach, 0, 0)
            + window(0, reach, 0)
            + window(0, -reach, 0)
            + window(0, 0, reach)
            + window(0, 0, -reach)
        )
        summed = summed + STENCIL[reach] * beside_all
    return summed


def pad_sides(field):
    return jnp.pad(field, ((4, 4), (0, 0), (4, 4)))


ROWS = 1
BLOCK = 8
SLAB_ROWS = 4
SLAB_UNROLL = 2


def step_kernel(moment, cur_ref, prev_ref, lo_ref, hi_ref, vel_ref, fwd_ref, src_ref, img_ref,
                next_ref, img_out_ref, first_ref, last_ref, pad_ref):
    cells_y, cells_x, cells_z = cur_ref.shape
    width = lo_ref.shape[1]
    block = pl.program_id(0)

    @pl.when(block == 0)
    def _():
        zeros = jnp.zeros((4, pad_ref.shape[1], cells_z), jnp.float32)
        pad_ref[0:4] = zeros
        pad_ref[4 + cells_y : 8 + cells_y] = zeros
        pad_ref[4 : 4 + cells_y, 8 - width : 8] = lo_ref[...]
        pad_ref[4 : 4 + cells_y, 8 : 8 + cells_x] = cur_ref[...]
        pad_ref[4 : 4 + cells_y, 8 + cells_x : 8 + cells_x + width] = hi_ref[...]

    def body(chunk, carry):
        y0 = pl.multiple_of(chunk * ROWS, ROWS)
        base = block * BLOCK + y0 + 4

        def window(shift_y, shift_x):
            return pad_ref[pl.ds(base + shift_y, ROWS), 8 + shift_x : 8 + shift_x + cells_x, :]

        center = window(0, 0)
        depth = lax.broadcasted_iota(jnp.int32, center.shape, 2)
        half = cells_z // 2
        low, high = center[..., :half], center[..., half:]
        lane = lax.broadcasted_iota(jnp.int32, low.shape, 2)

        def along_z(reach):
            low_up = pltpu.roll(low, half - reach, 2)
            high_up = pltpu.roll(high, half - reach, 2)
            low_down = pltpu.roll(low, reach, 2)
            high_down = pltpu.roll(high, reach, 2)
            head = lane < half - reach
            tail = lane >= reach
            up = jnp.concatenate(
                [jnp.where(head, low_up, high_up), jnp.where(head, high_up, 0.0)], axis=2
            )
            down = jnp.concatenate(
                [jnp.where(tail, low_down, 0.0), jnp.where(tail, high_down, low_down)], axis=2
            )
            return up, down

        summed = 3.0 * STENCIL[0] * center
        for reach in range(1, 5):
            z_up, z_down = along_z(reach)
            beside_all = (
                window(reach, 0)
                + window(-reach, 0)
                + window(0, reach)
                + window(0, -reach)
                + z_up
                + z_down
            )
            summed = summed + STENCIL[reach] * beside_all
        rows = pl.ds(y0, ROWS)
        advanced = 2.0 * center - prev_ref[rows] + vel_ref[rows] * summed
        source_rows = pl.ds(block * BLOCK + y0, ROWS)
        source = jnp.broadcast_to(src_ref[source_rows, :, pl.ds(moment, 1)], advanced.shape)
        advanced = jnp.where(depth == 0, advanced + source, advanced)
        next_ref[rows] = advanced
        img_out_ref[rows] = img_ref[rows] + fwd_ref[rows].astype(jnp.float32) * advanced
        first_ref[rows] = advanced[:, :width]
        last_ref[rows] = advanced[:, cells_x - width :]
        return carry

    lax.fori_loop(0, BLOCK // ROWS, body, 0, unroll=4)


def step_call(moment, current, previous, lo, hi, speed_sq, forward, source, imaging):
    cells_y, cells_x, cells_z = current.shape
    width = lo.shape[1]
    whole = pl.BlockSpec((cells_y, cells_x, cells_z), lambda i: (0, 0, 0))
    whole_rim = pl.BlockSpec((cells_y, width, cells_z), lambda i: (0, 0, 0))
    field = pl.BlockSpec((BLOCK, cells_x, cells_z), lambda i: (i, 0, 0))
    rim = pl.BlockSpec((BLOCK, width, cells_z), lambda i: (i, 0, 0))
    fwd_spec = pl.BlockSpec((None, BLOCK, cells_x, cells_z), lambda i: (moment, i, 0, 0))
    src_spec = pl.BlockSpec(source.shape, lambda i: (0, 0, 0))
    f32 = jnp.float32
    return pl.pallas_call(
        functools.partial(step_kernel, moment),
        grid=(cells_y // BLOCK,),
        out_shape=(
            jax.ShapeDtypeStruct(current.shape, f32),
            jax.ShapeDtypeStruct(current.shape, f32),
            jax.ShapeDtypeStruct(lo.shape, f32),
            jax.ShapeDtypeStruct(lo.shape, f32),
        ),
        in_specs=[whole, field, whole_rim, whole_rim, field, fwd_spec, src_spec, field],
        out_specs=(field, field, rim, rim),
        scratch_shapes=[pltpu.VMEM((cells_y + 8, cells_x + 16, cells_z), f32)],
        input_output_aliases={7: 1},
        compiler_params=pltpu.CompilerParams(
            dimension_semantics=("arbitrary",), vmem_limit_bytes=48 * 1024 * 1024
        ),
    )(current, previous, lo, hi, speed_sq, forward, source, imaging)


def tile_kernel(moment, chained, tile_ref, cur_ref, prev_ref, halo_ref, vel_ref, fwd_ref, src_ref,
                img_ref, *rest):
    if chained:
        rest = rest[1:]
    next_ref, img_out_ref, edge_ref, pad_ref = rest
    cells_y, cells_x, cells_z = cur_ref.shape
    width = halo_ref.shape[1]
    part = cells_x // 2
    zeros = jnp.zeros((4, pad_ref.shape[1], cells_z), jnp.float32)
    pad_ref[0:4] = zeros
    pad_ref[4 + cells_y : 8 + cells_y] = zeros
    pad_ref[4 : 4 + cells_y, 8 : 8 + cells_x] = cur_ref[...]

    def compute(tile):
        if tile == 0:
            pad_ref[4 : 4 + cells_y, 8 - width : 8] = halo_ref[...]
        else:
            pad_ref[4 : 4 + cells_y, 8 + cells_x : 8 + cells_x + width] = halo_ref[...]
        start = 8 + tile * part

        def body(chunk, carry):
            y0 = chunk * SLAB_ROWS
            base = y0 + 4
            slab = pad_ref[pl.ds(base - 4, SLAB_ROWS + 8), start : start + part, :]

            def window(shift_y, shift_x):
                if shift_x == 0:
                    return slab[4 + shift_y : 4 + shift_y + SLAB_ROWS]
                return pad_ref[
                    pl.ds(base + shift_y, SLAB_ROWS), start + shift_x : start + shift_x + part, :
                ]

            center = window(0, 0)
            depth = lax.broadcasted_iota(jnp.int32, center.shape, 2)

            def along_z(reach):
                up = pltpu.roll(center, cells_z - reach, 2)
                down = pltpu.roll(center, reach, 2)
                return (
                    jnp.where(depth + reach < cells_z, up, 0.0),
                    jnp.where(depth - reach >= 0, down, 0.0),
                )

            summed = 3.0 * STENCIL[0] * center
            for reach in range(1, 5):
                z_up, z_down = along_z(reach)
                beside_all = (
                    window(reach, 0)
                    + window(-reach, 0)
                    + window(0, reach)
                    + window(0, -reach)
                    + z_up
                    + z_down
                )
                summed = summed + STENCIL[reach] * beside_all
            rows = pl.ds(y0, SLAB_ROWS)
            advanced = 2.0 * center - prev_ref[rows] + vel_ref[rows] * summed
            source = src_ref[rows, tile * part : (tile + 1) * part, pl.ds(moment, 1)]
            source = jnp.broadcast_to(source, advanced.shape)
            advanced = jnp.where(depth == 0, advanced + source, advanced)
            next_ref[rows] = advanced
            accel = fwd_ref[rows].astype(jnp.float32)[:, tile * part : (tile + 1) * part]
            img_out_ref[rows] = img_ref[rows] + accel * advanced
            if tile == 0:
                edge_ref[rows] = advanced[:, :width]
            else:
                edge_ref[rows] = advanced[:, part - width :]
            return carry

        lax.fori_loop(0, cells_y // SLAB_ROWS, body, 0, unroll=SLAB_UNROLL)

    for tile in range(2):
        pl.when(tile_ref[0] == tile)(functools.partial(compute, tile))


def tile_call(moment, tile, current, previous, halo_rim, speed_sq, forward, source, imaging, chain):
    cells_y, cells_x, cells_z = current.shape
    width = halo_rim.shape[1]
    part = cells_x // 2
    whole = pl.BlockSpec((cells_y, cells_x, cells_z), lambda i, t: (0, 0, 0))
    rim = pl.BlockSpec((cells_y, width, cells_z), lambda i, t: (0, 0, 0))
    half = pl.BlockSpec((cells_y, part, cells_z), lambda i, t: (0, t[0], 0))
    fwd_spec = pl.BlockSpec((None, cells_y, cells_x, cells_z), lambda i, t: (moment, 0, 0, 0))
    src_spec = pl.BlockSpec(source.shape, lambda i, t: (0, 0, 0))
    f32 = jnp.float32
    cells = cells_y * part * cells_z
    chained = chain is not None
    in_specs = [whole, half, rim, half, fwd_spec, src_spec, half]
    operands = [tile, current, previous, halo_rim, speed_sq, forward, source, imaging]
    aliases = {7: 1}
    if chained:
        in_specs.append(pl.BlockSpec(memory_space=pl.ANY))
        operands.append(chain)
        aliases[8] = 0
    return pl.pallas_call(
        functools.partial(tile_kernel, moment, chained),
        grid_spec=pltpu.PrefetchScalarGridSpec(
            num_scalar_prefetch=1,
            grid=(1,),
            in_specs=in_specs,
            out_specs=(half, half, rim),
            scratch_shapes=[pltpu.VMEM((cells_y + 8, cells_x + 16, cells_z), f32)],
        ),
        out_shape=(
            jax.ShapeDtypeStruct(current.shape, f32),
            jax.ShapeDtypeStruct(current.shape, f32),
            jax.ShapeDtypeStruct(halo_rim.shape, f32),
        ),
        input_output_aliases=aliases,
        cost_estimate=pl.CostEstimate(
            flops=60 * cells, bytes_accessed=28 * cells, transcendentals=0
        ),
        compiler_params=pltpu.CompilerParams(vmem_limit_bytes=16 * 1024 * 1024),
    )(*operands)


def exact_select(select, table, dimension_numbers):
    high = lax.reduce_precision(table, exponent_bits=8, mantissa_bits=7)
    rest = table - high
    middle = lax.reduce_precision(rest, exponent_bits=8, mantissa_bits=7)
    low = rest - middle
    select = select.astype(jnp.bfloat16)
    parts = [
        lax.dot_general(
            select, part.astype(jnp.bfloat16), dimension_numbers,
            preferred_element_type=jnp.float32,
        )
        for part in (high, middle, low)
    ]
    return (parts[0] + parts[1]) + parts[2]


def halo(first, last):
    axis = "space"
    devices = lax.axis_size(axis)
    even = lax.axis_index(axis) % 2 == 0
    within = [(i, i ^ 1) for i in range(devices)]
    across = [(i, i + 1 - 2 * ((i + 1) % 2)) for i in range(1, devices - 1)]
    got_within = lax.ppermute(jnp.where(even, last, first), axis, within)
    got_across = lax.ppermute(jnp.where(even, first, last), axis, across)
    lo = jnp.where(even, got_across, got_within)
    hi = jnp.where(even, got_within, got_across)
    return lo, hi


def local(
    residual,
    record_tile,
    record_cell,
    time_filter,
    offsets,
    velocity,
    adjoint_prev,
    adjoint_now,
    forward_accel,
):
    tiles_count = lax.axis_size("space")
    record_count = residual.shape[1]
    cells_y = velocity.shape[1]
    cells_x = velocity.shape[2]
    cells_z = velocity.shape[3]
    step_count = forward_accel.shape[1]
    slot_count = record_count * 3 // 16
    surface = cells_y * cells_x
    block_rows = (cells_y + cells_y // 4) // lax.axis_size("shot")
    trace_rows = residual[0]
    tile_ids = record_tile[0, :, 0]
    cell_ids = record_cell[0]
    record_order = jnp.arange(record_count, dtype=jnp.int32)
    same_before = (tile_ids[:, None] == tile_ids[None, :]) & (
        record_order[:, None] < record_order[None, :]
    )
    order_rank = jnp.sum(same_before.astype(jnp.int32), axis=0)
    slot_index = tile_ids * slot_count + order_rank
    filtered = jnp.dot(trace_rows, time_filter.T, preferred_element_type=jnp.float32)
    payload = jnp.concatenate(
        [filtered, (cell_ids + 1).astype(jnp.float32)[:, None]], axis=1
    )
    slots = tiles_count * slot_count
    placing = (
        slot_index[None, :] == jnp.arange(slots, dtype=jnp.int32)[:, None]
    ).astype(jnp.float32)
    buffer = exact_select(placing, payload, (((1,), (0,)), ((), ())))
    buffer = buffer.reshape(tiles_count, slot_count, step_count + 1)
    arrived = lax.all_to_all(buffer, "space", split_axis=0, concat_axis=0, tiled=True)
    arrived = arrived.reshape(slots, step_count + 1)
    cell_of = arrived[:, step_count].astype(jnp.int32)
    gathering = (
        cell_of[:, None] == jnp.arange(1, surface + 1, dtype=jnp.int32)[None, :]
    ).astype(jnp.float32)
    source = exact_select(gathering, arrived[:, :step_count], (((0,), (0,)), ((), ())))
    source = source.reshape(cells_y, cells_x, step_count)
    shift_rows = offsets[0]
    speed_sq = velocity[0]
    previous = adjoint_prev[0]
    current = adjoint_now[0]
    forward = forward_accel[0]
    imaging = jnp.zeros_like(current)
    width = 4
    odd = lax.axis_index("space") % 2
    tile_near = (1 - odd).reshape(1).astype(jnp.int32)
    tile_far = odd.reshape(1).astype(jnp.int32)
    devices = lax.axis_size("space")
    within = [(i, i ^ 1) for i in range(devices)]
    across = [(i, i + 1 - 2 * ((i + 1) % 2)) for i in range(1, devices - 1)]
    zero = jnp.zeros((), jnp.int32)
    near_start = (1 - odd) * (cells_x - width)
    near_edge = lax.dynamic_slice(current, (zero, near_start, zero), (cells_y, width, cells_z))
    far_start = odd * (cells_x - width)
    far_edge = lax.dynamic_slice(current, (zero, far_start, zero), (cells_y, width, cells_z))
    for moment in range(step_count):
        near_halo = lax.ppermute(near_edge, "space", within)
        far_halo = lax.ppermute(far_edge, "space", across)
        partial_next, imaging, near_edge = tile_call(
            moment, tile_near, current, previous, near_halo, speed_sq, forward, source,
            imaging, None,
        )
        advanced, imaging, far_edge = tile_call(
            moment, tile_far, current, previous, far_halo, speed_sq, forward, source,
            imaging, partial_next,
        )
        previous, current = (current, advanced)
    row_index = jnp.arange(lax.axis_size("shot") * block_rows, dtype=jnp.int32) - shift_rows
    inside = (row_index >= 0) & (row_index < cells_y)
    chosen = jnp.take(imaging, jnp.clip(row_index, 0, cells_y - 1), axis=0)
    placed = jnp.where(inside[:, None, None], chosen, 0.0)
    shots = lax.axis_size("shot")
    placed = placed.reshape((shots, block_rows) + placed.shape[1:])
    arrived = lax.all_to_all(placed, "shot", split_axis=0, concat_axis=0, tiled=True)
    gradient = jnp.sum(arrived, axis=0)
    return (gradient, current[None])


def solution(mesh):
    in_specs = (
        P("shot", "space", None),
        P("shot", "space", None),
        P("shot", "space"),
        P(),
        P("shot"),
        P("shot", None, "space", None),
        P("shot", None, "space", None),
        P("shot", None, "space", None),
        P("shot", None, None, "space", None),
    )
    out_specs = (P("shot", "space", None), P("shot", None, "space", None))
    return jax.shard_map(local, mesh=mesh, in_specs=in_specs, out_specs=out_specs, check_vma=False)
```

```python
import functools

import jax
import jax.numpy as jnp
from jax import lax
from jax.sharding import PartitionSpec as P
from jax.experimental import pallas as pl
from jax.experimental.pallas import tpu as pltpu

STENCIL = (-205.0 / 72.0, 8.0 / 5.0, -1.0 / 5.0, 8.0 / 315.0, -1.0 / 560.0)


def extended(shard, sides, width):
    for axis, dim in sides:
        devices, length = (lax.axis_size(axis), shard.shape[dim])
        up = [(i, (i + 1) % devices) for i in range(devices - 1)]
        down = [(j, i) for i, j in up]
        last = lax.slice_in_dim(shard, length - width, length, axis=dim)
        leading = lax.slice_in_dim(shard, 0, width, axis=dim)
        before = lax.ppermute(last, axis, up)
        after = lax.ppermute(leading, axis, down)
        shard = jnp.concatenate([before, shard, after], axis=dim)
    return shard


def laplace(padded):
    span_y = padded.shape[0] - 8
    span_x = padded.shape[1] - 8
    span_z = padded.shape[2] - 8

    def window(shift_y, shift_x, shift_z):
        return padded[
            4 + shift_y : 4 + shift_y + span_y,
            4 + shift_x : 4 + shift_x + span_x,
            4 + shift_z : 4 + shift_z + span_z,
        ]

    summed = 3.0 * STENCIL[0] * window(0, 0, 0)
    for reach in range(1, 5):
        beside_all = (
            window(reach, 0, 0)
            + window(-reach, 0, 0)
            + window(0, reach, 0)
            + window(0, -reach, 0)
            + window(0, 0, reach)
            + window(0, 0, -reach)
        )
        summed = summed + STENCIL[reach] * beside_all
    return summed


def pad_sides(field):
    return jnp.pad(field, ((4, 4), (0, 0), (4, 4)))


ROWS = 1
BLOCK = 8
SLAB_ROWS = 4
SLAB_UNROLL = 2


def step_kernel(moment, cur_ref, prev_ref, lo_ref, hi_ref, vel_ref, fwd_ref, src_ref, img_ref,
                next_ref, img_out_ref, first_ref, last_ref, pad_ref):
    cells_y, cells_x, cells_z = cur_ref.shape
    width = lo_ref.shape[1]
    block = pl.program_id(0)

    @pl.when(block == 0)
    def _():
        zeros = jnp.zeros((4, pad_ref.shape[1], cells_z), jnp.float32)
        pad_ref[0:4] = zeros
        pad_ref[4 + cells_y : 8 + cells_y] = zeros
        pad_ref[4 : 4 + cells_y, 8 - width : 8] = lo_ref[...]
        pad_ref[4 : 4 + cells_y, 8 : 8 + cells_x] = cur_ref[...]
        pad_ref[4 : 4 + cells_y, 8 + cells_x : 8 + cells_x + width] = hi_ref[...]

    def body(chunk, carry):
        y0 = pl.multiple_of(chunk * ROWS, ROWS)
        base = block * BLOCK + y0 + 4

        def window(shift_y, shift_x):
            return pad_ref[pl.ds(base + shift_y, ROWS), 8 + shift_x : 8 + shift_x + cells_x, :]

        center = window(0, 0)
        depth = lax.broadcasted_iota(jnp.int32, center.shape, 2)
        half = cells_z // 2
        low, high = center[..., :half], center[..., half:]
        lane = lax.broadcasted_iota(jnp.int32, low.shape, 2)

        def along_z(reach):
            low_up = pltpu.roll(low, half - reach, 2)
            high_up = pltpu.roll(high, half - reach, 2)
            low_down = pltpu.roll(low, reach, 2)
            high_down = pltpu.roll(high, reach, 2)
            head = lane < half - reach
            tail = lane >= reach
            up = jnp.concatenate(
                [jnp.where(head, low_up, high_up), jnp.where(head, high_up, 0.0)], axis=2
            )
            down = jnp.concatenate(
                [jnp.where(tail, low_down, 0.0), jnp.where(tail, high_down, low_down)], axis=2
            )
            return up, down

        summed = 3.0 * STENCIL[0] * center
        for reach in range(1, 5):
            z_up, z_down = along_z(reach)
            beside_all = (
                window(reach, 0)
                + window(-reach, 0)
                + window(0, reach)
                + window(0, -reach)
                + z_up
                + z_down
            )
            summed = summed + STENCIL[reach] * beside_all
        rows = pl.ds(y0, ROWS)
        advanced = 2.0 * center - prev_ref[rows] + vel_ref[rows] * summed
        source_rows = pl.ds(block * BLOCK + y0, ROWS)
        source = jnp.broadcast_to(src_ref[source_rows, :, pl.ds(moment, 1)], advanced.shape)
        advanced = jnp.where(depth == 0, advanced + source, advanced)
        next_ref[rows] = advanced
        img_out_ref[rows] = img_ref[rows] + fwd_ref[rows].astype(jnp.float32) * advanced
        first_ref[rows] = advanced[:, :width]
        last_ref[rows] = advanced[:, cells_x - width :]
        return carry

    lax.fori_loop(0, BLOCK // ROWS, body, 0, unroll=4)


def step_call(moment, current, previous, lo, hi, speed_sq, forward, source, imaging):
    cells_y, cells_x, cells_z = current.shape
    width = lo.shape[1]
    whole = pl.BlockSpec((cells_y, cells_x, cells_z), lambda i: (0, 0, 0))
    whole_rim = pl.BlockSpec((cells_y, width, cells_z), lambda i: (0, 0, 0))
    field = pl.BlockSpec((BLOCK, cells_x, cells_z), lambda i: (i, 0, 0))
    rim = pl.BlockSpec((BLOCK, width, cells_z), lambda i: (i, 0, 0))
    fwd_spec = pl.BlockSpec((None, BLOCK, cells_x, cells_z), lambda i: (moment, i, 0, 0))
    src_spec = pl.BlockSpec(source.shape, lambda i: (0, 0, 0))
    f32 = jnp.float32
    return pl.pallas_call(
        functools.partial(step_kernel, moment),
        grid=(cells_y // BLOCK,),
        out_shape=(
            jax.ShapeDtypeStruct(current.shape, f32),
            jax.ShapeDtypeStruct(current.shape, f32),
            jax.ShapeDtypeStruct(lo.shape, f32),
            jax.ShapeDtypeStruct(lo.shape, f32),
        ),
        in_specs=[whole, field, whole_rim, whole_rim, field, fwd_spec, src_spec, field],
        out_specs=(field, field, rim, rim),
        scratch_shapes=[pltpu.VMEM((cells_y + 8, cells_x + 16, cells_z), f32)],
        input_output_aliases={7: 1},
        compiler_params=pltpu.CompilerParams(
            dimension_semantics=("arbitrary",), vmem_limit_bytes=48 * 1024 * 1024
        ),
    )(current, previous, lo, hi, speed_sq, forward, source, imaging)


def tile_kernel(moment, chained, tile_ref, cur_ref, prev_ref, halo_ref, vel_ref, fwd_ref, src_ref,
                img_ref, *rest):
    if chained:
        rest = rest[1:]
    next_ref, img_out_ref, edge_ref, pad_ref = rest
    cells_y, cells_x, cells_z = cur_ref.shape
    width = halo_ref.shape[1]
    part = cells_x // 2
    zeros = jnp.zeros((4, pad_ref.shape[1], cells_z), jnp.float32)
    pad_ref[0:4] = zeros
    pad_ref[4 + cells_y : 8 + cells_y] = zeros
    pad_ref[4 : 4 + cells_y, 8 : 8 + cells_x] = cur_ref[...]

    def compute(tile):
        if tile == 0:
            pad_ref[4 : 4 + cells_y, 8 - width : 8] = halo_ref[...]
        else:
            pad_ref[4 : 4 + cells_y, 8 + cells_x : 8 + cells_x + width] = halo_ref[...]
        start = 8 + tile * part

        def body(chunk, carry):
            y0 = chunk * SLAB_ROWS
            base = y0 + 4
            slab = pad_ref[pl.ds(base - 4, SLAB_ROWS + 8), start : start + part, :]

            def window(shift_y, shift_x):
                if shift_x == 0:
                    return slab[4 + shift_y : 4 + shift_y + SLAB_ROWS]
                return pad_ref[
                    pl.ds(base + shift_y, SLAB_ROWS), start + shift_x : start + shift_x + part, :
                ]

            center = window(0, 0)
            depth = lax.broadcasted_iota(jnp.int32, center.shape, 2)

            def along_z(reach):
                up = pltpu.roll(center, cells_z - reach, 2)
                down = pltpu.roll(center, reach, 2)
                return (
                    jnp.where(depth + reach < cells_z, up, 0.0),
                    jnp.where(depth - reach >= 0, down, 0.0),
                )

            summed = 3.0 * STENCIL[0] * center
            for reach in range(1, 5):
                z_up, z_down = along_z(reach)
                beside_all = (
                    window(reach, 0)
                    + window(-reach, 0)
                    + window(0, reach)
                    + window(0, -reach)
                    + z_up
                    + z_down
                )
                summed = summed + STENCIL[reach] * beside_all
            rows = pl.ds(y0, SLAB_ROWS)
            advanced = 2.0 * center - prev_ref[rows] + vel_ref[rows] * summed
            source = src_ref[rows, tile * part : (tile + 1) * part, pl.ds(moment, 1)]
            source = jnp.broadcast_to(source, advanced.shape)
            advanced = jnp.where(depth == 0, advanced + source, advanced)
            next_ref[rows] = advanced
            accel = fwd_ref[rows].astype(jnp.float32)[:, tile * part : (tile + 1) * part]
            img_out_ref[rows] = img_ref[rows] + accel * advanced
            if tile == 0:
                edge_ref[rows] = advanced[:, :width]
            else:
                edge_ref[rows] = advanced[:, part - width :]
            return carry

        lax.fori_loop(0, cells_y // SLAB_ROWS, body, 0, unroll=SLAB_UNROLL)

    for tile in range(2):
        pl.when(tile_ref[0] == tile)(functools.partial(compute, tile))


def tile_call(moment, tile, current, previous, halo_rim, speed_sq, forward, source, imaging, chain):
    cells_y, cells_x, cells_z = current.shape
    width = halo_rim.shape[1]
    part = cells_x // 2
    whole = pl.BlockSpec((cells_y, cells_x, cells_z), lambda i, t: (0, 0, 0))
    rim = pl.BlockSpec((cells_y, width, cells_z), lambda i, t: (0, 0, 0))
    half = pl.BlockSpec((cells_y, part, cells_z), lambda i, t: (0, t[0], 0))
    fwd_spec = pl.BlockSpec((None, cells_y, cells_x, cells_z), lambda i, t: (moment, 0, 0, 0))
    src_spec = pl.BlockSpec(source.shape, lambda i, t: (0, 0, 0))
    f32 = jnp.float32
    cells = cells_y * part * cells_z
    chained = chain is not None
    in_specs = [whole, half, rim, half, fwd_spec, src_spec, half]
    operands = [tile, current, previous, halo_rim, speed_sq, forward, source, imaging]
    aliases = {7: 1}
    if chained:
        in_specs.append(pl.BlockSpec(memory_space=pl.ANY))
        operands.append(chain)
        aliases[8] = 0
    return pl.pallas_call(
        functools.partial(tile_kernel, moment, chained),
        grid_spec=pltpu.PrefetchScalarGridSpec(
            num_scalar_prefetch=1,
            grid=(1,),
            in_specs=in_specs,
            out_specs=(half, half, rim),
            scratch_shapes=[pltpu.VMEM((cells_y + 8, cells_x + 16, cells_z), f32)],
        ),
        out_shape=(
            jax.ShapeDtypeStruct(current.shape, f32),
            jax.ShapeDtypeStruct(current.shape, f32),
            jax.ShapeDtypeStruct(halo_rim.shape, f32),
        ),
        input_output_aliases=aliases,
        cost_estimate=pl.CostEstimate(
            flops=60 * cells, bytes_accessed=28 * cells, transcendentals=0
        ),
        compiler_params=pltpu.CompilerParams(vmem_limit_bytes=12 * 1024 * 1024),
    )(*operands)


def exact_select(select, table, dimension_numbers):
    high = lax.reduce_precision(table, exponent_bits=8, mantissa_bits=7)
    rest = table - high
    middle = lax.reduce_precision(rest, exponent_bits=8, mantissa_bits=7)
    low = rest - middle
    select = select.astype(jnp.bfloat16)
    parts = [
        lax.dot_general(
            select, part.astype(jnp.bfloat16), dimension_numbers,
            preferred_element_type=jnp.float32,
        )
        for part in (high, middle, low)
    ]
    return (parts[0] + parts[1]) + parts[2]


def halo(first, last):
    axis = "space"
    devices = lax.axis_size(axis)
    even = lax.axis_index(axis) % 2 == 0
    within = [(i, i ^ 1) for i in range(devices)]
    across = [(i, i + 1 - 2 * ((i + 1) % 2)) for i in range(1, devices - 1)]
    got_within = lax.ppermute(jnp.where(even, last, first), axis, within)
    got_across = lax.ppermute(jnp.where(even, first, last), axis, across)
    lo = jnp.where(even, got_across, got_within)
    hi = jnp.where(even, got_within, got_across)
    return lo, hi


def local(
    residual,
    record_tile,
    record_cell,
    time_filter,
    offsets,
    velocity,
    adjoint_prev,
    adjoint_now,
    forward_accel,
):
    tiles_count = lax.axis_size("space")
    record_count = residual.shape[1]
    cells_y = velocity.shape[1]
    cells_x = velocity.shape[2]
    cells_z = velocity.shape[3]
    step_count = forward_accel.shape[1]
    slot_count = record_count * 3 // 16
    surface = cells_y * cells_x
    block_rows = (cells_y + cells_y // 4) // lax.axis_size("shot")
    trace_rows = residual[0]
    tile_ids = record_tile[0, :, 0]
    cell_ids = record_cell[0]
    record_order = jnp.arange(record_count, dtype=jnp.int32)
    same_before = (tile_ids[:, None] == tile_ids[None, :]) & (
        record_order[:, None] < record_order[None, :]
    )
    order_rank = jnp.sum(same_before.astype(jnp.int32), axis=0)
    slot_index = tile_ids * slot_count + order_rank
    filtered = jnp.dot(trace_rows, time_filter.T, preferred_element_type=jnp.float32)
    payload = jnp.concatenate(
        [filtered, (cell_ids + 1).astype(jnp.float32)[:, None]], axis=1
    )
    slots = tiles_count * slot_count
    placing = (
        slot_index[None, :] == jnp.arange(slots, dtype=jnp.int32)[:, None]
    ).astype(jnp.float32)
    buffer = exact_select(placing, payload, (((1,), (0,)), ((), ())))
    buffer = buffer.reshape(tiles_count, slot_count, step_count + 1)
    arrived = lax.all_to_all(buffer, "space", split_axis=0, concat_axis=0, tiled=True)
    arrived = arrived.reshape(slots, step_count + 1)
    cell_of = arrived[:, step_count].astype(jnp.int32)
    gathering = (
        cell_of[:, None] == jnp.arange(1, surface + 1, dtype=jnp.int32)[None, :]
    ).astype(jnp.float32)
    source = exact_select(gathering, arrived[:, :step_count], (((0,), (0,)), ((), ())))
    source = source.reshape(cells_y, cells_x, step_count)
    shift_rows = offsets[0]
    speed_sq = velocity[0]
    previous = adjoint_prev[0]
    current = adjoint_now[0]
    forward = forward_accel[0]
    imaging = jnp.zeros_like(current)
    width = 4
    odd = lax.axis_index("space") % 2
    tile_near = (1 - odd).reshape(1).astype(jnp.int32)
    tile_far = odd.reshape(1).astype(jnp.int32)
    devices = lax.axis_size("space")
    within = [(i, i ^ 1) for i in range(devices)]
    across = [(i, i + 1 - 2 * ((i + 1) % 2)) for i in range(1, devices - 1)]
    zero = jnp.zeros((), jnp.int32)
    near_start = (1 - odd) * (cells_x - width)
    near_edge = lax.dynamic_slice(current, (zero, near_start, zero), (cells_y, width, cells_z))
    far_start = odd * (cells_x - width)
    far_edge = lax.dynamic_slice(current, (zero, far_start, zero), (cells_y, width, cells_z))
    for moment in range(step_count):
        near_halo = lax.ppermute(near_edge, "space", within)
        far_halo = lax.ppermute(far_edge, "space", across)
        partial_next, imaging, near_edge = tile_call(
            moment, tile_near, current, previous, near_halo, speed_sq, forward, source,
            imaging, None,
        )
        advanced, imaging, far_edge = tile_call(
            moment, tile_far, current, previous, far_halo, speed_sq, forward, source,
            imaging, partial_next,
        )
        previous, current = (current, advanced)
    row_index = jnp.arange(lax.axis_size("shot") * block_rows, dtype=jnp.int32) - shift_rows
    inside = (row_index >= 0) & (row_index < cells_y)
    chosen = jnp.take(imaging, jnp.clip(row_index, 0, cells_y - 1), axis=0)
    placed = jnp.where(inside[:, None, None], chosen, 0.0)
    shots = lax.axis_size("shot")
    placed = placed.reshape((shots, block_rows) + placed.shape[1:])
    arrived = lax.all_to_all(placed, "shot", split_axis=0, concat_axis=0, tiled=True)
    gradient = jnp.sum(arrived, axis=0)
    return (gradient, current[None])


def solution(mesh):
    in_specs = (
        P("shot", "space", None),
        P("shot", "space", None),
        P("shot", "space"),
        P(),
        P("shot"),
        P("shot", None, "space", None),
        P("shot", None, "space", None),
        P("shot", None, "space", None),
        P("shot", None, None, "space", None),
    )
    out_specs = (P("shot", "space", None), P("shot", None, "space", None))
    return jax.shard_map(local, mesh=mesh, in_specs=in_specs, out_specs=out_specs, check_vma=False)
```

```python
import functools

import jax
import jax.numpy as jnp
from jax import lax
from jax.sharding import PartitionSpec as P
from jax.experimental import pallas as pl
from jax.experimental.pallas import tpu as pltpu

STENCIL = (-205.0 / 72.0, 8.0 / 5.0, -1.0 / 5.0, 8.0 / 315.0, -1.0 / 560.0)


def extended(shard, sides, width):
    for axis, dim in sides:
        devices, length = (lax.axis_size(axis), shard.shape[dim])
        up = [(i, (i + 1) % devices) for i in range(devices - 1)]
        down = [(j, i) for i, j in up]
        last = lax.slice_in_dim(shard, length - width, length, axis=dim)
        leading = lax.slice_in_dim(shard, 0, width, axis=dim)
        before = lax.ppermute(last, axis, up)
        after = lax.ppermute(leading, axis, down)
        shard = jnp.concatenate([before, shard, after], axis=dim)
    return shard


def laplace(padded):
    span_y = padded.shape[0] - 8
    span_x = padded.shape[1] - 8
    span_z = padded.shape[2] - 8

    def window(shift_y, shift_x, shift_z):
        return padded[
            4 + shift_y : 4 + shift_y + span_y,
            4 + shift_x : 4 + shift_x + span_x,
            4 + shift_z : 4 + shift_z + span_z,
        ]

    summed = 3.0 * STENCIL[0] * window(0, 0, 0)
    for reach in range(1, 5):
        beside_all = (
            window(reach, 0, 0)
            + window(-reach, 0, 0)
            + window(0, reach, 0)
            + window(0, -reach, 0)
            + window(0, 0, reach)
            + window(0, 0, -reach)
        )
        summed = summed + STENCIL[reach] * beside_all
    return summed


def pad_sides(field):
    return jnp.pad(field, ((4, 4), (0, 0), (4, 4)))


ROWS = 1
BLOCK = 8
SLAB_ROWS = 4
SLAB_UNROLL = 2


def step_kernel(moment, cur_ref, prev_ref, lo_ref, hi_ref, vel_ref, fwd_ref, src_ref, img_ref,
                next_ref, img_out_ref, first_ref, last_ref, pad_ref):
    cells_y, cells_x, cells_z = cur_ref.shape
    width = lo_ref.shape[1]
    block = pl.program_id(0)

    @pl.when(block == 0)
    def _():
        zeros = jnp.zeros((4, pad_ref.shape[1], cells_z), jnp.float32)
        pad_ref[0:4] = zeros
        pad_ref[4 + cells_y : 8 + cells_y] = zeros
        pad_ref[4 : 4 + cells_y, 8 - width : 8] = lo_ref[...]
        pad_ref[4 : 4 + cells_y, 8 : 8 + cells_x] = cur_ref[...]
        pad_ref[4 : 4 + cells_y, 8 + cells_x : 8 + cells_x + width] = hi_ref[...]

    def body(chunk, carry):
        y0 = pl.multiple_of(chunk * ROWS, ROWS)
        base = block * BLOCK + y0 + 4

        def window(shift_y, shift_x):
            return pad_ref[pl.ds(base + shift_y, ROWS), 8 + shift_x : 8 + shift_x + cells_x, :]

        center = window(0, 0)
        depth = lax.broadcasted_iota(jnp.int32, center.shape, 2)
        half = cells_z // 2
        low, high = center[..., :half], center[..., half:]
        lane = lax.broadcasted_iota(jnp.int32, low.shape, 2)

        def along_z(reach):
            low_up = pltpu.roll(low, half - reach, 2)
            high_up = pltpu.roll(high, half - reach, 2)
            low_down = pltpu.roll(low, reach, 2)
            high_down = pltpu.roll(high, reach, 2)
            head = lane < half - reach
            tail = lane >= reach
            up = jnp.concatenate(
                [jnp.where(head, low_up, high_up), jnp.where(head, high_up, 0.0)], axis=2
            )
            down = jnp.concatenate(
                [jnp.where(tail, low_down, 0.0), jnp.where(tail, high_down, low_down)], axis=2
            )
            return up, down

        summed = 3.0 * STENCIL[0] * center
        for reach in range(1, 5):
            z_up, z_down = along_z(reach)
            beside_all = (
                window(reach, 0)
                + window(-reach, 0)
                + window(0, reach)
                + window(0, -reach)
                + z_up
                + z_down
            )
            summed = summed + STENCIL[reach] * beside_all
        rows = pl.ds(y0, ROWS)
        advanced = 2.0 * center - prev_ref[rows] + vel_ref[rows] * summed
        source_rows = pl.ds(block * BLOCK + y0, ROWS)
        source = jnp.broadcast_to(src_ref[source_rows, :, pl.ds(moment, 1)], advanced.shape)
        advanced = jnp.where(depth == 0, advanced + source, advanced)
        next_ref[rows] = advanced
        img_out_ref[rows] = img_ref[rows] + fwd_ref[rows].astype(jnp.float32) * advanced
        first_ref[rows] = advanced[:, :width]
        last_ref[rows] = advanced[:, cells_x - width :]
        return carry

    lax.fori_loop(0, BLOCK // ROWS, body, 0, unroll=4)


def step_call(moment, current, previous, lo, hi, speed_sq, forward, source, imaging):
    cells_y, cells_x, cells_z = current.shape
    width = lo.shape[1]
    whole = pl.BlockSpec((cells_y, cells_x, cells_z), lambda i: (0, 0, 0))
    whole_rim = pl.BlockSpec((cells_y, width, cells_z), lambda i: (0, 0, 0))
    field = pl.BlockSpec((BLOCK, cells_x, cells_z), lambda i: (i, 0, 0))
    rim = pl.BlockSpec((BLOCK, width, cells_z), lambda i: (i, 0, 0))
    fwd_spec = pl.BlockSpec((None, BLOCK, cells_x, cells_z), lambda i: (moment, i, 0, 0))
    src_spec = pl.BlockSpec(source.shape, lambda i: (0, 0, 0))
    f32 = jnp.float32
    return pl.pallas_call(
        functools.partial(step_kernel, moment),
        grid=(cells_y // BLOCK,),
        out_shape=(
            jax.ShapeDtypeStruct(current.shape, f32),
            jax.ShapeDtypeStruct(current.shape, f32),
            jax.ShapeDtypeStruct(lo.shape, f32),
            jax.ShapeDtypeStruct(lo.shape, f32),
        ),
        in_specs=[whole, field, whole_rim, whole_rim, field, fwd_spec, src_spec, field],
        out_specs=(field, field, rim, rim),
        scratch_shapes=[pltpu.VMEM((cells_y + 8, cells_x + 16, cells_z), f32)],
        input_output_aliases={7: 1},
        compiler_params=pltpu.CompilerParams(
            dimension_semantics=("arbitrary",), vmem_limit_bytes=48 * 1024 * 1024
        ),
    )(current, previous, lo, hi, speed_sq, forward, source, imaging)


def tile_kernel(moment, chained, tile_ref, cur_ref, prev_ref, halo_ref, vel_ref, fwd_ref, src_ref,
                img_ref, *rest):
    if chained:
        rest = rest[1:]
    next_ref, img_out_ref, edge_ref, pad_ref = rest
    cells_y, cells_x, cells_z = cur_ref.shape
    width = halo_ref.shape[1]
    part = cells_x // 2
    zeros = jnp.zeros((4, pad_ref.shape[1], cells_z), jnp.float32)
    pad_ref[0:4] = zeros
    pad_ref[4 + cells_y : 8 + cells_y] = zeros
    pad_ref[4 : 4 + cells_y, 8 : 8 + cells_x] = cur_ref[...]

    def compute(tile):
        if tile == 0:
            pad_ref[4 : 4 + cells_y, 8 - width : 8] = halo_ref[...]
        else:
            pad_ref[4 : 4 + cells_y, 8 + cells_x : 8 + cells_x + width] = halo_ref[...]
        start = 8 + tile * part

        def body(chunk, carry):
            y0 = chunk * SLAB_ROWS
            base = y0 + 4
            slab = pad_ref[pl.ds(base - 4, SLAB_ROWS + 8), start : start + part, :]

            def window(shift_y, shift_x):
                if shift_x == 0:
                    return slab[4 + shift_y : 4 + shift_y + SLAB_ROWS]
                return pad_ref[
                    pl.ds(base + shift_y, SLAB_ROWS), start + shift_x : start + shift_x + part, :
                ]

            center = window(0, 0)
            depth = lax.broadcasted_iota(jnp.int32, center.shape, 2)

            def along_z(reach):
                up = pltpu.roll(center, cells_z - reach, 2)
                down = pltpu.roll(center, reach, 2)
                return (
                    jnp.where(depth + reach < cells_z, up, 0.0),
                    jnp.where(depth - reach >= 0, down, 0.0),
                )

            summed = 3.0 * STENCIL[0] * center
            for reach in range(1, 5):
                z_up, z_down = along_z(reach)
                beside_all = (
                    window(reach, 0)
                    + window(-reach, 0)
                    + window(0, reach)
                    + window(0, -reach)
                    + z_up
                    + z_down
                )
                summed = summed + STENCIL[reach] * beside_all
            rows = pl.ds(y0, SLAB_ROWS)
            advanced = 2.0 * center - prev_ref[rows] + vel_ref[rows] * summed
            source = src_ref[rows, tile * part : (tile + 1) * part, pl.ds(moment, 1)]
            source = jnp.broadcast_to(source, advanced.shape)
            advanced = jnp.where(depth == 0, advanced + source, advanced)
            next_ref[rows] = advanced
            accel = fwd_ref[rows].astype(jnp.float32)[:, tile * part : (tile + 1) * part]
            img_out_ref[rows] = img_ref[rows] + accel * advanced
            if tile == 0:
                edge_ref[rows] = advanced[:, :width]
            else:
                edge_ref[rows] = advanced[:, part - width :]
            return carry

        lax.fori_loop(0, cells_y // SLAB_ROWS, body, 0, unroll=SLAB_UNROLL)

    for tile in range(2):
        pl.when(tile_ref[0] == tile)(functools.partial(compute, tile))


def tile_call(moment, tile, current, previous, halo_rim, speed_sq, forward, source, imaging, chain):
    cells_y, cells_x, cells_z = current.shape
    width = halo_rim.shape[1]
    part = cells_x // 2
    whole = pl.BlockSpec((cells_y, cells_x, cells_z), lambda i, t: (0, 0, 0))
    rim = pl.BlockSpec((cells_y, width, cells_z), lambda i, t: (0, 0, 0))
    half = pl.BlockSpec((cells_y, part, cells_z), lambda i, t: (0, t[0], 0))
    fwd_spec = pl.BlockSpec((None, cells_y, cells_x, cells_z), lambda i, t: (moment, 0, 0, 0))
    src_spec = pl.BlockSpec(source.shape, lambda i, t: (0, 0, 0))
    f32 = jnp.float32
    cells = cells_y * part * cells_z
    chained = chain is not None
    in_specs = [whole, half, rim, half, fwd_spec, src_spec, half]
    operands = [tile, current, previous, halo_rim, speed_sq, forward, source, imaging]
    aliases = {7: 1}
    if chained:
        in_specs.append(pl.BlockSpec(memory_space=pl.ANY))
        operands.append(chain)
        aliases[8] = 0
    return pl.pallas_call(
        functools.partial(tile_kernel, moment, chained),
        grid_spec=pltpu.PrefetchScalarGridSpec(
            num_scalar_prefetch=1,
            grid=(1,),
            in_specs=in_specs,
            out_specs=(half, half, rim),
            scratch_shapes=[pltpu.VMEM((cells_y + 8, cells_x + 16, cells_z), f32)],
        ),
        out_shape=(
            jax.ShapeDtypeStruct(current.shape, f32),
            jax.ShapeDtypeStruct(current.shape, f32),
            jax.ShapeDtypeStruct(halo_rim.shape, f32),
        ),
        input_output_aliases=aliases,
        cost_estimate=pl.CostEstimate(
            flops=60 * cells, bytes_accessed=28 * cells, transcendentals=0
        ),
        compiler_params=pltpu.CompilerParams(vmem_limit_bytes=10 * 1024 * 1024),
    )(*operands)


def exact_select(select, table, dimension_numbers):
    high = lax.reduce_precision(table, exponent_bits=8, mantissa_bits=7)
    rest = table - high
    middle = lax.reduce_precision(rest, exponent_bits=8, mantissa_bits=7)
    low = rest - middle
    select = select.astype(jnp.bfloat16)
    parts = [
        lax.dot_general(
            select, part.astype(jnp.bfloat16), dimension_numbers,
            preferred_element_type=jnp.float32,
        )
        for part in (high, middle, low)
    ]
    return (parts[0] + parts[1]) + parts[2]


def halo(first, last):
    axis = "space"
    devices = lax.axis_size(axis)
    even = lax.axis_index(axis) % 2 == 0
    within = [(i, i ^ 1) for i in range(devices)]
    across = [(i, i + 1 - 2 * ((i + 1) % 2)) for i in range(1, devices - 1)]
    got_within = lax.ppermute(jnp.where(even, last, first), axis, within)
    got_across = lax.ppermute(jnp.where(even, first, last), axis, across)
    lo = jnp.where(even, got_across, got_within)
    hi = jnp.where(even, got_within, got_across)
    return lo, hi


def local(
    residual,
    record_tile,
    record_cell,
    time_filter,
    offsets,
    velocity,
    adjoint_prev,
    adjoint_now,
    forward_accel,
):
    tiles_count = lax.axis_size("space")
    record_count = residual.shape[1]
    cells_y = velocity.shape[1]
    cells_x = velocity.shape[2]
    cells_z = velocity.shape[3]
    step_count = forward_accel.shape[1]
    slot_count = record_count * 3 // 16
    surface = cells_y * cells_x
    block_rows = (cells_y + cells_y // 4) // lax.axis_size("shot")
    trace_rows = residual[0]
    tile_ids = record_tile[0, :, 0]
    cell_ids = record_cell[0]
    record_order = jnp.arange(record_count, dtype=jnp.int32)
    same_before = (tile_ids[:, None] == tile_ids[None, :]) & (
        record_order[:, None] < record_order[None, :]
    )
    order_rank = jnp.sum(same_before.astype(jnp.int32), axis=0)
    slot_index = tile_ids * slot_count + order_rank
    filtered = jnp.dot(trace_rows, time_filter.T, preferred_element_type=jnp.float32)
    payload = jnp.concatenate(
        [filtered, (cell_ids + 1).astype(jnp.float32)[:, None]], axis=1
    )
    slots = tiles_count * slot_count
    placing = (
        slot_index[None, :] == jnp.arange(slots, dtype=jnp.int32)[:, None]
    ).astype(jnp.float32)
    buffer = exact_select(placing, payload, (((1,), (0,)), ((), ())))
    buffer = buffer.reshape(tiles_count, slot_count, step_count + 1)
    arrived = lax.all_to_all(buffer, "space", split_axis=0, concat_axis=0, tiled=True)
    arrived = arrived.reshape(slots, step_count + 1)
    cell_of = arrived[:, step_count].astype(jnp.int32)
    gathering = (
        cell_of[:, None] == jnp.arange(1, surface + 1, dtype=jnp.int32)[None, :]
    ).astype(jnp.float32)
    source = exact_select(gathering, arrived[:, :step_count], (((0,), (0,)), ((), ())))
    source = source.reshape(cells_y, cells_x, step_count)
    shift_rows = offsets[0]
    speed_sq = velocity[0]
    previous = adjoint_prev[0]
    current = adjoint_now[0]
    forward = forward_accel[0]
    imaging = jnp.zeros_like(current)
    width = 4
    odd = lax.axis_index("space") % 2
    tile_near = (1 - odd).reshape(1).astype(jnp.int32)
    tile_far = odd.reshape(1).astype(jnp.int32)
    devices = lax.axis_size("space")
    within = [(i, i ^ 1) for i in range(devices)]
    across = [(i, i + 1 - 2 * ((i + 1) % 2)) for i in range(1, devices - 1)]
    zero = jnp.zeros((), jnp.int32)
    near_start = (1 - odd) * (cells_x - width)
    near_edge = lax.dynamic_slice(current, (zero, near_start, zero), (cells_y, width, cells_z))
    far_start = odd * (cells_x - width)
    far_edge = lax.dynamic_slice(current, (zero, far_start, zero), (cells_y, width, cells_z))
    for moment in range(step_count):
        near_halo = lax.ppermute(near_edge, "space", within)
        far_halo = lax.ppermute(far_edge, "space", across)
        partial_next, imaging, near_edge = tile_call(
            moment, tile_near, current, previous, near_halo, speed_sq, forward, source,
            imaging, None,
        )
        advanced, imaging, far_edge = tile_call(
            moment, tile_far, current, previous, far_halo, speed_sq, forward, source,
            imaging, partial_next,
        )
        previous, current = (current, advanced)
    row_index = jnp.arange(lax.axis_size("shot") * block_rows, dtype=jnp.int32) - shift_rows
    inside = (row_index >= 0) & (row_index < cells_y)
    chosen = jnp.take(imaging, jnp.clip(row_index, 0, cells_y - 1), axis=0)
    placed = jnp.where(inside[:, None, None], chosen, 0.0)
    shots = lax.axis_size("shot")
    placed = placed.reshape((shots, block_rows) + placed.shape[1:])
    arrived = lax.all_to_all(placed, "shot", split_axis=0, concat_axis=0, tiled=True)
    gradient = jnp.sum(arrived, axis=0)
    return (gradient, current[None])


def solution(mesh):
    in_specs = (
        P("shot", "space", None),
        P("shot", "space", None),
        P("shot", "space"),
        P(),
        P("shot"),
        P("shot", None, "space", None),
        P("shot", None, "space", None),
        P("shot", None, "space", None),
        P("shot", None, None, "space", None),
    )
    out_specs = (P("shot", "space", None), P("shot", None, "space", None))
    return jax.shard_map(local, mesh=mesh, in_specs=in_specs, out_specs=out_specs, check_vma=False)
```
